32 devices in a mesh: groups: 1, gx: 32 (over z, y, x, core).
Axes of the slice: x: 2, y: 2, z: 4, core: 2. Of those that a mesh axis runs over, the one named last changes fastest.
Arguments:
- solid_state: float32 [9, 2, 1, 256, 4, 128], P(None, None, 'groups', 'gx'), may hold values from -6 to 6
- water_state: float32 [4, 2, 1, 128, 12, 256], P(None, None, 'groups', 'gx'), may hold values from -6 to 6
- lame_lambda: float32 [256, 4, 128], P('gx'), may hold values from 0.4 to 1.2
- shear_mu: float32 [256, 4, 128], P('gx'), may hold values from 0.1 to 0.5
- solid_buoy: float32 [256, 4, 128], P('gx'), may hold values from 0.4 to 1
- water_kappa: float32 [128, 12, 256], P('gx'), may hold values from 0.5 to 1
- water_buoy: float32 [128, 12, 256], P('gx'), may hold values from 0.6 to 1.2
- seafloor: int32 [128, 256], P('gx'), may hold values from 6 to 12
- source_cell: int32 [1], P('groups'), may hold values from 0 to 196607
- wavelet: float32 [4, 1], P(None, 'groups'), may hold values from -48 to 48
- receiver_column: int32 [128], replicated, may hold values from 0 to 32767
- observed: float32 [4, 1, 128], P(None, 'groups'), may hold values from -6 to 6
Outputs:
- grad_lambda: float32 [256, 4, 128], P('gx', 'groups')
- grad_mu: float32 [256, 4, 128], P('gx', 'groups')
- grad_kappa: float32 [128, 12, 256], P('gx', 'groups')
- residuals: float32 [4, 1, 128], P(None, 'groups')
The draws below stay inside these ranges and needn't reach their ends.
Inputs may be any that keep to these rules, and one draw needn't show every extreme that they name: Every column holds water from z = 0 to z = seafloor - 1 and rock below it. source_cell is (z * 128 + y) * 256 + x of a water cell with z below 6. receiver_column is y * 256 + x; two nodes may share a column.
All inputs are finite; a program needn't handle non-finite values.
Results may differ from the reference program's by a relative error of at most 0.00014.
Values sent between devices are 32-bit elements; how exact they have to be, the bound alone decides.
No kernel may reach another device: no remote copies, remote signals or barrier semaphores. Data moves between devices by JAX's collectives and lax.ppermute only.
A program may use at most 64 MiB of HBM per device.

```python
import jax
import jax.numpy as jnp
from jax import lax

NZ = 4
WZ = 12
S = 1
R = 128
STEPS = 4
NX = 256
NY = 128


def plant(values, key, smallest, high):
    extent = values.shape
    place = [jax.random.randint(jax.random.fold_in(key, axis), (), 0, extent[axis]) for axis in range(len(extent))]
    values = values.at[tuple(place)].set(smallest)
    longest = extent.index(max(extent))
    place[longest] = (place[longest] + 1) % extent[longest]
    return values.at[tuple(place)].set(high)


def shard_levels(rng, shape, cuts, low, largest):
    def one(axis_at, blocks):
        heights = jax.random.uniform(jax.random.fold_in(jax.random.fold_in(rng, 6), axis_at), (blocks,), jnp.float32, low / len(cuts), largest / len(cuts))
        return jnp.repeat(jnp.exp(heights), shape[axis_at] // blocks).reshape((-1,) + (1,) * (len(shape) - axis_at - 1))

    level = one(*cuts[0])
    for cut in cuts[1:]:
        level = level * one(*cut)
    return level


def scatter_about(rng, extent, scale, most, split=(), held_as=jnp.bfloat16):
    factor_of = shard_levels(rng, extent, split, -0.22, 0.18) if split else 1.0
    entries = jax.random.normal(rng, extent, jnp.float32) * scale * factor_of
    return jnp.minimum(jnp.maximum(entries, -most), most).astype(held_as)


def setup_inputs(seed: int = 0, part: int = 0) -> dict:
    seeds = jax.random.split(jax.random.key(seed), 13)
    part_splits = jax.random.split(jax.random.fold_in(seeds[12], part), 13)
    return {
        "solid_state": scatter_about(part_splits[0], (9, 2, S, NX, NZ, NY), 1.0, 6.0, ((3, 32),), jnp.float32),
        "water_state": scatter_about(part_splits[1], (4, 2, S, NY, WZ, NX), 1.0, 6.0, ((3, 32),), jnp.float32),
        "lame_lambda": jnp.clip(0.4 + 0.800000042 * jax.random.uniform(seeds[2], (NX, NZ, NY), jnp.float32) ** shard_levels(seeds[2], (NX, NZ, NY), ((0, 32),), -0.2, 0.2), 0.4, 1.2),
        "shear_mu": jnp.clip(0.1 + 0.4 * jax.random.uniform(seeds[3], (NX, NZ, NY), jnp.float32) ** shard_levels(seeds[3], (NX, NZ, NY), ((0, 32),), -0.2, 0.2), 0.1, 0.5),
        "solid_buoy": jnp.clip(0.4 + 0.6 * jax.random.uniform(seeds[4], (NX, NZ, NY), jnp.float32) ** shard_levels(seeds[4], (NX, NZ, NY), ((0, 32),), -0.2, 0.2), 0.4, 1.0),
        "water_kappa": jnp.clip(0.5 + 0.5 * jax.random.uniform(seeds[5], (NY, WZ, NX), jnp.float32) ** shard_levels(seeds[5], (NY, WZ, NX), ((0, 32),), -0.2, 0.2), 0.5, 1.0),
        "water_buoy": jnp.clip(0.6 + 0.6 * jax.random.uniform(seeds[6], (NY, WZ, NX), jnp.float32) ** shard_levels(seeds[6], (NY, WZ, NX), ((0, 32),), -0.2, 0.2), 0.6, 1.2),
        "seafloor": plant(jax.random.randint(seeds[7], (NY, NX), WZ // 2, WZ + 1), jax.random.fold_in(seeds[7], 1), WZ // 2, WZ).astype(jnp.int32),
        "source_cell": jax.random.randint(part_splits[8], (S,), 0, (WZ // 2) * NY * NX).astype(jnp.int32),
        "wavelet": scatter_about(part_splits[9], (STEPS, S), 8.0, 48.0, (), jnp.float32),
        "receiver_column": plant(jax.random.randint(seeds[10], (R,), 0, NX * NY), jax.random.fold_in(seeds[10], 1), 0, (NX * NY) - 1).astype(jnp.int32),
        "observed": scatter_about(part_splits[11], (STEPS, S, R), 1.0, 6.0, (), jnp.float32),
    }


COEFF = (1225.0 / 1024.0, -245.0 / 3072.0, 49.0 / 5120.0, -5.0 / 7168.0)
TIME_STEP = 0.2

def stencil(padded, axis, forward):
    length = padded.shape[axis] - 8
    summed = None
    for offset in range(1, 5):
        if forward:
            front_at, back_at = (4 + offset, 5 - offset)
        else:
            front_at, back_at = (3 + offset, 4 - offset)
        front = lax.slice_in_dim(padded, front_at, front_at + length, axis=axis)
        back = lax.slice_in_dim(padded, back_at, back_at + length, axis=axis)
        addend = COEFF[offset - 1] * (front - back)
        summed = addend if summed is None else summed + addend
    return summed

def padded_zero(field, axis):
    widths = [(0, 0)] * field.ndim
    widths[axis] = (4, 4)
    return jnp.pad(field, widths)

def derive(field, axis, forward):
    return stencil(padded_zero(field, axis), axis, forward)

def reference(solid_state, water_state, lame_lambda, shear_mu, solid_buoy, water_kappa, water_buoy, seafloor, source_cell, wavelet, receiver_column, observed):
    vel_x, vel_y, vel_z = (solid_state[0], solid_state[1], solid_state[2])
    sig_xx, sig_yy, sig_zz = (solid_state[3], solid_state[4], solid_state[5])
    sig_xy, sig_xz, sig_yz = (solid_state[6], solid_state[7], solid_state[8])
    pressure, flow_x, flow_y, flow_z = (water_state[0], water_state[1], water_state[2], water_state[3])
    total_y, depth_rows, total_x = water_kappa.shape
    depth_idx = lax.broadcasted_iota(jnp.int32, (1, depth_rows, 1), 1)
    floor_rows = seafloor[:, None, :]
    live = (depth_idx < floor_rows).astype(jnp.float32)
    bottom = (depth_idx == floor_rows - 1).astype(jnp.float32)
    above = (depth_idx < floor_rows - 1).astype(jnp.float32)
    rows_y = lax.broadcasted_iota(jnp.int32, (total_y, 1, 1), 0)
    cols_x = lax.broadcasted_iota(jnp.int32, (1, 1, total_x), 2)
    flat_cell = (depth_idx * total_y + rows_y) * total_x + cols_x
    source_hot = (flat_cell[None] == source_cell[:, None, None, None]).astype(jnp.float32)
    node_y = receiver_column // total_x
    node_x = receiver_column % total_x
    grad_lambda = jnp.zeros(lame_lambda.shape, jnp.float32)
    grad_mu = jnp.zeros(lame_lambda.shape, jnp.float32)
    grad_kappa = jnp.zeros(water_kappa.shape, jnp.float32)
    misfits = []
    for step in range(wavelet.shape[0]):
        floor_pressure = lax.optimization_barrier(jnp.sum(pressure * bottom, axis=3))
        vel_x = vel_x + TIME_STEP * solid_buoy * (derive(sig_xx, 2, True) + derive(sig_xy, 4, False) + derive(sig_xz, 3, False))
        vel_y = vel_y + TIME_STEP * solid_buoy * (derive(sig_xy, 2, False) + derive(sig_yy, 4, True) + derive(sig_yz, 3, False))
        vel_z = vel_z + TIME_STEP * solid_buoy * (derive(sig_xz, 2, False) + derive(sig_yz, 4, False) + derive(sig_zz, 3, True))
        floor_velocity = jnp.transpose(vel_z[:, :, :, 0, :], (0, 1, 3, 2))
        flow_x = (flow_x - TIME_STEP * water_buoy * derive(pressure, 4, True)) * live
        flow_y = (flow_y - TIME_STEP * water_buoy * derive(pressure, 2, True)) * live
        flow_z = (flow_z - TIME_STEP * water_buoy * derive(pressure, 3, True)) * above + floor_velocity[:, :, :, None, :] * bottom
        strain_x = derive(vel_x, 2, False)
        strain_y = derive(vel_y, 4, False)
        strain_z = derive(vel_z, 3, False)
        dilation = strain_x + strain_y + strain_z
        shear_xy = derive(vel_x, 4, True) + derive(vel_y, 2, True)
        shear_xz = derive(vel_x, 3, True) + derive(vel_z, 2, True)
        shear_yz = derive(vel_y, 3, True) + derive(vel_z, 4, True)
        lam_part = lame_lambda * dilation
        sig_xx = sig_xx + TIME_STEP * (lam_part + 2.0 * shear_mu * strain_x)
        sig_yy = sig_yy + TIME_STEP * (lam_part + 2.0 * shear_mu * strain_y)
        sig_zz = sig_zz + TIME_STEP * (lam_part + 2.0 * shear_mu * strain_z)
        sig_xy = sig_xy + TIME_STEP * shear_mu * shear_xy
        sig_xz = sig_xz + TIME_STEP * shear_mu * shear_xz
        sig_yz = sig_yz + TIME_STEP * shear_mu * shear_yz
        sig_zz = sig_zz.at[:, :, :, 0, :].set(-jnp.transpose(floor_pressure, (0, 1, 3, 2)))
        grad_lambda = grad_lambda + lax.optimization_barrier(jnp.sum(dilation[0] * dilation[1], axis=0))
        normal_part = strain_x[0] * strain_x[1] + strain_y[0] * strain_y[1] + strain_z[0] * strain_z[1]
        shear_part = shear_xy[0] * shear_xy[1] + shear_xz[0] * shear_xz[1] + shear_yz[0] * shear_yz[1]
        grad_mu = grad_mu + lax.optimization_barrier(jnp.sum(2.0 * normal_part + shear_part, axis=0))
        pressure = (pressure - TIME_STEP * water_kappa * (derive(flow_x, 4, False) + derive(flow_y, 2, False) + derive(flow_z, 3, False))) * live
        pressure = pressure.at[0].add(wavelet[step][:, None, None, None] * source_hot)
        surface = lax.optimization_barrier(jnp.sum(pressure * bottom, axis=3))
        recorded = surface[0][:, node_y, node_x]
        misfit = recorded - observed[step]
        scaled = misfit * lax.rsqrt(lax.optimization_barrier(jnp.mean(misfit * misfit, axis=1, keepdims=True)) + 1e-06)
        inject = jnp.zeros(surface.shape[1:], jnp.float32).at[:, node_y, node_x].add(scaled)
        pressure = pressure.at[1].add(inject[:, :, None, :] * bottom)
        grad_kappa = grad_kappa + lax.optimization_barrier(jnp.sum(pressure[0] * pressure[1], axis=0))
        misfits.append(misfit)
    return (grad_lambda, grad_mu, grad_kappa, jnp.stack(misfits))
```

```python
import jax
import jax.numpy as jnp
from jax import lax
from jax.sharding import PartitionSpec as P

COEFF = (1225.0 / 1024.0, -245.0 / 3072.0, 49.0 / 5120.0, -5.0 / 7168.0)
TIME_STEP = 0.2


def with_halo(array, sides, width):
    for axis, dim in sides:
        devices, length = (lax.axis_size(axis), array.shape[dim])
        up = [(i, (i + 1) % devices) for i in range(devices - 1)]
        down = [(j, i) for i, j in up]
        last = lax.slice_in_dim(array, length - width, length, axis=dim)
        first = lax.slice_in_dim(array, 0, width, axis=dim)
        before = lax.ppermute(last, axis, up)
        after = lax.ppermute(first, axis, down)
        array = jnp.concatenate([before, array, after], axis=dim)
    return array


def gather_sum(partial, parts):
    copies = jnp.broadcast_to(partial[None], (parts,) + partial.shape)
    return jnp.sum(lax.all_to_all(copies, "gx", 0, 0, tiled=True), axis=0)


def stencil(padded, axis, forward):
    length = padded.shape[axis] - 8
    summed = None
    for offset in range(1, 5):
        if forward:
            front_at, back_at = (4 + offset, 5 - offset)
        else:
            front_at, back_at = (3 + offset, 4 - offset)
        front = lax.slice_in_dim(padded, front_at, front_at + length, axis=axis)
        back = lax.slice_in_dim(padded, back_at, back_at + length, axis=axis)
        addend = COEFF[offset - 1] * (front - back)
        summed = addend if summed is None else summed + addend
    return summed


def padded_zero(field, axis):
    widths = [(0, 0)] * field.ndim
    widths[axis] = (4, 4)
    return jnp.pad(field, widths)


def derive(field, axis, forward):
    return stencil(padded_zero(field, axis), axis, forward)


def on_device(
    solid_state,
    water_state,
    lame_lambda,
    shear_mu,
    solid_buoy,
    water_kappa,
    water_buoy,
    seafloor,
    source_cell,
    wavelet,
    receiver_column,
    observed,
):
    parts = lax.axis_size("gx")
    place = lax.axis_index("gx")
    width_x = solid_state.shape[3]
    total_y = solid_state.shape[5]
    total_x = width_x * parts
    shots = solid_state.shape[2]
    shard_axis = 2
    anchor_y = place * water_state.shape[3]
    anchor_x = 0

    def water_halo(field):
        return with_halo(field, (("gx", 2),), 4)

    def water_derive(field, axis, forward):
        if axis == shard_axis:
            return stencil(water_halo(field), axis, forward)
        return derive(field, axis, forward)

    def solid_halo(stacked):
        return with_halo(stacked, (("gx", 3),), 4)

    vel_x, vel_y, vel_z = (solid_state[0], solid_state[1], solid_state[2])
    sig_xx, sig_yy, sig_zz = (solid_state[3], solid_state[4], solid_state[5])
    sig_xy, sig_xz, sig_yz = (solid_state[6], solid_state[7], solid_state[8])
    pressure, flow_x, flow_y, flow_z = (
        water_state[0],
        water_state[1],
        water_state[2],
        water_state[3],
    )
    local_y = pressure.shape[2]
    depth_rows = pressure.shape[3]
    local_x = pressure.shape[4]
    depth_idx = lax.broadcasted_iota(jnp.int32, (1, depth_rows, 1), 1)
    floor_rows = seafloor[:, None, :]
    live = (depth_idx < floor_rows).astype(jnp.float32)
    bottom = (depth_idx == floor_rows - 1).astype(jnp.float32)
    above = (depth_idx < floor_rows - 1).astype(jnp.float32)
    rows_y = lax.broadcasted_iota(jnp.int32, (local_y, 1, 1), 0) + anchor_y
    cols_x = lax.broadcasted_iota(jnp.int32, (1, 1, local_x), 2) + anchor_x
    flat_cell = (depth_idx * total_y + rows_y) * total_x + cols_x
    source_hot = (flat_cell[None] == source_cell[:, None, None, None]).astype(jnp.float32)
    node_y = receiver_column // total_x
    node_x = receiver_column % total_x
    inside = (
        (node_y >= anchor_y)
        & (node_y < anchor_y + local_y)
        & (node_x >= anchor_x)
        & (node_x < anchor_x + local_x)
    )
    local_col = (node_y - anchor_y) * local_x + (node_x - anchor_x)
    column_iota = lax.broadcasted_iota(jnp.int32, (1, local_y * local_x), 1)
    node_hot = ((column_iota == local_col[:, None]) & inside[:, None]).astype(jnp.float32)
    grad_lambda = jnp.zeros(lame_lambda.shape, jnp.float32)
    grad_mu = jnp.zeros(lame_lambda.shape, jnp.float32)
    grad_kappa = jnp.zeros(water_kappa.shape, jnp.float32)
    misfits = []
    for step in range(wavelet.shape[0]):
        floor_pressure = jnp.sum(pressure * bottom, axis=3)
        stress_pad = solid_halo(jnp.stack([sig_xx, sig_xy, sig_xz]))
        vel_x = vel_x + TIME_STEP * solid_buoy * (
            stencil(stress_pad[0], 2, True) + derive(sig_xy, 4, False) + derive(sig_xz, 3, False)
        )
        vel_y = vel_y + TIME_STEP * solid_buoy * (
            stencil(stress_pad[1], 2, False) + derive(sig_yy, 4, True) + derive(sig_yz, 3, False)
        )
        vel_z = vel_z + TIME_STEP * solid_buoy * (
            stencil(stress_pad[2], 2, False) + derive(sig_yz, 4, False) + derive(sig_zz, 3, True)
        )
        floor_velocity = lax.all_to_all(
            jnp.transpose(vel_z[:, :, :, 0, :], (0, 1, 3, 2)),
            "gx",
            split_axis=2,
            concat_axis=3,
            tiled=True,
        )
        flow_x = (flow_x - TIME_STEP * water_buoy * water_derive(pressure, 4, True)) * live
        flow_y = (flow_y - TIME_STEP * water_buoy * water_derive(pressure, 2, True)) * live
        flow_z = (
            flow_z - TIME_STEP * water_buoy * derive(pressure, 3, True)
        ) * above + floor_velocity[:, :, :, None, :] * bottom
        velocity_pad = solid_halo(jnp.stack([vel_x, vel_y, vel_z]))
        strain_x = stencil(velocity_pad[0], 2, False)
        strain_y = derive(vel_y, 4, False)
        strain_z = derive(vel_z, 3, False)
        dilation = strain_x + strain_y + strain_z
        shear_xy = derive(vel_x, 4, True) + stencil(velocity_pad[1], 2, True)
        shear_xz = derive(vel_x, 3, True) + stencil(velocity_pad[2], 2, True)
        shear_yz = derive(vel_y, 3, True) + derive(vel_z, 4, True)
        lam_part = lame_lambda * dilation
        sig_xx = sig_xx + TIME_STEP * (lam_part + 2.0 * shear_mu * strain_x)
        sig_yy = sig_yy + TIME_STEP * (lam_part + 2.0 * shear_mu * strain_y)
        sig_zz = sig_zz + TIME_STEP * (lam_part + 2.0 * shear_mu * strain_z)
        sig_xy = sig_xy + TIME_STEP * shear_mu * shear_xy
        sig_xz = sig_xz + TIME_STEP * shear_mu * shear_xz
        sig_yz = sig_yz + TIME_STEP * shear_mu * shear_yz
        rock_pressure = jnp.transpose(
            lax.all_to_all(floor_pressure, "gx", split_axis=3, concat_axis=2, tiled=True),
            (0, 1, 3, 2),
        )
        sig_zz = sig_zz.at[:, :, :, 0, :].set(-rock_pressure)
        grad_lambda = grad_lambda + jnp.sum(dilation[0] * dilation[1], axis=0)
        normal_part = (
            strain_x[0] * strain_x[1] + strain_y[0] * strain_y[1] + strain_z[0] * strain_z[1]
        )
        shear_part = (
            shear_xy[0] * shear_xy[1] + shear_xz[0] * shear_xz[1] + shear_yz[0] * shear_yz[1]
        )
        grad_mu = grad_mu + jnp.sum(2.0 * normal_part + shear_part, axis=0)
        pressure = (
            pressure
            - TIME_STEP
            * water_kappa
            * (
                water_derive(flow_x, 4, False)
                + water_derive(flow_y, 2, False)
                + derive(flow_z, 3, False)
            )
        ) * live
        pressure = pressure.at[0].add(wavelet[step][:, None, None, None] * source_hot)
        surface = jnp.sum(pressure * bottom, axis=3)
        partial_record = jnp.einsum(
            "sc,rc->sr",
            surface[0].reshape(shots, local_y * local_x),
            node_hot,
            precision=lax.Precision.HIGHEST,
        )
        recorded = gather_sum(partial_record, parts)
        misfit = recorded - observed[step]
        scaled = misfit * lax.rsqrt(jnp.mean(misfit * misfit, axis=1, keepdims=True) + 1e-06)
        inject = jnp.dot(
            scaled, node_hot, precision=lax.Precision.HIGHEST, preferred_element_type=jnp.float32
        ).reshape(shots, local_y, local_x)
        pressure = pressure.at[1].add(inject[:, :, None, :] * bottom)
        grad_kappa = grad_kappa + jnp.sum(pressure[0] * pressure[1], axis=0)
        misfits.append(misfit)
    return (grad_lambda, grad_mu, grad_kappa, jnp.stack(misfits))


def solution(mesh):
    placed = (
        P(None, None, "groups", "gx", None, None),
        P(None, None, "groups", "gx", None, None),
        P("gx", None, None),
        P("gx", None, None),
        P("gx", None, None),
        P("gx", None, None),
        P("gx", None, None),
        P("gx", None),
        P("groups"),
        P(None, "groups"),
        P(),
        P(None, "groups", None),
    )
    return jax.shard_map(
        on_device,
        mesh=mesh,
        in_specs=placed,
        out_specs=(
            P("gx", "groups", None),
            P("gx", "groups", None),
            P("gx", "groups", None),
            P(None, "groups", None),
        ),
        check_vma=False,
    )
```

```python
import jax
import jax.numpy as jnp
from jax import lax
from jax.sharding import PartitionSpec as P

COEFF = (1225.0 / 1024.0, -245.0 / 3072.0, 49.0 / 5120.0, -5.0 / 7168.0)
TIME_STEP = 0.2
HALO = 4
ROW_AXIS = 2
DEPTH_AXIS = 3


def halo_rows(fields):
    devices = lax.axis_size("gx")
    up = [(i, i + 1) for i in range(devices - 1)]
    down = [(i + 1, i) for i in range(devices - 1)]
    packed = jnp.concatenate(fields, axis=DEPTH_AXIS)
    length = packed.shape[ROW_AXIS]
    before = lax.ppermute(
        lax.slice_in_dim(packed, length - HALO, length, axis=ROW_AXIS), "gx", up
    )
    after = lax.ppermute(lax.slice_in_dim(packed, 0, HALO, axis=ROW_AXIS), "gx", down)
    padded = jnp.concatenate([before, packed, after], axis=ROW_AXIS)
    out, start = [], 0
    for f in fields:
        depth = f.shape[DEPTH_AXIS]
        out.append(lax.slice_in_dim(padded, start, start + depth, axis=DEPTH_AXIS))
        start += depth
    return out


def gather_sum(partial, parts):
    copies = jnp.broadcast_to(partial[None], (parts,) + partial.shape)
    return jnp.sum(lax.all_to_all(copies, "gx", 0, 0, tiled=True), axis=0)


def stencil(padded, axis, forward):
    length = padded.shape[axis] - 8
    summed = None
    for offset in range(1, 5):
        if forward:
            front_at, back_at = (4 + offset, 5 - offset)
        else:
            front_at, back_at = (3 + offset, 4 - offset)
        front = lax.slice_in_dim(padded, front_at, front_at + length, axis=axis)
        back = lax.slice_in_dim(padded, back_at, back_at + length, axis=axis)
        addend = COEFF[offset - 1] * (front - back)
        summed = addend if summed is None else summed + addend
    return summed


def padded_zero(field, axis):
    widths = [(0, 0)] * field.ndim
    widths[axis] = (4, 4)
    return jnp.pad(field, widths)


def derive(field, axis, forward):
    return stencil(padded_zero(field, axis), axis, forward)


def on_device(
    solid_state,
    water_state,
    lame_lambda,
    shear_mu,
    solid_buoy,
    water_kappa,
    water_buoy,
    seafloor,
    source_cell,
    wavelet,
    receiver_column,
    observed,
):
    parts = lax.axis_size("gx")
    place = lax.axis_index("gx")
    n_fields, waves, shots, width_x, rock_z, total_y = solid_state.shape
    local_y = water_state.shape[3]
    depth_rows = water_state.shape[4]
    total_x = water_state.shape[5]
    anchor_y = place * local_y

    rock_in = jnp.concatenate(
        [
            solid_state.reshape(n_fields * waves * shots, width_x, rock_z, total_y),
            jnp.stack([lame_lambda, shear_mu, solid_buoy]),
        ],
        axis=0,
    )
    rock = lax.all_to_all(
        jnp.transpose(rock_in, (0, 3, 2, 1)), "gx", split_axis=1, concat_axis=3, tiled=True
    )
    rock_state = rock[: n_fields * waves * shots].reshape(
        n_fields, waves, shots, local_y, rock_z, total_x
    )
    lam, mu, buoy = rock[-3], rock[-2], rock[-1]

    vel_x, vel_y, vel_z = (rock_state[0], rock_state[1], rock_state[2])
    sig_xx, sig_yy, sig_zz = (rock_state[3], rock_state[4], rock_state[5])
    sig_xy, sig_xz, sig_yz = (rock_state[6], rock_state[7], rock_state[8])
    pressure, flow_x, flow_y, flow_z = (
        water_state[0],
        water_state[1],
        water_state[2],
        water_state[3],
    )
    depth_idx = lax.broadcasted_iota(jnp.int32, (1, depth_rows, 1), 1)
    floor_rows = seafloor[:, None, :]
    live = (depth_idx < floor_rows).astype(jnp.float32)
    bottom = (depth_idx == floor_rows - 1).astype(jnp.float32)
    above = (depth_idx < floor_rows - 1).astype(jnp.float32)
    rows_y = lax.broadcasted_iota(jnp.int32, (local_y, 1, 1), 0) + anchor_y
    cols_x = lax.broadcasted_iota(jnp.int32, (1, 1, total_x), 2)
    flat_cell = (depth_idx * total_y + rows_y) * total_x + cols_x
    source_hot = (flat_cell[None] == source_cell[:, None, None, None]).astype(jnp.float32)
    node_y = receiver_column // total_x
    node_x = receiver_column % total_x
    inside = (node_y >= anchor_y) & (node_y < anchor_y + local_y)
    local_col = (node_y - anchor_y) * total_x + node_x
    column_iota = lax.broadcasted_iota(jnp.int32, (1, local_y * total_x), 1)
    node_hot = ((column_iota == local_col[:, None]) & inside[:, None]).astype(jnp.float32)
    grad_lambda = jnp.zeros(lam.shape, jnp.float32)
    grad_mu = jnp.zeros(lam.shape, jnp.float32)
    grad_kappa = jnp.zeros(water_kappa.shape, jnp.float32)
    misfits = []
    for step in range(wavelet.shape[0]):
        floor_pressure = jnp.sum(pressure * bottom, axis=3)
        sxy_pad, syy_pad, syz_pad, p_pad = halo_rows([sig_xy, sig_yy, sig_yz, pressure])
        vel_x = vel_x + TIME_STEP * buoy * (
            derive(sig_xx, 4, True) + stencil(sxy_pad, 2, False) + derive(sig_xz, 3, False)
        )
        vel_y = vel_y + TIME_STEP * buoy * (
            derive(sig_xy, 4, False) + stencil(syy_pad, 2, True) + derive(sig_yz, 3, False)
        )
        vel_z = vel_z + TIME_STEP * buoy * (
            derive(sig_xz, 4, False) + stencil(syz_pad, 2, False) + derive(sig_zz, 3, True)
        )
        floor_velocity = vel_z[:, :, :, 0, :]
        flow_x = (flow_x - TIME_STEP * water_buoy * derive(pressure, 4, True)) * live
        flow_y = (flow_y - TIME_STEP * water_buoy * stencil(p_pad, 2, True)) * live
        flow_z = (
            flow_z - TIME_STEP * water_buoy * derive(pressure, 3, True)
        ) * above + floor_velocity[:, :, :, None, :] * bottom
        vx_pad, vy_pad, vz_pad, uy_pad = halo_rows([vel_x, vel_y, vel_z, flow_y])
        strain_x = derive(vel_x, 4, False)
        strain_y = stencil(vy_pad, 2, False)
        strain_z = derive(vel_z, 3, False)
        dilation = strain_x + strain_y + strain_z
        shear_xy = stencil(vx_pad, 2, True) + derive(vel_y, 4, True)
        shear_xz = derive(vel_x, 3, True) + derive(vel_z, 4, True)
        shear_yz = derive(vel_y, 3, True) + stencil(vz_pad, 2, True)
        lam_part = lam * dilation
        sig_xx = sig_xx + TIME_STEP * (lam_part + 2.0 * mu * strain_x)
        sig_yy = sig_yy + TIME_STEP * (lam_part + 2.0 * mu * strain_y)
        sig_zz = sig_zz + TIME_STEP * (lam_part + 2.0 * mu * strain_z)
        sig_xy = sig_xy + TIME_STEP * mu * shear_xy
        sig_xz = sig_xz + TIME_STEP * mu * shear_xz
        sig_yz = sig_yz + TIME_STEP * mu * shear_yz
        sig_zz = sig_zz.at[:, :, :, 0, :].set(-floor_pressure)
        grad_lambda = grad_lambda + jnp.sum(dilation[0] * dilation[1], axis=0)
        normal_part = (
            strain_x[0] * strain_x[1] + strain_y[0] * strain_y[1] + strain_z[0] * strain_z[1]
        )
        shear_part = (
            shear_xy[0] * shear_xy[1] + shear_xz[0] * shear_xz[1] + shear_yz[0] * shear_yz[1]
        )
        grad_mu = grad_mu + jnp.sum(2.0 * normal_part + shear_part, axis=0)
        pressure = (
            pressure
            - TIME_STEP
            * water_kappa
            * (derive(flow_x, 4, False) + stencil(uy_pad, 2, False) + derive(flow_z, 3, False))
        ) * live
        pressure = pressure.at[0].add(wavelet[step][:, None, None, None] * source_hot)
        surface = jnp.sum(pressure * bottom, axis=3)
        partial_record = jnp.einsum(
            "sc,rc->sr",
            surface[0].reshape(shots, local_y * total_x),
            node_hot,
            precision=lax.Precision.HIGHEST,
        )
        recorded = gather_sum(partial_record, parts)
        misfit = recorded - observed[step]
        scaled = misfit * lax.rsqrt(jnp.mean(misfit * misfit, axis=1, keepdims=True) + 1e-06)
        inject = jnp.dot(
            scaled, node_hot, precision=lax.Precision.HIGHEST, preferred_element_type=jnp.float32
        ).reshape(shots, local_y, total_x)
        pressure = pressure.at[1].add(inject[:, :, None, :] * bottom)
        grad_kappa = grad_kappa + jnp.sum(pressure[0] * pressure[1], axis=0)
        misfits.append(misfit)

    grads = lax.all_to_all(
        jnp.stack([grad_lambda, grad_mu]), "gx", split_axis=3, concat_axis=1, tiled=True
    )
    grads = jnp.transpose(grads, (0, 3, 2, 1))
    return (grads[0], grads[1], grad_kappa, jnp.stack(misfits))


def solution(mesh):
    placed = (
        P(None, None, "groups", "gx", None, None),
        P(None, None, "groups", "gx", None, None),
        P("gx", None, None),
        P("gx", None, None),
        P("gx", None, None),
        P("gx", None, None),
        P("gx", None, None),
        P("gx", None),
        P("groups"),
        P(None, "groups"),
        P(),
        P(None, "groups", None),
    )
    return jax.shard_map(
        on_device,
        mesh=mesh,
        in_specs=placed,
        out_specs=(
            P("gx", "groups", None),
            P("gx", "groups", None),
            P("gx", "groups", None),
            P(None, "groups", None),
        ),
        check_vma=False,
    )
```

```python
import jax
import jax.numpy as jnp
from jax import lax
from jax.sharding import PartitionSpec as P

COEFF = (1225.0 / 1024.0, -245.0 / 3072.0, 49.0 / 5120.0, -5.0 / 7168.0)
TIME_STEP = 0.2
HALO = 4
ROW_AXIS = 2
DEPTH_AXIS = 3


def halo_rows(fields):
    devices = lax.axis_size("gx")
    up = [(i, i + 1) for i in range(devices - 1)]
    down = [(i + 1, i) for i in range(devices - 1)]
    packed = jnp.concatenate(fields, axis=DEPTH_AXIS)
    length = packed.shape[ROW_AXIS]
    before = lax.ppermute(
        lax.slice_in_dim(packed, length - HALO, length, axis=ROW_AXIS), "gx", up
    )
    after = lax.ppermute(lax.slice_in_dim(packed, 0, HALO, axis=ROW_AXIS), "gx", down)
    padded = jnp.concatenate([before, packed, after], axis=ROW_AXIS)
    out, start = [], 0
    for f in fields:
        depth = f.shape[DEPTH_AXIS]
        out.append(lax.slice_in_dim(padded, start, start + depth, axis=DEPTH_AXIS))
        start += depth
    return out


def gather_sum(partial, parts):
    copies = jnp.broadcast_to(partial[None], (parts,) + partial.shape)
    return jnp.sum(lax.all_to_all(copies, "gx", 0, 0, tiled=True), axis=0)


def stencil(padded, axis, forward):
    length = padded.shape[axis] - 8
    summed = None
    for offset in range(1, 5):
        if forward:
            front_at, back_at = (4 + offset, 5 - offset)
        else:
            front_at, back_at = (3 + offset, 4 - offset)
        front = lax.slice_in_dim(padded, front_at, front_at + length, axis=axis)
        back = lax.slice_in_dim(padded, back_at, back_at + length, axis=axis)
        addend = COEFF[offset - 1] * (front - back)
        summed = addend if summed is None else summed + addend
    return summed


def padded_zero(field, axis):
    widths = [(0, 0)] * field.ndim
    widths[axis] = (4, 4)
    return jnp.pad(field, widths)


def derive(field, axis, forward):
    return stencil(padded_zero(field, axis), axis, forward)


def on_device(
    solid_state,
    water_state,
    lame_lambda,
    shear_mu,
    solid_buoy,
    water_kappa,
    water_buoy,
    seafloor,
    source_cell,
    wavelet,
    receiver_column,
    observed,
):
    parts = lax.axis_size("gx")
    place = lax.axis_index("gx")
    n_fields, waves, shots, width_x, rock_z, total_y = solid_state.shape
    local_y = water_state.shape[3]
    depth_rows = water_state.shape[4]
    total_x = water_state.shape[5]
    anchor_y = place * local_y

    rock_in = jnp.concatenate(
        [
            solid_state.reshape(n_fields * waves * shots, width_x, rock_z, total_y),
            jnp.stack([lame_lambda, shear_mu, solid_buoy]),
        ],
        axis=0,
    )
    rock = lax.all_to_all(
        jnp.transpose(rock_in, (0, 3, 2, 1)), "gx", split_axis=1, concat_axis=3, tiled=True
    )
    rock_state = rock[: n_fields * waves * shots].reshape(
        n_fields, waves, shots, local_y, rock_z, total_x
    )
    lam, mu, buoy = rock[-3], rock[-2], rock[-1]

    vel_x, vel_y, vel_z = (rock_state[0], rock_state[1], rock_state[2])
    sig_xx, sig_yy, sig_zz = (rock_state[3], rock_state[4], rock_state[5])
    sig_xy, sig_xz, sig_yz = (rock_state[6], rock_state[7], rock_state[8])
    pressure, flow_x, flow_y, flow_z = (
        water_state[0],
        water_state[1],
        water_state[2],
        water_state[3],
    )
    depth_idx = lax.broadcasted_iota(jnp.int32, (1, depth_rows, 1), 1)
    floor_rows = seafloor[:, None, :]
    live = (depth_idx < floor_rows).astype(jnp.float32)
    bottom = (depth_idx == floor_rows - 1).astype(jnp.float32)
    above = (depth_idx < floor_rows - 1).astype(jnp.float32)
    rows_y = lax.broadcasted_iota(jnp.int32, (local_y, 1, 1), 0) + anchor_y
    cols_x = lax.broadcasted_iota(jnp.int32, (1, 1, total_x), 2)
    flat_cell = (depth_idx * total_y + rows_y) * total_x + cols_x
    source_hot = (flat_cell[None] == source_cell[:, None, None, None]).astype(jnp.float32)
    node_y = receiver_column // total_x
    node_x = receiver_column % total_x
    inside = (node_y >= anchor_y) & (node_y < anchor_y + local_y)
    local_col = (node_y - anchor_y) * total_x + node_x
    column_iota = lax.broadcasted_iota(jnp.int32, (1, local_y * total_x), 1)
    node_hot = ((column_iota == local_col[:, None]) & inside[:, None]).astype(jnp.float32)
    steps = wavelet.shape[0]
    lam_acc = jnp.zeros((1, shots) + lam.shape, jnp.float32)
    mu_acc = jnp.zeros((1, shots) + lam.shape, jnp.float32)
    kappa_acc = jnp.zeros((1, shots) + water_kappa.shape, jnp.float32)
    partial_records = []
    for step in range(steps):
        floor_pressure = jnp.sum(pressure * bottom, axis=3)
        sxy_pad, syy_pad, syz_pad, p_pad = halo_rows([sig_xy, sig_yy, sig_yz, pressure])
        vel_x = vel_x + TIME_STEP * buoy * (
            derive(sig_xx, 4, True) + stencil(sxy_pad, 2, False) + derive(sig_xz, 3, False)
        )
        vel_y = vel_y + TIME_STEP * buoy * (
            derive(sig_xy, 4, False) + stencil(syy_pad, 2, True) + derive(sig_yz, 3, False)
        )
        vel_z = vel_z + TIME_STEP * buoy * (
            derive(sig_xz, 4, False) + stencil(syz_pad, 2, False) + derive(sig_zz, 3, True)
        )
        floor_velocity = vel_z[:, :, :, 0, :]
        flow_x = (flow_x - TIME_STEP * water_buoy * derive(pressure, 4, True)) * live
        flow_y = (flow_y - TIME_STEP * water_buoy * stencil(p_pad, 2, True)) * live
        flow_z = (
            flow_z - TIME_STEP * water_buoy * derive(pressure, 3, True)
        ) * above + floor_velocity[:, :, :, None, :] * bottom
        vx_pad, vy_pad, vz_pad, uy_pad = halo_rows([vel_x, vel_y, vel_z, flow_y])
        strain_x = derive(vel_x, 4, False)
        strain_y = stencil(vy_pad, 2, False)
        strain_z = derive(vel_z, 3, False)
        dilation = strain_x + strain_y + strain_z
        shear_xy = stencil(vx_pad, 2, True) + derive(vel_y, 4, True)
        shear_xz = derive(vel_x, 3, True) + derive(vel_z, 4, True)
        shear_yz = derive(vel_y, 3, True) + stencil(vz_pad, 2, True)
        lam_part = lam * dilation
        sig_xx = sig_xx + TIME_STEP * (lam_part + 2.0 * mu * strain_x)
        sig_yy = sig_yy + TIME_STEP * (lam_part + 2.0 * mu * strain_y)
        sig_zz = sig_zz + TIME_STEP * (lam_part + 2.0 * mu * strain_z)
        sig_xy = sig_xy + TIME_STEP * mu * shear_xy
        sig_xz = sig_xz + TIME_STEP * mu * shear_xz
        sig_yz = sig_yz + TIME_STEP * mu * shear_yz
        sig_zz = sig_zz.at[:, :, :, 0, :].set(-floor_pressure)
        lam_acc = lam_acc + dilation[:1] * dilation[1:]
        normal_part = (
            strain_x[:1] * strain_x[1:] + strain_y[:1] * strain_y[1:] + strain_z[:1] * strain_z[1:]
        )
        shear_part = (
            shear_xy[:1] * shear_xy[1:] + shear_xz[:1] * shear_xz[1:] + shear_yz[:1] * shear_yz[1:]
        )
        mu_acc = mu_acc + (2.0 * normal_part + shear_part)
        pressure = (
            pressure
            - TIME_STEP
            * water_kappa
            * (derive(flow_x, 4, False) + stencil(uy_pad, 2, False) + derive(flow_z, 3, False))
        ) * live
        pressure = pressure.at[0].add(wavelet[step][:, None, None, None] * source_hot)
        surface = jnp.sum(pressure[0] * bottom, axis=2)
        partial_record = jnp.einsum(
            "sc,rc->sr",
            surface.reshape(shots, local_y * total_x),
            node_hot,
            precision=lax.Precision.HIGHEST,
        )
        partial_records.append(partial_record)
        local_misfit = partial_record - observed[step]
        inject = jnp.dot(
            local_misfit, node_hot, precision=lax.Precision.HIGHEST, preferred_element_type=jnp.float32
        ).reshape(shots, local_y, total_x)
        kick = inject[:, :, None, :] * bottom
        kappa_acc = jnp.concatenate(
            [kappa_acc + pressure[:1] * pressure[1:], (pressure[0] * kick)[None]], axis=0
        )
        if step + 1 < steps:
            rock_zero = jnp.zeros((1,) + vel_x.shape[1:], jnp.float32)
            water_zero = jnp.zeros((1,) + flow_x.shape[1:], jnp.float32)
            vel_x, vel_y, vel_z = [jnp.concatenate([f, rock_zero]) for f in (vel_x, vel_y, vel_z)]
            sig_xx, sig_yy, sig_zz, sig_xy, sig_xz, sig_yz = [
                jnp.concatenate([f, rock_zero])
                for f in (sig_xx, sig_yy, sig_zz, sig_xy, sig_xz, sig_yz)
            ]
            flow_x, flow_y, flow_z = [jnp.concatenate([f, water_zero]) for f in (flow_x, flow_y, flow_z)]
            pressure = jnp.concatenate([pressure, kick[None]])
            lam_acc = jnp.concatenate([lam_acc, jnp.zeros((1,) + lam_acc.shape[1:], jnp.float32)])
            mu_acc = jnp.concatenate([mu_acc, jnp.zeros((1,) + mu_acc.shape[1:], jnp.float32)])

    recorded = gather_sum(jnp.stack(partial_records), parts)
    misfits = recorded - observed
    scales = lax.rsqrt(jnp.mean(misfits * misfits, axis=2) + 1e-06)
    weights = jnp.concatenate([jnp.ones((1, shots), jnp.float32), scales])
    grad_kappa = jnp.sum(kappa_acc * weights[:, :, None, None, None], axis=(0, 1))
    rock_weights = weights[: lam_acc.shape[0], :, None, None, None]
    grad_lambda = jnp.sum(lam_acc * rock_weights, axis=(0, 1))
    grad_mu = jnp.sum(mu_acc * rock_weights, axis=(0, 1))

    grads = lax.all_to_all(
        jnp.stack([grad_lambda, grad_mu]), "gx", split_axis=3, concat_axis=1, tiled=True
    )
    grads = jnp.transpose(grads, (0, 3, 2, 1))
    return (grads[0], grads[1], grad_kappa, misfits)


def solution(mesh):
    placed = (
        P(None, None, "groups", "gx", None, None),
        P(None, None, "groups", "gx", None, None),
        P("gx", None, None),
        P("gx", None, None),
        P("gx", None, None),
        P("gx", None, None),
        P("gx", None, None),
        P("gx", None),
        P("groups"),
        P(None, "groups"),
        P(),
        P(None, "groups", None),
    )
    return jax.shard_map(
        on_device,
        mesh=mesh,
        in_specs=placed,
        out_specs=(
            P("gx", "groups", None),
            P("gx", "groups", None),
            P("gx", "groups", None),
            P(None, "groups", None),
        ),
        check_vma=False,
    )
```

```python
import jax
import jax.numpy as jnp
from jax import lax
from jax.sharding import PartitionSpec as P

COEFF = (1225.0 / 1024.0, -245.0 / 3072.0, 49.0 / 5120.0, -5.0 / 7168.0)
TIME_STEP = 0.2
HALO = 4
ROW_AXIS = 2
DEPTH_AXIS = 3
DEFERRED = 2


def halo_rows(fields):
    devices = lax.axis_size("gx")
    up = [(i, i + 1) for i in range(devices - 1)]
    down = [(i + 1, i) for i in range(devices - 1)]
    packed = jnp.concatenate(fields, axis=DEPTH_AXIS)
    length = packed.shape[ROW_AXIS]
    before = lax.ppermute(
        lax.slice_in_dim(packed, length - HALO, length, axis=ROW_AXIS), "gx", up
    )
    after = lax.ppermute(lax.slice_in_dim(packed, 0, HALO, axis=ROW_AXIS), "gx", down)
    padded = jnp.concatenate([before, packed, after], axis=ROW_AXIS)
    out, start = [], 0
    for f in fields:
        depth = f.shape[DEPTH_AXIS]
        out.append(lax.slice_in_dim(padded, start, start + depth, axis=DEPTH_AXIS))
        start += depth
    return out


def gather_sum(partial, parts):
    copies = jnp.broadcast_to(partial[None], (parts,) + partial.shape)
    return jnp.sum(lax.all_to_all(copies, "gx", 0, 0, tiled=True), axis=0)


def stencil(padded, axis, forward):
    length = padded.shape[axis] - 8
    summed = None
    for offset in range(1, 5):
        if forward:
            front_at, back_at = (4 + offset, 5 - offset)
        else:
            front_at, back_at = (3 + offset, 4 - offset)
        front = lax.slice_in_dim(padded, front_at, front_at + length, axis=axis)
        back = lax.slice_in_dim(padded, back_at, back_at + length, axis=axis)
        addend = COEFF[offset - 1] * (front - back)
        summed = addend if summed is None else summed + addend
    return summed


def padded_zero(field, axis):
    widths = [(0, 0)] * field.ndim
    widths[axis] = (4, 4)
    return jnp.pad(field, widths)


def derive(field, axis, forward):
    return stencil(padded_zero(field, axis), axis, forward)


def on_device(
    solid_state,
    water_state,
    lame_lambda,
    shear_mu,
    solid_buoy,
    water_kappa,
    water_buoy,
    seafloor,
    source_cell,
    wavelet,
    receiver_column,
    observed,
):
    parts = lax.axis_size("gx")
    place = lax.axis_index("gx")
    n_fields, waves, shots, width_x, rock_z, total_y = solid_state.shape
    local_y = water_state.shape[3]
    depth_rows = water_state.shape[4]
    total_x = water_state.shape[5]
    anchor_y = place * local_y

    rock_in = jnp.concatenate(
        [
            solid_state.reshape(n_fields * waves * shots, width_x, rock_z, total_y),
            jnp.stack([lame_lambda, shear_mu, solid_buoy]),
        ],
        axis=0,
    )
    rock = lax.all_to_all(
        jnp.transpose(rock_in, (0, 3, 2, 1)), "gx", split_axis=1, concat_axis=3, tiled=True
    )
    rock_state = rock[: n_fields * waves * shots].reshape(
        n_fields, waves, shots, local_y, rock_z, total_x
    )
    lam, mu, buoy = rock[-3], rock[-2], rock[-1]

    vel_x, vel_y, vel_z = (rock_state[0], rock_state[1], rock_state[2])
    sig_xx, sig_yy, sig_zz = (rock_state[3], rock_state[4], rock_state[5])
    sig_xy, sig_xz, sig_yz = (rock_state[6], rock_state[7], rock_state[8])
    pressure, flow_x, flow_y, flow_z = (
        water_state[0],
        water_state[1],
        water_state[2],
        water_state[3],
    )
    depth_idx = lax.broadcasted_iota(jnp.int32, (1, depth_rows, 1), 1)
    floor_rows = seafloor[:, None, :]
    live = (depth_idx < floor_rows).astype(jnp.float32)
    bottom = (depth_idx == floor_rows - 1).astype(jnp.float32)
    above = (depth_idx < floor_rows - 1).astype(jnp.float32)
    rows_y = lax.broadcasted_iota(jnp.int32, (local_y, 1, 1), 0) + anchor_y
    cols_x = lax.broadcasted_iota(jnp.int32, (1, 1, total_x), 2)
    flat_cell = (depth_idx * total_y + rows_y) * total_x + cols_x
    source_hot = (flat_cell[None] == source_cell[:, None, None, None]).astype(jnp.float32)
    node_y = receiver_column // total_x
    node_x = receiver_column % total_x
    inside = (node_y >= anchor_y) & (node_y < anchor_y + local_y)
    local_col = (node_y - anchor_y) * total_x + node_x
    column_iota = lax.broadcasted_iota(jnp.int32, (1, local_y * total_x), 1)
    node_hot = ((column_iota == local_col[:, None]) & inside[:, None]).astype(jnp.float32)
    steps = wavelet.shape[0]
    first_late = steps - min(DEFERRED, steps)
    lam_acc = jnp.zeros((1, shots) + lam.shape, jnp.float32)
    mu_acc = jnp.zeros((1, shots) + lam.shape, jnp.float32)
    kappa_acc = jnp.zeros((1, shots) + water_kappa.shape, jnp.float32)
    early_misfits = []
    late_records = []
    for step in range(steps):
        floor_pressure = jnp.sum(pressure * bottom, axis=3)
        sxy_pad, syy_pad, syz_pad, p_pad = halo_rows([sig_xy, sig_yy, sig_yz, pressure])
        vel_x = vel_x + TIME_STEP * buoy * (
            derive(sig_xx, 4, True) + stencil(sxy_pad, 2, False) + derive(sig_xz, 3, False)
        )
        vel_y = vel_y + TIME_STEP * buoy * (
            derive(sig_xy, 4, False) + stencil(syy_pad, 2, True) + derive(sig_yz, 3, False)
        )
        vel_z = vel_z + TIME_STEP * buoy * (
            derive(sig_xz, 4, False) + stencil(syz_pad, 2, False) + derive(sig_zz, 3, True)
        )
        floor_velocity = vel_z[:, :, :, 0, :]
        flow_x = (flow_x - TIME_STEP * water_buoy * derive(pressure, 4, True)) * live
        flow_y = (flow_y - TIME_STEP * water_buoy * stencil(p_pad, 2, True)) * live
        flow_z = (
            flow_z - TIME_STEP * water_buoy * derive(pressure, 3, True)
        ) * above + floor_velocity[:, :, :, None, :] * bottom
        vx_pad, vy_pad, vz_pad, uy_pad = halo_rows([vel_x, vel_y, vel_z, flow_y])
        strain_x = derive(vel_x, 4, False)
        strain_y = stencil(vy_pad, 2, False)
        strain_z = derive(vel_z, 3, False)
        dilation = strain_x + strain_y + strain_z
        shear_xy = stencil(vx_pad, 2, True) + derive(vel_y, 4, True)
        shear_xz = derive(vel_x, 3, True) + derive(vel_z, 4, True)
        shear_yz = derive(vel_y, 3, True) + stencil(vz_pad, 2, True)
        lam_part = lam * dilation
        sig_xx = sig_xx + TIME_STEP * (lam_part + 2.0 * mu * strain_x)
        sig_yy = sig_yy + TIME_STEP * (lam_part + 2.0 * mu * strain_y)
        sig_zz = sig_zz + TIME_STEP * (lam_part + 2.0 * mu * strain_z)
        sig_xy = sig_xy + TIME_STEP * mu * shear_xy
        sig_xz = sig_xz + TIME_STEP * mu * shear_xz
        sig_yz = sig_yz + TIME_STEP * mu * shear_yz
        sig_zz = sig_zz.at[:, :, :, 0, :].set(-floor_pressure)
        lam_acc = lam_acc + dilation[:1] * dilation[1:]
        normal_part = (
            strain_x[:1] * strain_x[1:] + strain_y[:1] * strain_y[1:] + strain_z[:1] * strain_z[1:]
        )
        shear_part = (
            shear_xy[:1] * shear_xy[1:] + shear_xz[:1] * shear_xz[1:] + shear_yz[:1] * shear_yz[1:]
        )
        mu_acc = mu_acc + (2.0 * normal_part + shear_part)
        pressure = (
            pressure
            - TIME_STEP
            * water_kappa
            * (derive(flow_x, 4, False) + stencil(uy_pad, 2, False) + derive(flow_z, 3, False))
        ) * live
        pressure = pressure.at[0].add(wavelet[step][:, None, None, None] * source_hot)
        surface = jnp.sum(pressure[0] * bottom, axis=2)
        partial_record = jnp.einsum(
            "sc,rc->sr",
            surface.reshape(shots, local_y * total_x),
            node_hot,
            precision=lax.Precision.HIGHEST,
        )
        if step < first_late:
            misfit = gather_sum(partial_record, parts) - observed[step]
            scaled = misfit * lax.rsqrt(jnp.mean(misfit * misfit, axis=1, keepdims=True) + 1e-06)
            inject = jnp.dot(
                scaled, node_hot, precision=lax.Precision.HIGHEST, preferred_element_type=jnp.float32
            ).reshape(shots, local_y, total_x)
            pressure = pressure.at[1].add(inject[:, :, None, :] * bottom)
            kappa_acc = kappa_acc + pressure[:1] * pressure[1:]
            early_misfits.append(misfit)
            continue
        late_records.append(partial_record)
        local_misfit = partial_record - observed[step]
        inject = jnp.dot(
            local_misfit, node_hot, precision=lax.Precision.HIGHEST, preferred_element_type=jnp.float32
        ).reshape(shots, local_y, total_x)
        kick = inject[:, :, None, :] * bottom
        kappa_acc = jnp.concatenate(
            [kappa_acc + pressure[:1] * pressure[1:], (pressure[0] * kick)[None]], axis=0
        )
        if step + 1 < steps:
            rock_zero = jnp.zeros((1,) + vel_x.shape[1:], jnp.float32)
            water_zero = jnp.zeros((1,) + flow_x.shape[1:], jnp.float32)
            vel_x, vel_y, vel_z = [jnp.concatenate([f, rock_zero]) for f in (vel_x, vel_y, vel_z)]
            sig_xx, sig_yy, sig_zz, sig_xy, sig_xz, sig_yz = [
                jnp.concatenate([f, rock_zero])
                for f in (sig_xx, sig_yy, sig_zz, sig_xy, sig_xz, sig_yz)
            ]
            flow_x, flow_y, flow_z = [jnp.concatenate([f, water_zero]) for f in (flow_x, flow_y, flow_z)]
            pressure = jnp.concatenate([pressure, kick[None]])
            lam_acc = jnp.concatenate([lam_acc, jnp.zeros((1,) + lam_acc.shape[1:], jnp.float32)])
            mu_acc = jnp.concatenate([mu_acc, jnp.zeros((1,) + mu_acc.shape[1:], jnp.float32)])

    slots = lam_acc.shape[0]
    rock_acc = jnp.concatenate([lam_acc, mu_acc]).reshape(
        2 * slots * shots, local_y, rock_z, parts, width_x
    )
    rock_out = jnp.transpose(rock_acc, (3, 0, 1, 2, 4)).reshape(parts, -1)
    records = jnp.stack(late_records).reshape(1, -1)
    packed = jnp.concatenate([jnp.broadcast_to(records, (parts, records.shape[1])), rock_out], axis=1)
    got = lax.all_to_all(packed, "gx", 0, 0, tiled=True)
    late_count = len(late_records)
    recorded = jnp.sum(got[:, : records.shape[1]], axis=0).reshape(late_count, shots, -1)
    rock_back = got[:, records.shape[1] :].reshape(
        parts, 2 * slots * shots, local_y, rock_z, width_x
    )
    rock_back = jnp.transpose(rock_back, (1, 4, 3, 0, 2)).reshape(
        2, slots, shots, width_x, rock_z, parts * local_y
    )
    late_misfits = recorded - observed[first_late:]
    scales = lax.rsqrt(jnp.mean(late_misfits * late_misfits, axis=2) + 1e-06)
    weights = jnp.concatenate([jnp.ones((1, shots), jnp.float32), scales])
    grad_kappa = jnp.sum(kappa_acc * weights[:, :, None, None, None], axis=(0, 1))
    rock_weights = weights[:slots, :, None, None, None]
    grad_lambda = jnp.sum(rock_back[0] * rock_weights, axis=(0, 1))
    grad_mu = jnp.sum(rock_back[1] * rock_weights, axis=(0, 1))
    misfits = jnp.concatenate([jnp.stack(early_misfits), late_misfits]) if early_misfits else late_misfits
    return (grad_lambda, grad_mu, grad_kappa, misfits)


def solution(mesh):
    placed = (
        P(None, None, "groups", "gx", None, None),
        P(None, None, "groups", "gx", None, None),
        P("gx", None, None),
        P("gx", None, None),
        P("gx", None, None),
        P("gx", None, None),
        P("gx", None, None),
        P("gx", None),
        P("groups"),
        P(None, "groups"),
        P(),
        P(None, "groups", None),
    )
    return jax.shard_map(
        on_device,
        mesh=mesh,
        in_specs=placed,
        out_specs=(
            P("gx", "groups", None),
            P("gx", "groups", None),
            P("gx", "groups", None),
            P(None, "groups", None),
        ),
        check_vma=False,
    )
```

```python
import jax
import jax.numpy as jnp
from jax import lax
from jax.sharding import PartitionSpec as P

COEFF = (1225.0 / 1024.0, -245.0 / 3072.0, 49.0 / 5120.0, -5.0 / 7168.0)
TIME_STEP = 0.2
HALO = 4
ROW_AXIS = 2
DEPTH_AXIS = 3
DEFERRED = 2


def halo_rows(fields):
    devices = lax.axis_size("gx")
    up = [(i, i + 1) for i in range(devices - 1)]
    down = [(i + 1, i) for i in range(devices - 1)]
    packed = jnp.concatenate(fields, axis=DEPTH_AXIS)
    length = packed.shape[ROW_AXIS]
    before = lax.ppermute(
        lax.slice_in_dim(packed, length - HALO, length, axis=ROW_AXIS), "gx", up
    )
    after = lax.ppermute(lax.slice_in_dim(packed, 0, HALO, axis=ROW_AXIS), "gx", down)
    padded = jnp.concatenate([before, packed, after], axis=ROW_AXIS)
    out, start = [], 0
    for f in fields:
        depth = f.shape[DEPTH_AXIS]
        out.append(lax.slice_in_dim(padded, start, start + depth, axis=DEPTH_AXIS))
        start += depth
    return out


def gather_sum(partial, parts):
    copies = jnp.broadcast_to(partial[None], (parts,) + partial.shape)
    return jnp.sum(lax.all_to_all(copies, "gx", 0, 0, tiled=True), axis=0)


def stencil(padded, axis, forward):
    length = padded.shape[axis] - 8
    summed = None
    for offset in range(1, 5):
        if forward:
            front_at, back_at = (4 + offset, 5 - offset)
        else:
            front_at, back_at = (3 + offset, 4 - offset)
        front = lax.slice_in_dim(padded, front_at, front_at + length, axis=axis)
        back = lax.slice_in_dim(padded, back_at, back_at + length, axis=axis)
        addend = COEFF[offset - 1] * (front - back)
        summed = addend if summed is None else summed + addend
    return summed


def padded_zero(field, axis):
    widths = [(0, 0)] * field.ndim
    widths[axis] = (4, 4)
    return jnp.pad(field, widths)


def derive(field, axis, forward):
    return stencil(padded_zero(field, axis), axis, forward)


def on_device(
    solid_state,
    water_state,
    lame_lambda,
    shear_mu,
    solid_buoy,
    water_kappa,
    water_buoy,
    seafloor,
    source_cell,
    wavelet,
    receiver_column,
    observed,
):
    parts = lax.axis_size("gx")
    place = lax.axis_index("gx")
    n_fields, waves, shots, width_x, rock_z, total_y = solid_state.shape
    local_y = water_state.shape[3]
    depth_rows = water_state.shape[4]
    total_x = water_state.shape[5]
    anchor_y = place * local_y

    rock_in = jnp.concatenate(
        [
            solid_state.reshape(n_fields * waves * shots, width_x, rock_z, total_y),
            jnp.stack([lame_lambda, shear_mu, solid_buoy]),
        ],
        axis=0,
    )
    rock = jnp.transpose(
        lax.all_to_all(rock_in, "gx", split_axis=3, concat_axis=1, tiled=True), (0, 3, 2, 1)
    )
    rock_state = rock[: n_fields * waves * shots].reshape(
        n_fields, waves, shots, local_y, rock_z, total_x
    )
    lam, mu, buoy = rock[-3], rock[-2], rock[-1]

    vel_x, vel_y, vel_z = (rock_state[0], rock_state[1], rock_state[2])
    sig_xx, sig_yy, sig_zz = (rock_state[3], rock_state[4], rock_state[5])
    sig_xy, sig_xz, sig_yz = (rock_state[6], rock_state[7], rock_state[8])
    pressure, flow_x, flow_y, flow_z = (
        water_state[0],
        water_state[1],
        water_state[2],
        water_state[3],
    )
    depth_idx = lax.broadcasted_iota(jnp.int32, (1, depth_rows, 1), 1)
    floor_rows = seafloor[:, None, :]
    live = (depth_idx < floor_rows).astype(jnp.float32)
    bottom = (depth_idx == floor_rows - 1).astype(jnp.float32)
    above = (depth_idx < floor_rows - 1).astype(jnp.float32)
    rows_y = lax.broadcasted_iota(jnp.int32, (local_y, 1, 1), 0) + anchor_y
    cols_x = lax.broadcasted_iota(jnp.int32, (1, 1, total_x), 2)
    flat_cell = (depth_idx * total_y + rows_y) * total_x + cols_x
    source_hot = (flat_cell[None] == source_cell[:, None, None, None]).astype(jnp.float32)
    node_y = receiver_column // total_x
    node_x = receiver_column % total_x
    inside = (node_y >= anchor_y) & (node_y < anchor_y + local_y)
    local_col = (node_y - anchor_y) * total_x + node_x
    column_iota = lax.broadcasted_iota(jnp.int32, (1, local_y * total_x), 1)
    node_hot = ((column_iota == local_col[:, None]) & inside[:, None]).astype(jnp.float32)
    steps = wavelet.shape[0]
    first_late = steps - min(DEFERRED, steps)
    lam_acc = jnp.zeros((1, shots) + lam.shape, jnp.float32)
    mu_acc = jnp.zeros((1, shots) + lam.shape, jnp.float32)
    kappa_acc = jnp.zeros((1, shots) + water_kappa.shape, jnp.float32)
    early_misfits = []
    late_records = []
    for step in range(steps):
        floor_pressure = jnp.sum(pressure * bottom, axis=3)
        sxy_pad, syy_pad, syz_pad, p_pad = halo_rows([sig_xy, sig_yy, sig_yz, pressure])
        vel_x = vel_x + TIME_STEP * buoy * (
            derive(sig_xx, 4, True) + stencil(sxy_pad, 2, False) + derive(sig_xz, 3, False)
        )
        vel_y = vel_y + TIME_STEP * buoy * (
            derive(sig_xy, 4, False) + stencil(syy_pad, 2, True) + derive(sig_yz, 3, False)
        )
        vel_z = vel_z + TIME_STEP * buoy * (
            derive(sig_xz, 4, False) + stencil(syz_pad, 2, False) + derive(sig_zz, 3, True)
        )
        floor_velocity = vel_z[:, :, :, 0, :]
        flow_x = (flow_x - TIME_STEP * water_buoy * derive(pressure, 4, True)) * live
        flow_y = (flow_y - TIME_STEP * water_buoy * stencil(p_pad, 2, True)) * live
        flow_z = (
            flow_z - TIME_STEP * water_buoy * derive(pressure, 3, True)
        ) * above + floor_velocity[:, :, :, None, :] * bottom
        vx_pad, vy_pad, vz_pad, uy_pad = halo_rows([vel_x, vel_y, vel_z, flow_y])
        strain_x = derive(vel_x, 4, False)
        strain_y = stencil(vy_pad, 2, False)
        strain_z = derive(vel_z, 3, False)
        dilation = strain_x + strain_y + strain_z
        shear_xy = stencil(vx_pad, 2, True) + derive(vel_y, 4, True)
        shear_xz = derive(vel_x, 3, True) + derive(vel_z, 4, True)
        shear_yz = derive(vel_y, 3, True) + stencil(vz_pad, 2, True)
        lam_part = lam * dilation
        sig_xx = sig_xx + TIME_STEP * (lam_part + 2.0 * mu * strain_x)
        sig_yy = sig_yy + TIME_STEP * (lam_part + 2.0 * mu * strain_y)
        sig_zz = sig_zz + TIME_STEP * (lam_part + 2.0 * mu * strain_z)
        sig_xy = sig_xy + TIME_STEP * mu * shear_xy
        sig_xz = sig_xz + TIME_STEP * mu * shear_xz
        sig_yz = sig_yz + TIME_STEP * mu * shear_yz
        sig_zz = sig_zz.at[:, :, :, 0, :].set(-floor_pressure)
        lam_acc = lam_acc + dilation[:1] * dilation[1:]
        normal_part = (
            strain_x[:1] * strain_x[1:] + strain_y[:1] * strain_y[1:] + strain_z[:1] * strain_z[1:]
        )
        shear_part = (
            shear_xy[:1] * shear_xy[1:] + shear_xz[:1] * shear_xz[1:] + shear_yz[:1] * shear_yz[1:]
        )
        mu_acc = mu_acc + (2.0 * normal_part + shear_part)
        pressure = (
            pressure
            - TIME_STEP
            * water_kappa
            * (derive(flow_x, 4, False) + stencil(uy_pad, 2, False) + derive(flow_z, 3, False))
        ) * live
        pressure = pressure.at[0].add(wavelet[step][:, None, None, None] * source_hot)
        surface = jnp.sum(pressure[0] * bottom, axis=2)
        partial_record = jnp.einsum(
            "sc,rc->sr",
            surface.reshape(shots, local_y * total_x),
            node_hot,
            precision=lax.Precision.HIGHEST,
        )
        if step < first_late:
            misfit = gather_sum(partial_record, parts) - observed[step]
            scaled = misfit * lax.rsqrt(jnp.mean(misfit * misfit, axis=1, keepdims=True) + 1e-06)
            inject = jnp.dot(
                scaled, node_hot, precision=lax.Precision.HIGHEST, preferred_element_type=jnp.float32
            ).reshape(shots, local_y, total_x)
            pressure = pressure.at[1].add(inject[:, :, None, :] * bottom)
            kappa_acc = kappa_acc + pressure[:1] * pressure[1:]
            early_misfits.append(misfit)
            continue
        late_records.append(partial_record)
        local_misfit = partial_record - observed[step]
        inject = jnp.dot(
            local_misfit, node_hot, precision=lax.Precision.HIGHEST, preferred_element_type=jnp.float32
        ).reshape(shots, local_y, total_x)
        kick = inject[:, :, None, :] * bottom
        kappa_acc = jnp.concatenate(
            [kappa_acc + pressure[:1] * pressure[1:], (pressure[0] * kick)[None]], axis=0
        )
        if step + 1 < steps:
            rock_zero = jnp.zeros((1,) + vel_x.shape[1:], jnp.float32)
            water_zero = jnp.zeros((1,) + flow_x.shape[1:], jnp.float32)
            vel_x, vel_y, vel_z = [jnp.concatenate([f, rock_zero]) for f in (vel_x, vel_y, vel_z)]
            sig_xx, sig_yy, sig_zz, sig_xy, sig_xz, sig_yz = [
                jnp.concatenate([f, rock_zero])
                for f in (sig_xx, sig_yy, sig_zz, sig_xy, sig_xz, sig_yz)
            ]
            flow_x, flow_y, flow_z = [jnp.concatenate([f, water_zero]) for f in (flow_x, flow_y, flow_z)]
            pressure = jnp.concatenate([pressure, kick[None]])
            lam_acc = jnp.concatenate([lam_acc, jnp.zeros((1,) + lam_acc.shape[1:], jnp.float32)])
            mu_acc = jnp.concatenate([mu_acc, jnp.zeros((1,) + mu_acc.shape[1:], jnp.float32)])

    slots = lam_acc.shape[0]
    rock_acc = jnp.concatenate([lam_acc, mu_acc]).reshape(
        2 * slots * shots, local_y, rock_z, parts, width_x
    )
    rock_out = jnp.transpose(rock_acc, (3, 0, 1, 2, 4)).reshape(parts, -1)
    records = jnp.stack(late_records).reshape(1, -1)
    packed = jnp.concatenate([jnp.broadcast_to(records, (parts, records.shape[1])), rock_out], axis=1)
    got = lax.all_to_all(packed, "gx", 0, 0, tiled=True)
    late_count = len(late_records)
    recorded = jnp.sum(got[:, : records.shape[1]], axis=0).reshape(late_count, shots, -1)
    rock_back = got[:, records.shape[1] :].reshape(
        parts, 2 * slots * shots, local_y, rock_z, width_x
    )
    rock_back = jnp.transpose(rock_back, (1, 4, 3, 0, 2)).reshape(
        2, slots, shots, width_x, rock_z, parts * local_y
    )
    late_misfits = recorded - observed[first_late:]
    scales = lax.rsqrt(jnp.mean(late_misfits * late_misfits, axis=2) + 1e-06)
    weights = jnp.concatenate([jnp.ones((1, shots), jnp.float32), scales])
    grad_kappa = jnp.sum(kappa_acc * weights[:, :, None, None, None], axis=(0, 1))
    rock_weights = weights[:slots, :, None, None, None]
    grad_lambda = jnp.sum(rock_back[0] * rock_weights, axis=(0, 1))
    grad_mu = jnp.sum(rock_back[1] * rock_weights, axis=(0, 1))
    misfits = jnp.concatenate([jnp.stack(early_misfits), late_misfits]) if early_misfits else late_misfits
    return (grad_lambda, grad_mu, grad_kappa, misfits)


def solution(mesh):
    placed = (
        P(None, None, "groups", "gx", None, None),
        P(None, None, "groups", "gx", None, None),
        P("gx", None, None),
        P("gx", None, None),
        P("gx", None, None),
        P("gx", None, None),
        P("gx", None, None),
        P("gx", None),
        P("groups"),
        P(None, "groups"),
        P(),
        P(None, "groups", None),
    )
    return jax.shard_map(
        on_device,
        mesh=mesh,
        in_specs=placed,
        out_specs=(
            P("gx", "groups", None),
            P("gx", "groups", None),
            P("gx", "groups", None),
            P(None, "groups", None),
        ),
        check_vma=False,
    )
```

```python
import jax
import jax.numpy as jnp
from jax import lax
from jax.sharding import PartitionSpec as P

COEFF = (1225.0 / 1024.0, -245.0 / 3072.0, 49.0 / 5120.0, -5.0 / 7168.0)
TIME_STEP = 0.2
HALO = 4
ROW_AXIS = 2
DEPTH_AXIS = 3
DEFERRED = 2


def halo_rows(fields):
    devices = lax.axis_size("gx")
    up = [(i, i + 1) for i in range(devices - 1)]
    down = [(i + 1, i) for i in range(devices - 1)]
    packed = jnp.concatenate(fields, axis=DEPTH_AXIS)
    length = packed.shape[ROW_AXIS]
    before = lax.ppermute(
        lax.slice_in_dim(packed, length - HALO, length, axis=ROW_AXIS), "gx", up
    )
    after = lax.ppermute(lax.slice_in_dim(packed, 0, HALO, axis=ROW_AXIS), "gx", down)
    padded = jnp.concatenate([before, packed, after], axis=ROW_AXIS)
    out, start = [], 0
    for f in fields:
        depth = f.shape[DEPTH_AXIS]
        out.append(lax.slice_in_dim(padded, start, start + depth, axis=DEPTH_AXIS))
        start += depth
    return out


def gather_sum(partial, parts):
    copies = jnp.broadcast_to(partial[None], (parts,) + partial.shape)
    return jnp.sum(lax.all_to_all(copies, "gx", 0, 0, tiled=True), axis=0)


def stencil(padded, axis, forward):
    length = padded.shape[axis] - 8
    summed = None
    for offset in range(1, 5):
        if forward:
            front_at, back_at = (4 + offset, 5 - offset)
        else:
            front_at, back_at = (3 + offset, 4 - offset)
        front = lax.slice_in_dim(padded, front_at, front_at + length, axis=axis)
        back = lax.slice_in_dim(padded, back_at, back_at + length, axis=axis)
        addend = COEFF[offset - 1] * (front - back)
        summed = addend if summed is None else summed + addend
    return summed


def padded_zero(field, axis):
    widths = [(0, 0)] * field.ndim
    widths[axis] = (4, 4)
    return jnp.pad(field, widths)


def derive(field, axis, forward):
    return stencil(padded_zero(field, axis), axis, forward)


def on_device(
    solid_state,
    water_state,
    lame_lambda,
    shear_mu,
    solid_buoy,
    water_kappa,
    water_buoy,
    seafloor,
    source_cell,
    wavelet,
    receiver_column,
    observed,
):
    parts = lax.axis_size("gx")
    place = lax.axis_index("gx")
    n_fields, waves, shots, width_x, rock_z, total_y = solid_state.shape
    local_y = water_state.shape[3]
    depth_rows = water_state.shape[4]
    total_x = water_state.shape[5]
    anchor_y = place * local_y

    rock_in = jnp.concatenate(
        [
            solid_state.reshape(n_fields * waves * shots, width_x, rock_z, total_y),
            jnp.stack([lame_lambda, shear_mu, solid_buoy]),
        ],
        axis=0,
    )
    rock = jnp.transpose(
        lax.all_to_all(rock_in, "gx", split_axis=3, concat_axis=1, tiled=True), (0, 3, 2, 1)
    )
    rock_state = rock[: n_fields * waves * shots].reshape(
        n_fields, waves, shots, local_y, rock_z, total_x
    )
    lam, mu, buoy = rock[-3], rock[-2], rock[-1]

    vel_x, vel_y, vel_z = (rock_state[0], rock_state[1], rock_state[2])
    sig_xx, sig_yy, sig_zz = (rock_state[3], rock_state[4], rock_state[5])
    sig_xy, sig_xz, sig_yz = (rock_state[6], rock_state[7], rock_state[8])
    pressure, flow_x, flow_y, flow_z = (
        water_state[0],
        water_state[1],
        water_state[2],
        water_state[3],
    )
    depth_idx = lax.broadcasted_iota(jnp.int32, (1, depth_rows, 1), 1)
    floor_rows = seafloor[:, None, :]
    live = (depth_idx < floor_rows).astype(jnp.float32)
    bottom = (depth_idx == floor_rows - 1).astype(jnp.float32)
    above = (depth_idx < floor_rows - 1).astype(jnp.float32)
    rows_y = lax.broadcasted_iota(jnp.int32, (local_y, 1, 1), 0) + anchor_y
    cols_x = lax.broadcasted_iota(jnp.int32, (1, 1, total_x), 2)
    flat_cell = (depth_idx * total_y + rows_y) * total_x + cols_x
    source_hot = (flat_cell[None] == source_cell[:, None, None, None]).astype(jnp.float32)
    node_y = receiver_column // total_x
    node_x = receiver_column % total_x
    inside = (node_y >= anchor_y) & (node_y < anchor_y + local_y)
    local_col = (node_y - anchor_y) * total_x + node_x
    column_iota = lax.broadcasted_iota(jnp.int32, (1, local_y * total_x), 1)
    node_hot = ((column_iota == local_col[:, None]) & inside[:, None]).astype(jnp.float32)
    steps = wavelet.shape[0]
    first_late = steps - min(DEFERRED, steps)
    lam_acc = jnp.zeros((1, shots) + lam.shape, jnp.float32)
    mu_acc = jnp.zeros((1, shots) + lam.shape, jnp.float32)
    kappa_acc = jnp.zeros((1, shots) + water_kappa.shape, jnp.float32)
    early_misfits = []
    late_records = []
    for step in range(steps):
        floor_pressure = jnp.sum(pressure * bottom, axis=3)
        if step == 0:
            (p_pad,) = halo_rows([pressure])
            sxy_pad, syy_pad, syz_pad = halo_rows([sig_xy, sig_yy, sig_yz])
        else:
            sxy_pad, syy_pad, syz_pad, p_pad = halo_rows([sig_xy, sig_yy, sig_yz, pressure])
        vel_x = vel_x + TIME_STEP * buoy * (
            derive(sig_xx, 4, True) + stencil(sxy_pad, 2, False) + derive(sig_xz, 3, False)
        )
        vel_y = vel_y + TIME_STEP * buoy * (
            derive(sig_xy, 4, False) + stencil(syy_pad, 2, True) + derive(sig_yz, 3, False)
        )
        vel_z = vel_z + TIME_STEP * buoy * (
            derive(sig_xz, 4, False) + stencil(syz_pad, 2, False) + derive(sig_zz, 3, True)
        )
        floor_velocity = vel_z[:, :, :, 0, :]
        flow_x = (flow_x - TIME_STEP * water_buoy * derive(pressure, 4, True)) * live
        flow_y = (flow_y - TIME_STEP * water_buoy * stencil(p_pad, 2, True)) * live
        flow_z = (
            flow_z - TIME_STEP * water_buoy * derive(pressure, 3, True)
        ) * above + floor_velocity[:, :, :, None, :] * bottom
        vx_pad, vy_pad, vz_pad, uy_pad = halo_rows([vel_x, vel_y, vel_z, flow_y])
        strain_x = derive(vel_x, 4, False)
        strain_y = stencil(vy_pad, 2, False)
        strain_z = derive(vel_z, 3, False)
        dilation = strain_x + strain_y + strain_z
        shear_xy = stencil(vx_pad, 2, True) + derive(vel_y, 4, True)
        shear_xz = derive(vel_x, 3, True) + derive(vel_z, 4, True)
        shear_yz = derive(vel_y, 3, True) + stencil(vz_pad, 2, True)
        lam_part = lam * dilation
        sig_xx = sig_xx + TIME_STEP * (lam_part + 2.0 * mu * strain_x)
        sig_yy = sig_yy + TIME_STEP * (lam_part + 2.0 * mu * strain_y)
        sig_zz = sig_zz + TIME_STEP * (lam_part + 2.0 * mu * strain_z)
        sig_xy = sig_xy + TIME_STEP * mu * shear_xy
        sig_xz = sig_xz + TIME_STEP * mu * shear_xz
        sig_yz = sig_yz + TIME_STEP * mu * shear_yz
        sig_zz = sig_zz.at[:, :, :, 0, :].set(-floor_pressure)
        lam_acc = lam_acc + dilation[:1] * dilation[1:]
        normal_part = (
            strain_x[:1] * strain_x[1:] + strain_y[:1] * strain_y[1:] + strain_z[:1] * strain_z[1:]
        )
        shear_part = (
            shear_xy[:1] * shear_xy[1:] + shear_xz[:1] * shear_xz[1:] + shear_yz[:1] * shear_yz[1:]
        )
        mu_acc = mu_acc + (2.0 * normal_part + shear_part)
        pressure = (
            pressure
            - TIME_STEP
            * water_kappa
            * (derive(flow_x, 4, False) + stencil(uy_pad, 2, False) + derive(flow_z, 3, False))
        ) * live
        pressure = pressure.at[0].add(wavelet[step][:, None, None, None] * source_hot)
        surface = jnp.sum(pressure[0] * bottom, axis=2)
        partial_record = jnp.einsum(
            "sc,rc->sr",
            surface.reshape(shots, local_y * total_x),
            node_hot,
            precision=lax.Precision.HIGHEST,
        )
        if step < first_late:
            misfit = gather_sum(partial_record, parts) - observed[step]
            scaled = misfit * lax.rsqrt(jnp.mean(misfit * misfit, axis=1, keepdims=True) + 1e-06)
            inject = jnp.dot(
                scaled, node_hot, precision=lax.Precision.HIGHEST, preferred_element_type=jnp.float32
            ).reshape(shots, local_y, total_x)
            pressure = pressure.at[1].add(inject[:, :, None, :] * bottom)
            kappa_acc = kappa_acc + pressure[:1] * pressure[1:]
            early_misfits.append(misfit)
            continue
        late_records.append(partial_record)
        local_misfit = partial_record - observed[step]
        inject = jnp.dot(
            local_misfit, node_hot, precision=lax.Precision.HIGHEST, preferred_element_type=jnp.float32
        ).reshape(shots, local_y, total_x)
        kick = inject[:, :, None, :] * bottom
        kappa_acc = jnp.concatenate(
            [kappa_acc + pressure[:1] * pressure[1:], (pressure[0] * kick)[None]], axis=0
        )
        if step + 1 < steps:
            rock_zero = jnp.zeros((1,) + vel_x.shape[1:], jnp.float32)
            water_zero = jnp.zeros((1,) + flow_x.shape[1:], jnp.float32)
            vel_x, vel_y, vel_z = [jnp.concatenate([f, rock_zero]) for f in (vel_x, vel_y, vel_z)]
            sig_xx, sig_yy, sig_zz, sig_xy, sig_xz, sig_yz = [
                jnp.concatenate([f, rock_zero])
                for f in (sig_xx, sig_yy, sig_zz, sig_xy, sig_xz, sig_yz)
            ]
            flow_x, flow_y, flow_z = [jnp.concatenate([f, water_zero]) for f in (flow_x, flow_y, flow_z)]
            pressure = jnp.concatenate([pressure, kick[None]])
            lam_acc = jnp.concatenate([lam_acc, jnp.zeros((1,) + lam_acc.shape[1:], jnp.float32)])
            mu_acc = jnp.concatenate([mu_acc, jnp.zeros((1,) + mu_acc.shape[1:], jnp.float32)])

    slots = lam_acc.shape[0]
    rock_acc = jnp.concatenate([lam_acc, mu_acc]).reshape(
        2 * slots * shots, local_y, rock_z, parts, width_x
    )
    rock_out = jnp.transpose(rock_acc, (3, 0, 1, 2, 4)).reshape(parts, -1)
    records = jnp.stack(late_records).reshape(1, -1)
    packed = jnp.concatenate([jnp.broadcast_to(records, (parts, records.shape[1])), rock_out], axis=1)
    got = lax.all_to_all(packed, "gx", 0, 0, tiled=True)
    late_count = len(late_records)
    recorded = jnp.sum(got[:, : records.shape[1]], axis=0).reshape(late_count, shots, -1)
    rock_back = got[:, records.shape[1] :].reshape(
        parts, 2 * slots * shots, local_y, rock_z, width_x
    )
    rock_back = jnp.transpose(rock_back, (1, 4, 3, 0, 2)).reshape(
        2, slots, shots, width_x, rock_z, parts * local_y
    )
    late_misfits = recorded - observed[first_late:]
    scales = lax.rsqrt(jnp.mean(late_misfits * late_misfits, axis=2) + 1e-06)
    weights = jnp.concatenate([jnp.ones((1, shots), jnp.float32), scales])
    grad_kappa = jnp.sum(kappa_acc * weights[:, :, None, None, None], axis=(0, 1))
    rock_weights = weights[:slots, :, None, None, None]
    grad_lambda = jnp.sum(rock_back[0] * rock_weights, axis=(0, 1))
    grad_mu = jnp.sum(rock_back[1] * rock_weights, axis=(0, 1))
    misfits = jnp.concatenate([jnp.stack(early_misfits), late_misfits]) if early_misfits else late_misfits
    return (grad_lambda, grad_mu, grad_kappa, misfits)


def solution(mesh):
    placed = (
        P(None, None, "groups", "gx", None, None),
        P(None, None, "groups", "gx", None, None),
        P("gx", None, None),
        P("gx", None, None),
        P("gx", None, None),
        P("gx", None, None),
        P("gx", None, None),
        P("gx", None),
        P("groups"),
        P(None, "groups"),
        P(),
        P(None, "groups", None),
    )
    return jax.shard_map(
        on_device,
        mesh=mesh,
        in_specs=placed,
        out_specs=(
            P("gx", "groups", None),
            P("gx", "groups", None),
            P("gx", "groups", None),
            P(None, "groups", None),
        ),
        check_vma=False,
    )
```

```python
import jax
import jax.numpy as jnp
from jax import lax
from jax.sharding import PartitionSpec as P

COEFF = (1225.0 / 1024.0, -245.0 / 3072.0, 49.0 / 5120.0, -5.0 / 7168.0)
TIME_STEP = 0.2
HALO = 4
ROW_AXIS = 2
DEPTH_AXIS = 3
DEFERRED = 2


def halo_rows(fields):
    devices = lax.axis_size("gx")
    up = [(i, i + 1) for i in range(devices - 1)]
    down = [(i + 1, i) for i in range(devices - 1)]
    packed = jnp.concatenate(fields, axis=DEPTH_AXIS)
    length = packed.shape[ROW_AXIS]
    before = lax.ppermute(
        lax.slice_in_dim(packed, length - HALO, length, axis=ROW_AXIS), "gx", up
    )
    after = lax.ppermute(lax.slice_in_dim(packed, 0, HALO, axis=ROW_AXIS), "gx", down)
    padded = jnp.concatenate([before, packed, after], axis=ROW_AXIS)
    out, start = [], 0
    for f in fields:
        depth = f.shape[DEPTH_AXIS]
        out.append(lax.slice_in_dim(padded, start, start + depth, axis=DEPTH_AXIS))
        start += depth
    return out


def fill_waves(field, waves):
    extra = waves - field.shape[0]
    if extra == 0:
        return field
    return jnp.concatenate([field, jnp.zeros((extra,) + field.shape[1:], field.dtype)])


def gather_sum(partial, parts):
    copies = jnp.broadcast_to(partial[None], (parts,) + partial.shape)
    return jnp.sum(lax.all_to_all(copies, "gx", 0, 0, tiled=True), axis=0)


def stencil(padded, axis, forward):
    length = padded.shape[axis] - 8
    summed = None
    for offset in range(1, 5):
        if forward:
            front_at, back_at = (4 + offset, 5 - offset)
        else:
            front_at, back_at = (3 + offset, 4 - offset)
        front = lax.slice_in_dim(padded, front_at, front_at + length, axis=axis)
        back = lax.slice_in_dim(padded, back_at, back_at + length, axis=axis)
        addend = COEFF[offset - 1] * (front - back)
        summed = addend if summed is None else summed + addend
    return summed


def padded_zero(field, axis):
    widths = [(0, 0)] * field.ndim
    widths[axis] = (4, 4)
    return jnp.pad(field, widths)


def derive(field, axis, forward):
    return stencil(padded_zero(field, axis), axis, forward)


def on_device(
    solid_state,
    water_state,
    lame_lambda,
    shear_mu,
    solid_buoy,
    water_kappa,
    water_buoy,
    seafloor,
    source_cell,
    wavelet,
    receiver_column,
    observed,
):
    parts = lax.axis_size("gx")
    place = lax.axis_index("gx")
    n_fields, waves, shots, width_x, rock_z, total_y = solid_state.shape
    local_y = water_state.shape[3]
    depth_rows = water_state.shape[4]
    total_x = water_state.shape[5]
    anchor_y = place * local_y

    rock_in = jnp.concatenate(
        [
            solid_state.reshape(n_fields * waves * shots, width_x, rock_z, total_y),
            jnp.stack([lame_lambda, shear_mu, solid_buoy]),
        ],
        axis=0,
    )
    rock = jnp.transpose(
        lax.all_to_all(rock_in, "gx", split_axis=3, concat_axis=1, tiled=True), (0, 3, 2, 1)
    )
    rock_state = rock[: n_fields * waves * shots].reshape(
        n_fields, waves, shots, local_y, rock_z, total_x
    )
    lam, mu, buoy = rock[-3], rock[-2], rock[-1]

    vel_x, vel_y, vel_z = (rock_state[0], rock_state[1], rock_state[2])
    sig_xx, sig_yy, sig_zz = (rock_state[3], rock_state[4], rock_state[5])
    sig_xy, sig_xz, sig_yz = (rock_state[6], rock_state[7], rock_state[8])
    pressure, flow_x, flow_y, flow_z = (
        water_state[0],
        water_state[1],
        water_state[2],
        water_state[3],
    )
    depth_idx = lax.broadcasted_iota(jnp.int32, (1, depth_rows, 1), 1)
    floor_rows = seafloor[:, None, :]
    live = (depth_idx < floor_rows).astype(jnp.float32)
    bottom = (depth_idx == floor_rows - 1).astype(jnp.float32)
    above = (depth_idx < floor_rows - 1).astype(jnp.float32)
    rows_y = lax.broadcasted_iota(jnp.int32, (local_y, 1, 1), 0) + anchor_y
    cols_x = lax.broadcasted_iota(jnp.int32, (1, 1, total_x), 2)
    flat_cell = (depth_idx * total_y + rows_y) * total_x + cols_x
    source_hot = (flat_cell[None] == source_cell[:, None, None, None]).astype(jnp.float32)
    node_y = receiver_column // total_x
    node_x = receiver_column % total_x
    inside = (node_y >= anchor_y) & (node_y < anchor_y + local_y)
    local_col = (node_y - anchor_y) * total_x + node_x
    column_iota = lax.broadcasted_iota(jnp.int32, (1, local_y * total_x), 1)
    node_hot = ((column_iota == local_col[:, None]) & inside[:, None]).astype(jnp.float32)
    steps = wavelet.shape[0]
    first_late = steps - min(DEFERRED, steps)
    lam_acc = jnp.zeros((1, shots) + lam.shape, jnp.float32)
    mu_acc = jnp.zeros((1, shots) + lam.shape, jnp.float32)
    kappa_acc = jnp.zeros((1, shots) + water_kappa.shape, jnp.float32)
    early_misfits = []
    late_records = []
    pending = []
    for step in range(steps):
        if pending and pending[0][0] == step - 2:
            _, saved_floor = pending.pop(0)
            rock_zero = jnp.zeros((1,) + vel_x.shape[1:], jnp.float32)
            vel_x, vel_y, vel_z = [jnp.concatenate([f, rock_zero]) for f in (vel_x, vel_y, vel_z)]
            sig_xx, sig_yy, sig_xy, sig_xz, sig_yz = [
                jnp.concatenate([f, rock_zero]) for f in (sig_xx, sig_yy, sig_xy, sig_xz, sig_yz)
            ]
            sig_zz = jnp.concatenate([sig_zz, rock_zero.at[:, :, :, 0, :].set(-saved_floor)])
            lam_acc = jnp.concatenate([lam_acc, jnp.zeros((1,) + lam_acc.shape[1:], jnp.float32)])
            mu_acc = jnp.concatenate([mu_acc, jnp.zeros((1,) + mu_acc.shape[1:], jnp.float32)])
        rock_waves = vel_x.shape[0]
        water_waves = pressure.shape[0]
        floor_pressure = jnp.sum(pressure * bottom, axis=3)
        pending = [(at, floor_pressure[rock_waves + i : rock_waves + i + 1]) for i, (at, _) in enumerate(pending)]
        sxy_pad, syy_pad, syz_pad, p_pad = halo_rows(
            [fill_waves(f, water_waves) for f in (sig_xy, sig_yy, sig_yz)] + [pressure]
        )
        sxy_pad, syy_pad, syz_pad = [f[:rock_waves] for f in (sxy_pad, syy_pad, syz_pad)]
        vel_x = vel_x + TIME_STEP * buoy * (
            derive(sig_xx, 4, True) + stencil(sxy_pad, 2, False) + derive(sig_xz, 3, False)
        )
        vel_y = vel_y + TIME_STEP * buoy * (
            derive(sig_xy, 4, False) + stencil(syy_pad, 2, True) + derive(sig_yz, 3, False)
        )
        vel_z = vel_z + TIME_STEP * buoy * (
            derive(sig_xz, 4, False) + stencil(syz_pad, 2, False) + derive(sig_zz, 3, True)
        )
        floor_velocity = fill_waves(vel_z[:, :, :, 0, :], water_waves)
        flow_x = (flow_x - TIME_STEP * water_buoy * derive(pressure, 4, True)) * live
        flow_y = (flow_y - TIME_STEP * water_buoy * stencil(p_pad, 2, True)) * live
        flow_z = (
            flow_z - TIME_STEP * water_buoy * derive(pressure, 3, True)
        ) * above + floor_velocity[:, :, :, None, :] * bottom
        vx_pad, vy_pad, vz_pad, uy_pad = halo_rows(
            [fill_waves(f, water_waves) for f in (vel_x, vel_y, vel_z)] + [flow_y]
        )
        vx_pad, vy_pad, vz_pad = [f[:rock_waves] for f in (vx_pad, vy_pad, vz_pad)]
        strain_x = derive(vel_x, 4, False)
        strain_y = stencil(vy_pad, 2, False)
        strain_z = derive(vel_z, 3, False)
        dilation = strain_x + strain_y + strain_z
        shear_xy = stencil(vx_pad, 2, True) + derive(vel_y, 4, True)
        shear_xz = derive(vel_x, 3, True) + derive(vel_z, 4, True)
        shear_yz = derive(vel_y, 3, True) + stencil(vz_pad, 2, True)
        lam_part = lam * dilation
        sig_xx = sig_xx + TIME_STEP * (lam_part + 2.0 * mu * strain_x)
        sig_yy = sig_yy + TIME_STEP * (lam_part + 2.0 * mu * strain_y)
        sig_zz = sig_zz + TIME_STEP * (lam_part + 2.0 * mu * strain_z)
        sig_xy = sig_xy + TIME_STEP * mu * shear_xy
        sig_xz = sig_xz + TIME_STEP * mu * shear_xz
        sig_yz = sig_yz + TIME_STEP * mu * shear_yz
        sig_zz = sig_zz.at[:, :, :, 0, :].set(-floor_pressure[:rock_waves])
        lam_acc = lam_acc + dilation[:1] * dilation[1:]
        normal_part = (
            strain_x[:1] * strain_x[1:] + strain_y[:1] * strain_y[1:] + strain_z[:1] * strain_z[1:]
        )
        shear_part = (
            shear_xy[:1] * shear_xy[1:] + shear_xz[:1] * shear_xz[1:] + shear_yz[:1] * shear_yz[1:]
        )
        mu_acc = mu_acc + (2.0 * normal_part + shear_part)
        pressure = (
            pressure
            - TIME_STEP
            * water_kappa
            * (derive(flow_x, 4, False) + stencil(uy_pad, 2, False) + derive(flow_z, 3, False))
        ) * live
        pressure = pressure.at[0].add(wavelet[step][:, None, None, None] * source_hot)
        surface = jnp.sum(pressure[0] * bottom, axis=2)
        partial_record = jnp.einsum(
            "sc,rc->sr",
            surface.reshape(shots, local_y * total_x),
            node_hot,
            precision=lax.Precision.HIGHEST,
        )
        if step < first_late:
            misfit = gather_sum(partial_record, parts) - observed[step]
            scaled = misfit * lax.rsqrt(jnp.mean(misfit * misfit, axis=1, keepdims=True) + 1e-06)
            inject = jnp.dot(
                scaled, node_hot, precision=lax.Precision.HIGHEST, preferred_element_type=jnp.float32
            ).reshape(shots, local_y, total_x)
            pressure = pressure.at[1].add(inject[:, :, None, :] * bottom)
            kappa_acc = kappa_acc + pressure[:1] * pressure[1:]
            early_misfits.append(misfit)
            continue
        late_records.append(partial_record)
        local_misfit = partial_record - observed[step]
        inject = jnp.dot(
            local_misfit, node_hot, precision=lax.Precision.HIGHEST, preferred_element_type=jnp.float32
        ).reshape(shots, local_y, total_x)
        kick = inject[:, :, None, :] * bottom
        kappa_acc = jnp.concatenate(
            [kappa_acc + pressure[:1] * pressure[1:], (pressure[0] * kick)[None]], axis=0
        )
        if step + 1 < steps:
            water_zero = jnp.zeros((1,) + flow_x.shape[1:], jnp.float32)
            flow_x, flow_y, flow_z = [jnp.concatenate([f, water_zero]) for f in (flow_x, flow_y, flow_z)]
            pressure = jnp.concatenate([pressure, kick[None]])
            pending.append((step, None))

    slots = lam_acc.shape[0]
    rock_acc = jnp.concatenate([lam_acc, mu_acc]).reshape(
        2 * slots * shots, local_y, rock_z, parts, width_x
    )
    rock_out = jnp.transpose(rock_acc, (3, 0, 1, 2, 4)).reshape(parts, -1)
    records = jnp.stack(late_records).reshape(1, -1)
    packed = jnp.concatenate([jnp.broadcast_to(records, (parts, records.shape[1])), rock_out], axis=1)
    got = lax.all_to_all(packed, "gx", 0, 0, tiled=True)
    late_count = len(late_records)
    recorded = jnp.sum(got[:, : records.shape[1]], axis=0).reshape(late_count, shots, -1)
    rock_back = got[:, records.shape[1] :].reshape(
        parts, 2 * slots * shots, local_y, rock_z, width_x
    )
    rock_back = jnp.transpose(rock_back, (1, 4, 3, 0, 2)).reshape(
        2, slots, shots, width_x, rock_z, parts * local_y
    )
    late_misfits = recorded - observed[first_late:]
    scales = lax.rsqrt(jnp.mean(late_misfits * late_misfits, axis=2) + 1e-06)
    weights = jnp.concatenate([jnp.ones((1, shots), jnp.float32), scales])
    grad_kappa = jnp.sum(kappa_acc * weights[:, :, None, None, None], axis=(0, 1))
    rock_weights = weights[:slots, :, None, None, None]
    grad_lambda = jnp.sum(rock_back[0] * rock_weights, axis=(0, 1))
    grad_mu = jnp.sum(rock_back[1] * rock_weights, axis=(0, 1))
    misfits = jnp.concatenate([jnp.stack(early_misfits), late_misfits]) if early_misfits else late_misfits
    return (grad_lambda, grad_mu, grad_kappa, misfits)


def solution(mesh):
    placed = (
        P(None, None, "groups", "gx", None, None),
        P(None, None, "groups", "gx", None, None),
        P("gx", None, None),
        P("gx", None, None),
        P("gx", None, None),
        P("gx", None, None),
        P("gx", None, None),
        P("gx", None),
        P("groups"),
        P(None, "groups"),
        P(),
        P(None, "groups", None),
    )
    return jax.shard_map(
        on_device,
        mesh=mesh,
        in_specs=placed,
        out_specs=(
            P("gx", "groups", None),
            P("gx", "groups", None),
            P("gx", "groups", None),
            P(None, "groups", None),
        ),
        check_vma=False,
    )
```

```python
import jax
import jax.numpy as jnp
from jax import lax
from jax.sharding import PartitionSpec as P

COEFF = (1225.0 / 1024.0, -245.0 / 3072.0, 49.0 / 5120.0, -5.0 / 7168.0)
TIME_STEP = 0.2
HALO = 4
ROW_AXIS = 2
DEPTH_AXIS = 3
DEFERRED = 3


def halo_rows(fields):
    devices = lax.axis_size("gx")
    up = [(i, i + 1) for i in range(devices - 1)]
    down = [(i + 1, i) for i in range(devices - 1)]
    packed = jnp.concatenate(fields, axis=DEPTH_AXIS)
    length = packed.shape[ROW_AXIS]
    before = lax.ppermute(
        lax.slice_in_dim(packed, length - HALO, length, axis=ROW_AXIS), "gx", up
    )
    after = lax.ppermute(lax.slice_in_dim(packed, 0, HALO, axis=ROW_AXIS), "gx", down)
    padded = jnp.concatenate([before, packed, after], axis=ROW_AXIS)
    out, start = [], 0
    for f in fields:
        depth = f.shape[DEPTH_AXIS]
        out.append(lax.slice_in_dim(padded, start, start + depth, axis=DEPTH_AXIS))
        start += depth
    return out


def fill_waves(field, waves):
    extra = waves - field.shape[0]
    if extra == 0:
        return field
    return jnp.concatenate([field, jnp.zeros((extra,) + field.shape[1:], field.dtype)])


def gather_sum(partial, parts):
    copies = jnp.broadcast_to(partial[None], (parts,) + partial.shape)
    return jnp.sum(lax.all_to_all(copies, "gx", 0, 0, tiled=True), axis=0)


def stencil(padded, axis, forward):
    length = padded.shape[axis] - 8
    summed = None
    for offset in range(1, 5):
        if forward:
            front_at, back_at = (4 + offset, 5 - offset)
        else:
            front_at, back_at = (3 + offset, 4 - offset)
        front = lax.slice_in_dim(padded, front_at, front_at + length, axis=axis)
        back = lax.slice_in_dim(padded, back_at, back_at + length, axis=axis)
        addend = COEFF[offset - 1] * (front - back)
        summed = addend if summed is None else summed + addend
    return summed


def padded_zero(field, axis):
    widths = [(0, 0)] * field.ndim
    widths[axis] = (4, 4)
    return jnp.pad(field, widths)


def derive(field, axis, forward):
    return stencil(padded_zero(field, axis), axis, forward)


def on_device(
    solid_state,
    water_state,
    lame_lambda,
    shear_mu,
    solid_buoy,
    water_kappa,
    water_buoy,
    seafloor,
    source_cell,
    wavelet,
    receiver_column,
    observed,
):
    parts = lax.axis_size("gx")
    place = lax.axis_index("gx")
    n_fields, waves, shots, width_x, rock_z, total_y = solid_state.shape
    local_y = water_state.shape[3]
    depth_rows = water_state.shape[4]
    total_x = water_state.shape[5]
    anchor_y = place * local_y

    rock_in = jnp.concatenate(
        [
            solid_state.reshape(n_fields * waves * shots, width_x, rock_z, total_y),
            jnp.stack([lame_lambda, shear_mu, solid_buoy]),
        ],
        axis=0,
    )
    rock = jnp.transpose(
        lax.all_to_all(rock_in, "gx", split_axis=3, concat_axis=1, tiled=True), (0, 3, 2, 1)
    )
    rock_state = rock[: n_fields * waves * shots].reshape(
        n_fields, waves, shots, local_y, rock_z, total_x
    )
    lam, mu, buoy = rock[-3], rock[-2], rock[-1]

    vel_x, vel_y, vel_z = (rock_state[0], rock_state[1], rock_state[2])
    sig_xx, sig_yy, sig_zz = (rock_state[3], rock_state[4], rock_state[5])
    sig_xy, sig_xz, sig_yz = (rock_state[6], rock_state[7], rock_state[8])
    pressure, flow_x, flow_y, flow_z = (
        water_state[0],
        water_state[1],
        water_state[2],
        water_state[3],
    )
    depth_idx = lax.broadcasted_iota(jnp.int32, (1, depth_rows, 1), 1)
    floor_rows = seafloor[:, None, :]
    live = (depth_idx < floor_rows).astype(jnp.float32)
    bottom = (depth_idx == floor_rows - 1).astype(jnp.float32)
    above = (depth_idx < floor_rows - 1).astype(jnp.float32)
    rows_y = lax.broadcasted_iota(jnp.int32, (local_y, 1, 1), 0) + anchor_y
    cols_x = lax.broadcasted_iota(jnp.int32, (1, 1, total_x), 2)
    flat_cell = (depth_idx * total_y + rows_y) * total_x + cols_x
    source_hot = (flat_cell[None] == source_cell[:, None, None, None]).astype(jnp.float32)
    node_y = receiver_column // total_x
    node_x = receiver_column % total_x
    inside = (node_y >= anchor_y) & (node_y < anchor_y + local_y)
    local_col = (node_y - anchor_y) * total_x + node_x
    column_iota = lax.broadcasted_iota(jnp.int32, (1, local_y * total_x), 1)
    node_hot = ((column_iota == local_col[:, None]) & inside[:, None]).astype(jnp.float32)
    steps = wavelet.shape[0]
    first_late = steps - min(DEFERRED, steps)
    lam_acc = jnp.zeros((1, shots) + lam.shape, jnp.float32)
    mu_acc = jnp.zeros((1, shots) + lam.shape, jnp.float32)
    kappa_acc = jnp.zeros((1, shots) + water_kappa.shape, jnp.float32)
    early_misfits = []
    late_records = []
    pending = []
    for step in range(steps):
        if pending and pending[0][0] == step - 2:
            _, saved_floor = pending.pop(0)
            rock_zero = jnp.zeros((1,) + vel_x.shape[1:], jnp.float32)
            vel_x, vel_y, vel_z = [jnp.concatenate([f, rock_zero]) for f in (vel_x, vel_y, vel_z)]
            sig_xx, sig_yy, sig_xy, sig_xz, sig_yz = [
                jnp.concatenate([f, rock_zero]) for f in (sig_xx, sig_yy, sig_xy, sig_xz, sig_yz)
            ]
            sig_zz = jnp.concatenate([sig_zz, rock_zero.at[:, :, :, 0, :].set(-saved_floor)])
            lam_acc = jnp.concatenate([lam_acc, jnp.zeros((1,) + lam_acc.shape[1:], jnp.float32)])
            mu_acc = jnp.concatenate([mu_acc, jnp.zeros((1,) + mu_acc.shape[1:], jnp.float32)])
        rock_waves = vel_x.shape[0]
        water_waves = pressure.shape[0]
        floor_pressure = jnp.sum(pressure * bottom, axis=3)
        pending = [(at, floor_pressure[rock_waves + i : rock_waves + i + 1]) for i, (at, _) in enumerate(pending)]
        sxy_pad, syy_pad, syz_pad, p_pad = halo_rows(
            [fill_waves(f, water_waves) for f in (sig_xy, sig_yy, sig_yz)] + [pressure]
        )
        sxy_pad, syy_pad, syz_pad = [f[:rock_waves] for f in (sxy_pad, syy_pad, syz_pad)]
        vel_x = vel_x + TIME_STEP * buoy * (
            derive(sig_xx, 4, True) + stencil(sxy_pad, 2, False) + derive(sig_xz, 3, False)
        )
        vel_y = vel_y + TIME_STEP * buoy * (
            derive(sig_xy, 4, False) + stencil(syy_pad, 2, True) + derive(sig_yz, 3, False)
        )
        vel_z = vel_z + TIME_STEP * buoy * (
            derive(sig_xz, 4, False) + stencil(syz_pad, 2, False) + derive(sig_zz, 3, True)
        )
        floor_velocity = fill_waves(vel_z[:, :, :, 0, :], water_waves)
        flow_x = (flow_x - TIME_STEP * water_buoy * derive(pressure, 4, True)) * live
        flow_y = (flow_y - TIME_STEP * water_buoy * stencil(p_pad, 2, True)) * live
        flow_z = (
            flow_z - TIME_STEP * water_buoy * derive(pressure, 3, True)
        ) * above + floor_velocity[:, :, :, None, :] * bottom
        vx_pad, vy_pad, vz_pad, uy_pad = halo_rows(
            [fill_waves(f, water_waves) for f in (vel_x, vel_y, vel_z)] + [flow_y]
        )
        vx_pad, vy_pad, vz_pad = [f[:rock_waves] for f in (vx_pad, vy_pad, vz_pad)]
        strain_x = derive(vel_x, 4, False)
        strain_y = stencil(vy_pad, 2, False)
        strain_z = derive(vel_z, 3, False)
        dilation = strain_x + strain_y + strain_z
        shear_xy = stencil(vx_pad, 2, True) + derive(vel_y, 4, True)
        shear_xz = derive(vel_x, 3, True) + derive(vel_z, 4, True)
        shear_yz = derive(vel_y, 3, True) + stencil(vz_pad, 2, True)
        lam_part = lam * dilation
        sig_xx = sig_xx + TIME_STEP * (lam_part + 2.0 * mu * strain_x)
        sig_yy = sig_yy + TIME_STEP * (lam_part + 2.0 * mu * strain_y)
        sig_zz = sig_zz + TIME_STEP * (lam_part + 2.0 * mu * strain_z)
        sig_xy = sig_xy + TIME_STEP * mu * shear_xy
        sig_xz = sig_xz + TIME_STEP * mu * shear_xz
        sig_yz = sig_yz + TIME_STEP * mu * shear_yz
        sig_zz = sig_zz.at[:, :, :, 0, :].set(-floor_pressure[:rock_waves])
        lam_acc = lam_acc + dilation[:1] * dilation[1:]
        normal_part = (
            strain_x[:1] * strain_x[1:] + strain_y[:1] * strain_y[1:] + strain_z[:1] * strain_z[1:]
        )
        shear_part = (
            shear_xy[:1] * shear_xy[1:] + shear_xz[:1] * shear_xz[1:] + shear_yz[:1] * shear_yz[1:]
        )
        mu_acc = mu_acc + (2.0 * normal_part + shear_part)
        pressure = (
            pressure
            - TIME_STEP
            * water_kappa
            * (derive(flow_x, 4, False) + stencil(uy_pad, 2, False) + derive(flow_z, 3, False))
        ) * live
        pressure = pressure.at[0].add(wavelet[step][:, None, None, None] * source_hot)
        surface = jnp.sum(pressure[0] * bottom, axis=2)
        partial_record = jnp.einsum(
            "sc,rc->sr",
            surface.reshape(shots, local_y * total_x),
            node_hot,
            precision=lax.Precision.HIGHEST,
        )
        if step < first_late:
            misfit = gather_sum(partial_record, parts) - observed[step]
            scaled = misfit * lax.rsqrt(jnp.mean(misfit * misfit, axis=1, keepdims=True) + 1e-06)
            inject = jnp.dot(
                scaled, node_hot, precision=lax.Precision.HIGHEST, preferred_element_type=jnp.float32
            ).reshape(shots, local_y, total_x)
            pressure = pressure.at[1].add(inject[:, :, None, :] * bottom)
            kappa_acc = kappa_acc + pressure[:1] * pressure[1:]
            early_misfits.append(misfit)
            continue
        late_records.append(partial_record)
        local_misfit = partial_record - observed[step]
        inject = jnp.dot(
            local_misfit, node_hot, precision=lax.Precision.HIGHEST, preferred_element_type=jnp.float32
        ).reshape(shots, local_y, total_x)
        kick = inject[:, :, None, :] * bottom
        kappa_acc = jnp.concatenate(
            [kappa_acc + pressure[:1] * pressure[1:], (pressure[0] * kick)[None]], axis=0
        )
        if step + 1 < steps:
            water_zero = jnp.zeros((1,) + flow_x.shape[1:], jnp.float32)
            flow_x, flow_y, flow_z = [jnp.concatenate([f, water_zero]) for f in (flow_x, flow_y, flow_z)]
            pressure = jnp.concatenate([pressure, kick[None]])
            pending.append((step, None))

    slots = lam_acc.shape[0]
    rock_acc = jnp.concatenate([lam_acc, mu_acc]).reshape(
        2 * slots * shots, local_y, rock_z, parts, width_x
    )
    rock_out = jnp.transpose(rock_acc, (3, 0, 1, 2, 4)).reshape(parts, -1)
    records = jnp.stack(late_records).reshape(1, -1)
    packed = jnp.concatenate([jnp.broadcast_to(records, (parts, records.shape[1])), rock_out], axis=1)
    got = lax.all_to_all(packed, "gx", 0, 0, tiled=True)
    late_count = len(late_records)
    recorded = jnp.sum(got[:, : records.shape[1]], axis=0).reshape(late_count, shots, -1)
    rock_back = got[:, records.shape[1] :].reshape(
        parts, 2 * slots * shots, local_y, rock_z, width_x
    )
    rock_back = jnp.transpose(rock_back, (1, 4, 3, 0, 2)).reshape(
        2, slots, shots, width_x, rock_z, parts * local_y
    )
    late_misfits = recorded - observed[first_late:]
    scales = lax.rsqrt(jnp.mean(late_misfits * late_misfits, axis=2) + 1e-06)
    weights = jnp.concatenate([jnp.ones((1, shots), jnp.float32), scales])
    grad_kappa = jnp.sum(kappa_acc * weights[:, :, None, None, None], axis=(0, 1))
    rock_weights = weights[:slots, :, None, None, None]
    grad_lambda = jnp.sum(rock_back[0] * rock_weights, axis=(0, 1))
    grad_mu = jnp.sum(rock_back[1] * rock_weights, axis=(0, 1))
    misfits = jnp.concatenate([jnp.stack(early_misfits), late_misfits]) if early_misfits else late_misfits
    return (grad_lambda, grad_mu, grad_kappa, misfits)


def solution(mesh):
    placed = (
        P(None, None, "groups", "gx", None, None),
        P(None, None, "groups", "gx", None, None),
        P("gx", None, None),
        P("gx", None, None),
        P("gx", None, None),
        P("gx", None, None),
        P("gx", None, None),
        P("gx", None),
        P("groups"),
        P(None, "groups"),
        P(),
        P(None, "groups", None),
    )
    return jax.shard_map(
        on_device,
        mesh=mesh,
        in_specs=placed,
        out_specs=(
            P("gx", "groups", None),
            P("gx", "groups", None),
            P("gx", "groups", None),
            P(None, "groups", None),
        ),
        check_vma=False,
    )
```

```python
import jax
import jax.numpy as jnp
from jax import lax
from jax.sharding import PartitionSpec as P

COEFF = (1225.0 / 1024.0, -245.0 / 3072.0, 49.0 / 5120.0, -5.0 / 7168.0)
TIME_STEP = 0.2
HALO = 4
ROW_AXIS = 2
DEPTH_AXIS = 3
DEFERRED = 4


def halo_rows(fields):
    devices = lax.axis_size("gx")
    up = [(i, i + 1) for i in range(devices - 1)]
    down = [(i + 1, i) for i in range(devices - 1)]
    packed = jnp.concatenate(fields, axis=DEPTH_AXIS)
    length = packed.shape[ROW_AXIS]
    before = lax.ppermute(
        lax.slice_in_dim(packed, length - HALO, length, axis=ROW_AXIS), "gx", up
    )
    after = lax.ppermute(lax.slice_in_dim(packed, 0, HALO, axis=ROW_AXIS), "gx", down)
    padded = jnp.concatenate([before, packed, after], axis=ROW_AXIS)
    out, start = [], 0
    for f in fields:
        depth = f.shape[DEPTH_AXIS]
        out.append(lax.slice_in_dim(padded, start, start + depth, axis=DEPTH_AXIS))
        start += depth
    return out


def fill_waves(field, waves):
    extra = waves - field.shape[0]
    if extra == 0:
        return field
    return jnp.concatenate([field, jnp.zeros((extra,) + field.shape[1:], field.dtype)])


def gather_sum(partial, parts):
    copies = jnp.broadcast_to(partial[None], (parts,) + partial.shape)
    return jnp.sum(lax.all_to_all(copies, "gx", 0, 0, tiled=True), axis=0)


def stencil(padded, axis, forward):
    length = padded.shape[axis] - 8
    summed = None
    for offset in range(1, 5):
        if forward:
            front_at, back_at = (4 + offset, 5 - offset)
        else:
            front_at, back_at = (3 + offset, 4 - offset)
        front = lax.slice_in_dim(padded, front_at, front_at + length, axis=axis)
        back = lax.slice_in_dim(padded, back_at, back_at + length, axis=axis)
        addend = COEFF[offset - 1] * (front - back)
        summed = addend if summed is None else summed + addend
    return summed


def padded_zero(field, axis):
    widths = [(0, 0)] * field.ndim
    widths[axis] = (4, 4)
    return jnp.pad(field, widths)


def derive(field, axis, forward):
    return stencil(padded_zero(field, axis), axis, forward)


def on_device(
    solid_state,
    water_state,
    lame_lambda,
    shear_mu,
    solid_buoy,
    water_kappa,
    water_buoy,
    seafloor,
    source_cell,
    wavelet,
    receiver_column,
    observed,
):
    parts = lax.axis_size("gx")
    place = lax.axis_index("gx")
    n_fields, waves, shots, width_x, rock_z, total_y = solid_state.shape
    local_y = water_state.shape[3]
    depth_rows = water_state.shape[4]
    total_x = water_state.shape[5]
    anchor_y = place * local_y

    rock_in = jnp.concatenate(
        [
            solid_state.reshape(n_fields * waves * shots, width_x, rock_z, total_y),
            jnp.stack([lame_lambda, shear_mu, solid_buoy]),
        ],
        axis=0,
    )
    rock = jnp.transpose(
        lax.all_to_all(rock_in, "gx", split_axis=3, concat_axis=1, tiled=True), (0, 3, 2, 1)
    )
    rock_state = rock[: n_fields * waves * shots].reshape(
        n_fields, waves, shots, local_y, rock_z, total_x
    )
    lam, mu, buoy = rock[-3], rock[-2], rock[-1]

    vel_x, vel_y, vel_z = (rock_state[0], rock_state[1], rock_state[2])
    sig_xx, sig_yy, sig_zz = (rock_state[3], rock_state[4], rock_state[5])
    sig_xy, sig_xz, sig_yz = (rock_state[6], rock_state[7], rock_state[8])
    pressure, flow_x, flow_y, flow_z = (
        water_state[0],
        water_state[1],
        water_state[2],
        water_state[3],
    )
    depth_idx = lax.broadcasted_iota(jnp.int32, (1, depth_rows, 1), 1)
    floor_rows = seafloor[:, None, :]
    live = (depth_idx < floor_rows).astype(jnp.float32)
    bottom = (depth_idx == floor_rows - 1).astype(jnp.float32)
    above = (depth_idx < floor_rows - 1).astype(jnp.float32)
    rows_y = lax.broadcasted_iota(jnp.int32, (local_y, 1, 1), 0) + anchor_y
    cols_x = lax.broadcasted_iota(jnp.int32, (1, 1, total_x), 2)
    flat_cell = (depth_idx * total_y + rows_y) * total_x + cols_x
    source_hot = (flat_cell[None] == source_cell[:, None, None, None]).astype(jnp.float32)
    node_y = receiver_column // total_x
    node_x = receiver_column % total_x
    inside = (node_y >= anchor_y) & (node_y < anchor_y + local_y)
    local_col = (node_y - anchor_y) * total_x + node_x
    column_iota = lax.broadcasted_iota(jnp.int32, (1, local_y * total_x), 1)
    node_hot = ((column_iota == local_col[:, None]) & inside[:, None]).astype(jnp.float32)
    steps = wavelet.shape[0]
    first_late = steps - min(DEFERRED, steps)
    lam_acc = jnp.zeros((1, shots) + lam.shape, jnp.float32)
    mu_acc = jnp.zeros((1, shots) + lam.shape, jnp.float32)
    kappa_acc = jnp.zeros((1, shots) + water_kappa.shape, jnp.float32)
    early_misfits = []
    late_records = []
    pending = []
    for step in range(steps):
        if pending and pending[0][0] == step - 2:
            _, saved_floor = pending.pop(0)
            rock_zero = jnp.zeros((1,) + vel_x.shape[1:], jnp.float32)
            vel_x, vel_y, vel_z = [jnp.concatenate([f, rock_zero]) for f in (vel_x, vel_y, vel_z)]
            sig_xx, sig_yy, sig_xy, sig_xz, sig_yz = [
                jnp.concatenate([f, rock_zero]) for f in (sig_xx, sig_yy, sig_xy, sig_xz, sig_yz)
            ]
            sig_zz = jnp.concatenate([sig_zz, rock_zero.at[:, :, :, 0, :].set(-saved_floor)])
            lam_acc = jnp.concatenate([lam_acc, jnp.zeros((1,) + lam_acc.shape[1:], jnp.float32)])
            mu_acc = jnp.concatenate([mu_acc, jnp.zeros((1,) + mu_acc.shape[1:], jnp.float32)])
        rock_waves = vel_x.shape[0]
        water_waves = pressure.shape[0]
        floor_pressure = jnp.sum(pressure * bottom, axis=3)
        pending = [(at, floor_pressure[rock_waves + i : rock_waves + i + 1]) for i, (at, _) in enumerate(pending)]
        sxy_pad, syy_pad, syz_pad, p_pad = halo_rows(
            [fill_waves(f, water_waves) for f in (sig_xy, sig_yy, sig_yz)] + [pressure]
        )
        sxy_pad, syy_pad, syz_pad = [f[:rock_waves] for f in (sxy_pad, syy_pad, syz_pad)]
        vel_x = vel_x + TIME_STEP * buoy * (
            derive(sig_xx, 4, True) + stencil(sxy_pad, 2, False) + derive(sig_xz, 3, False)
        )
        vel_y = vel_y + TIME_STEP * buoy * (
            derive(sig_xy, 4, False) + stencil(syy_pad, 2, True) + derive(sig_yz, 3, False)
        )
        vel_z = vel_z + TIME_STEP * buoy * (
            derive(sig_xz, 4, False) + stencil(syz_pad, 2, False) + derive(sig_zz, 3, True)
        )
        floor_velocity = fill_waves(vel_z[:, :, :, 0, :], water_waves)
        flow_x = (flow_x - TIME_STEP * water_buoy * derive(pressure, 4, True)) * live
        flow_y = (flow_y - TIME_STEP * water_buoy * stencil(p_pad, 2, True)) * live
        flow_z = (
            flow_z - TIME_STEP * water_buoy * derive(pressure, 3, True)
        ) * above + floor_velocity[:, :, :, None, :] * bottom
        vx_pad, vy_pad, vz_pad, uy_pad = halo_rows(
            [fill_waves(f, water_waves) for f in (vel_x, vel_y, vel_z)] + [flow_y]
        )
        vx_pad, vy_pad, vz_pad = [f[:rock_waves] for f in (vx_pad, vy_pad, vz_pad)]
        strain_x = derive(vel_x, 4, False)
        strain_y = stencil(vy_pad, 2, False)
        strain_z = derive(vel_z, 3, False)
        dilation = strain_x + strain_y + strain_z
        shear_xy = stencil(vx_pad, 2, True) + derive(vel_y, 4, True)
        shear_xz = derive(vel_x, 3, True) + derive(vel_z, 4, True)
        shear_yz = derive(vel_y, 3, True) + stencil(vz_pad, 2, True)
        lam_part = lam * dilation
        sig_xx = sig_xx + TIME_STEP * (lam_part + 2.0 * mu * strain_x)
        sig_yy = sig_yy + TIME_STEP * (lam_part + 2.0 * mu * strain_y)
        sig_zz = sig_zz + TIME_STEP * (lam_part + 2.0 * mu * strain_z)
        sig_xy = sig_xy + TIME_STEP * mu * shear_xy
        sig_xz = sig_xz + TIME_STEP * mu * shear_xz
        sig_yz = sig_yz + TIME_STEP * mu * shear_yz
        sig_zz = sig_zz.at[:, :, :, 0, :].set(-floor_pressure[:rock_waves])
        lam_acc = lam_acc + dilation[:1] * dilation[1:]
        normal_part = (
            strain_x[:1] * strain_x[1:] + strain_y[:1] * strain_y[1:] + strain_z[:1] * strain_z[1:]
        )
        shear_part = (
            shear_xy[:1] * shear_xy[1:] + shear_xz[:1] * shear_xz[1:] + shear_yz[:1] * shear_yz[1:]
        )
        mu_acc = mu_acc + (2.0 * normal_part + shear_part)
        pressure = (
            pressure
            - TIME_STEP
            * water_kappa
            * (derive(flow_x, 4, False) + stencil(uy_pad, 2, False) + derive(flow_z, 3, False))
        ) * live
        pressure = pressure.at[0].add(wavelet[step][:, None, None, None] * source_hot)
        surface = jnp.sum(pressure[0] * bottom, axis=2)
        partial_record = jnp.einsum(
            "sc,rc->sr",
            surface.reshape(shots, local_y * total_x),
            node_hot,
            precision=lax.Precision.HIGHEST,
        )
        if step < first_late:
            misfit = gather_sum(partial_record, parts) - observed[step]
            scaled = misfit * lax.rsqrt(jnp.mean(misfit * misfit, axis=1, keepdims=True) + 1e-06)
            inject = jnp.dot(
                scaled, node_hot, precision=lax.Precision.HIGHEST, preferred_element_type=jnp.float32
            ).reshape(shots, local_y, total_x)
            pressure = pressure.at[1].add(inject[:, :, None, :] * bottom)
            kappa_acc = kappa_acc + pressure[:1] * pressure[1:]
            early_misfits.append(misfit)
            continue
        late_records.append(partial_record)
        local_misfit = partial_record - observed[step]
        inject = jnp.dot(
            local_misfit, node_hot, precision=lax.Precision.HIGHEST, preferred_element_type=jnp.float32
        ).reshape(shots, local_y, total_x)
        kick = inject[:, :, None, :] * bottom
        kappa_acc = jnp.concatenate(
            [kappa_acc + pressure[:1] * pressure[1:], (pressure[0] * kick)[None]], axis=0
        )
        if step + 1 < steps:
            water_zero = jnp.zeros((1,) + flow_x.shape[1:], jnp.float32)
            flow_x, flow_y, flow_z = [jnp.concatenate([f, water_zero]) for f in (flow_x, flow_y, flow_z)]
            pressure = jnp.concatenate([pressure, kick[None]])
            pending.append((step, None))

    slots = lam_acc.shape[0]
    rock_acc = jnp.concatenate([lam_acc, mu_acc]).reshape(
        2 * slots * shots, local_y, rock_z, parts, width_x
    )
    rock_out = jnp.transpose(rock_acc, (3, 0, 1, 2, 4)).reshape(parts, -1)
    records = jnp.stack(late_records).reshape(1, -1)
    packed = jnp.concatenate([jnp.broadcast_to(records, (parts, records.shape[1])), rock_out], axis=1)
    got = lax.all_to_all(packed, "gx", 0, 0, tiled=True)
    late_count = len(late_records)
    recorded = jnp.sum(got[:, : records.shape[1]], axis=0).reshape(late_count, shots, -1)
    rock_back = got[:, records.shape[1] :].reshape(
        parts, 2 * slots * shots, local_y, rock_z, width_x
    )
    rock_back = jnp.transpose(rock_back, (1, 4, 3, 0, 2)).reshape(
        2, slots, shots, width_x, rock_z, parts * local_y
    )
    late_misfits = recorded - observed[first_late:]
    scales = lax.rsqrt(jnp.mean(late_misfits * late_misfits, axis=2) + 1e-06)
    weights = jnp.concatenate([jnp.ones((1, shots), jnp.float32), scales])
    grad_kappa = jnp.sum(kappa_acc * weights[:, :, None, None, None], axis=(0, 1))
    rock_weights = weights[:slots, :, None, None, None]
    grad_lambda = jnp.sum(rock_back[0] * rock_weights, axis=(0, 1))
    grad_mu = jnp.sum(rock_back[1] * rock_weights, axis=(0, 1))
    misfits = jnp.concatenate([jnp.stack(early_misfits), late_misfits]) if early_misfits else late_misfits
    return (grad_lambda, grad_mu, grad_kappa, misfits)


def solution(mesh):
    placed = (
        P(None, None, "groups", "gx", None, None),
        P(None, None, "groups", "gx", None, None),
        P("gx", None, None),
        P("gx", None, None),
        P("gx", None, None),
        P("gx", None, None),
        P("gx", None, None),
        P("gx", None),
        P("groups"),
        P(None, "groups"),
        P(),
        P(None, "groups", None),
    )
    return jax.shard_map(
        on_device,
        mesh=mesh,
        in_specs=placed,
        out_specs=(
            P("gx", "groups", None),
            P("gx", "groups", None),
            P("gx", "groups", None),
            P(None, "groups", None),
        ),
        check_vma=False,
    )
```

```python
import jax
import jax.numpy as jnp
from jax import lax
from jax.sharding import PartitionSpec as P

COEFF = (1225.0 / 1024.0, -245.0 / 3072.0, 49.0 / 5120.0, -5.0 / 7168.0)
TIME_STEP = 0.2
HALO = 4
ROW_AXIS = 2
DEPTH_AXIS = 3
DEFERRED = 3


def halo_rows(fields):
    devices = lax.axis_size("gx")
    odd = lax.axis_index("gx") % 2 == 1
    within = [(i, i ^ 1) for i in range(devices) if i ^ 1 < devices]
    across = [(i, i + 1) for i in range(1, devices - 1, 2)] + [(i + 1, i) for i in range(1, devices - 1, 2)]
    packed = jnp.concatenate(fields, axis=DEPTH_AXIS)
    length = packed.shape[ROW_AXIS]
    last = lax.slice_in_dim(packed, length - HALO, length, axis=ROW_AXIS)
    first = lax.slice_in_dim(packed, 0, HALO, axis=ROW_AXIS)
    got_within = lax.ppermute(jnp.where(odd, first, last), "gx", within)
    got_across = lax.ppermute(jnp.where(odd, last, first), "gx", across)
    before = jnp.where(odd, got_within, got_across)
    after = jnp.where(odd, got_across, got_within)
    padded = jnp.concatenate([before, packed, after], axis=ROW_AXIS)
    out, start = [], 0
    for f in fields:
        depth = f.shape[DEPTH_AXIS]
        out.append(lax.slice_in_dim(padded, start, start + depth, axis=DEPTH_AXIS))
        start += depth
    return out


def fill_waves(field, waves):
    extra = waves - field.shape[0]
    if extra == 0:
        return field
    return jnp.concatenate([field, jnp.zeros((extra,) + field.shape[1:], field.dtype)])


def gather_sum(partial, parts):
    copies = jnp.broadcast_to(partial[None], (parts,) + partial.shape)
    return jnp.sum(lax.all_to_all(copies, "gx", 0, 0, tiled=True), axis=0)


def stencil(padded, axis, forward):
    length = padded.shape[axis] - 8
    summed = None
    for offset in range(1, 5):
        if forward:
            front_at, back_at = (4 + offset, 5 - offset)
        else:
            front_at, back_at = (3 + offset, 4 - offset)
        front = lax.slice_in_dim(padded, front_at, front_at + length, axis=axis)
        back = lax.slice_in_dim(padded, back_at, back_at + length, axis=axis)
        addend = COEFF[offset - 1] * (front - back)
        summed = addend if summed is None else summed + addend
    return summed


def padded_zero(field, axis):
    widths = [(0, 0)] * field.ndim
    widths[axis] = (4, 4)
    return jnp.pad(field, widths)


def derive(field, axis, forward):
    return stencil(padded_zero(field, axis), axis, forward)


def on_device(
    solid_state,
    water_state,
    lame_lambda,
    shear_mu,
    solid_buoy,
    water_kappa,
    water_buoy,
    seafloor,
    source_cell,
    wavelet,
    receiver_column,
    observed,
):
    parts = lax.axis_size("gx")
    place = lax.axis_index("gx")
    n_fields, waves, shots, width_x, rock_z, total_y = solid_state.shape
    local_y = water_state.shape[3]
    depth_rows = water_state.shape[4]
    total_x = water_state.shape[5]
    anchor_y = place * local_y

    rock_in = jnp.concatenate(
        [
            solid_state.reshape(n_fields * waves * shots, width_x, rock_z, total_y),
            jnp.stack([lame_lambda, shear_mu, solid_buoy]),
        ],
        axis=0,
    )
    rock = jnp.transpose(
        lax.all_to_all(rock_in, "gx", split_axis=3, concat_axis=1, tiled=True), (0, 3, 2, 1)
    )
    rock_state = rock[: n_fields * waves * shots].reshape(
        n_fields, waves, shots, local_y, rock_z, total_x
    )
    lam, mu, buoy = rock[-3], rock[-2], rock[-1]

    vel_x, vel_y, vel_z = (rock_state[0], rock_state[1], rock_state[2])
    sig_xx, sig_yy, sig_zz = (rock_state[3], rock_state[4], rock_state[5])
    sig_xy, sig_xz, sig_yz = (rock_state[6], rock_state[7], rock_state[8])
    pressure, flow_x, flow_y, flow_z = (
        water_state[0],
        water_state[1],
        water_state[2],
        water_state[3],
    )
    depth_idx = lax.broadcasted_iota(jnp.int32, (1, depth_rows, 1), 1)
    floor_rows = seafloor[:, None, :]
    live = (depth_idx < floor_rows).astype(jnp.float32)
    bottom = (depth_idx == floor_rows - 1).astype(jnp.float32)
    above = (depth_idx < floor_rows - 1).astype(jnp.float32)
    rows_y = lax.broadcasted_iota(jnp.int32, (local_y, 1, 1), 0) + anchor_y
    cols_x = lax.broadcasted_iota(jnp.int32, (1, 1, total_x), 2)
    flat_cell = (depth_idx * total_y + rows_y) * total_x + cols_x
    source_hot = (flat_cell[None] == source_cell[:, None, None, None]).astype(jnp.float32)
    node_y = receiver_column // total_x
    node_x = receiver_column % total_x
    inside = (node_y >= anchor_y) & (node_y < anchor_y + local_y)
    local_col = (node_y - anchor_y) * total_x + node_x
    column_iota = lax.broadcasted_iota(jnp.int32, (1, local_y * total_x), 1)
    node_hot = ((column_iota == local_col[:, None]) & inside[:, None]).astype(jnp.float32)
    steps = wavelet.shape[0]
    first_late = steps - min(DEFERRED, steps)
    lam_acc = jnp.zeros((1, shots) + lam.shape, jnp.float32)
    mu_acc = jnp.zeros((1, shots) + lam.shape, jnp.float32)
    kappa_acc = jnp.zeros((1, shots) + water_kappa.shape, jnp.float32)
    early_misfits = []
    late_records = []
    pending = []
    for step in range(steps):
        if pending and pending[0][0] == step - 2:
            _, saved_floor = pending.pop(0)
            rock_zero = jnp.zeros((1,) + vel_x.shape[1:], jnp.float32)
            vel_x, vel_y, vel_z = [jnp.concatenate([f, rock_zero]) for f in (vel_x, vel_y, vel_z)]
            sig_xx, sig_yy, sig_xy, sig_xz, sig_yz = [
                jnp.concatenate([f, rock_zero]) for f in (sig_xx, sig_yy, sig_xy, sig_xz, sig_yz)
            ]
            sig_zz = jnp.concatenate([sig_zz, rock_zero.at[:, :, :, 0, :].set(-saved_floor)])
            lam_acc = jnp.concatenate([lam_acc, jnp.zeros((1,) + lam_acc.shape[1:], jnp.float32)])
            mu_acc = jnp.concatenate([mu_acc, jnp.zeros((1,) + mu_acc.shape[1:], jnp.float32)])
        rock_waves = vel_x.shape[0]
        water_waves = pressure.shape[0]
        floor_pressure = jnp.sum(pressure * bottom, axis=3)
        pending = [(at, floor_pressure[rock_waves + i : rock_waves + i + 1]) for i, (at, _) in enumerate(pending)]
        sxy_pad, syy_pad, syz_pad, p_pad = halo_rows(
            [fill_waves(f, water_waves) for f in (sig_xy, sig_yy, sig_yz)] + [pressure]
        )
        sxy_pad, syy_pad, syz_pad = [f[:rock_waves] for f in (sxy_pad, syy_pad, syz_pad)]
        vel_x = vel_x + TIME_STEP * buoy * (
            derive(sig_xx, 4, True) + stencil(sxy_pad, 2, False) + derive(sig_xz, 3, False)
        )
        vel_y = vel_y + TIME_STEP * buoy * (
            derive(sig_xy, 4, False) + stencil(syy_pad, 2, True) + derive(sig_yz, 3, False)
        )
        vel_z = vel_z + TIME_STEP * buoy * (
            derive(sig_xz, 4, False) + stencil(syz_pad, 2, False) + derive(sig_zz, 3, True)
        )
        floor_velocity = fill_waves(vel_z[:, :, :, 0, :], water_waves)
        flow_x = (flow_x - TIME_STEP * water_buoy * derive(pressure, 4, True)) * live
        flow_y = (flow_y - TIME_STEP * water_buoy * stencil(p_pad, 2, True)) * live
        flow_z = (
            flow_z - TIME_STEP * water_buoy * derive(pressure, 3, True)
        ) * above + floor_velocity[:, :, :, None, :] * bottom
        vx_pad, vy_pad, vz_pad, uy_pad = halo_rows(
            [fill_waves(f, water_waves) for f in (vel_x, vel_y, vel_z)] + [flow_y]
        )
        vx_pad, vy_pad, vz_pad = [f[:rock_waves] for f in (vx_pad, vy_pad, vz_pad)]
        strain_x = derive(vel_x, 4, False)
        strain_y = stencil(vy_pad, 2, False)
        strain_z = derive(vel_z, 3, False)
        dilation = strain_x + strain_y + strain_z
        shear_xy = stencil(vx_pad, 2, True) + derive(vel_y, 4, True)
        shear_xz = derive(vel_x, 3, True) + derive(vel_z, 4, True)
        shear_yz = derive(vel_y, 3, True) + stencil(vz_pad, 2, True)
        lam_part = lam * dilation
        sig_xx = sig_xx + TIME_STEP * (lam_part + 2.0 * mu * strain_x)
        sig_yy = sig_yy + TIME_STEP * (lam_part + 2.0 * mu * strain_y)
        sig_zz = sig_zz + TIME_STEP * (lam_part + 2.0 * mu * strain_z)
        sig_xy = sig_xy + TIME_STEP * mu * shear_xy
        sig_xz = sig_xz + TIME_STEP * mu * shear_xz
        sig_yz = sig_yz + TIME_STEP * mu * shear_yz
        sig_zz = sig_zz.at[:, :, :, 0, :].set(-floor_pressure[:rock_waves])
        lam_acc = lam_acc + dilation[:1] * dilation[1:]
        normal_part = (
            strain_x[:1] * strain_x[1:] + strain_y[:1] * strain_y[1:] + strain_z[:1] * strain_z[1:]
        )
        shear_part = (
            shear_xy[:1] * shear_xy[1:] + shear_xz[:1] * shear_xz[1:] + shear_yz[:1] * shear_yz[1:]
        )
        mu_acc = mu_acc + (2.0 * normal_part + shear_part)
        pressure = (
            pressure
            - TIME_STEP
            * water_kappa
            * (derive(flow_x, 4, False) + stencil(uy_pad, 2, False) + derive(flow_z, 3, False))
        ) * live
        pressure = pressure.at[0].add(wavelet[step][:, None, None, None] * source_hot)
        surface = jnp.sum(pressure[0] * bottom, axis=2)
        partial_record = jnp.einsum(
            "sc,rc->sr",
            surface.reshape(shots, local_y * total_x),
            node_hot,
            precision=lax.Precision.HIGHEST,
        )
        if step < first_late:
            misfit = gather_sum(partial_record, parts) - observed[step]
            scaled = misfit * lax.rsqrt(jnp.mean(misfit * misfit, axis=1, keepdims=True) + 1e-06)
            inject = jnp.dot(
                scaled, node_hot, precision=lax.Precision.HIGHEST, preferred_element_type=jnp.float32
            ).reshape(shots, local_y, total_x)
            pressure = pressure.at[1].add(inject[:, :, None, :] * bottom)
            kappa_acc = kappa_acc + pressure[:1] * pressure[1:]
            early_misfits.append(misfit)
            continue
        late_records.append(partial_record)
        local_misfit = partial_record - observed[step]
        inject = jnp.dot(
            local_misfit, node_hot, precision=lax.Precision.HIGHEST, preferred_element_type=jnp.float32
        ).reshape(shots, local_y, total_x)
        kick = inject[:, :, None, :] * bottom
        kappa_acc = jnp.concatenate(
            [kappa_acc + pressure[:1] * pressure[1:], (pressure[0] * kick)[None]], axis=0
        )
        if step + 1 < steps:
            water_zero = jnp.zeros((1,) + flow_x.shape[1:], jnp.float32)
            flow_x, flow_y, flow_z = [jnp.concatenate([f, water_zero]) for f in (flow_x, flow_y, flow_z)]
            pressure = jnp.concatenate([pressure, kick[None]])
            pending.append((step, None))

    slots = lam_acc.shape[0]
    rock_acc = jnp.concatenate([lam_acc, mu_acc]).reshape(
        2 * slots * shots, local_y, rock_z, parts, width_x
    )
    rock_out = jnp.transpose(rock_acc, (3, 0, 1, 2, 4)).reshape(parts, -1)
    records = jnp.stack(late_records).reshape(1, -1)
    packed = jnp.concatenate([jnp.broadcast_to(records, (parts, records.shape[1])), rock_out], axis=1)
    got = lax.all_to_all(packed, "gx", 0, 0, tiled=True)
    late_count = len(late_records)
    recorded = jnp.sum(got[:, : records.shape[1]], axis=0).reshape(late_count, shots, -1)
    rock_back = got[:, records.shape[1] :].reshape(
        parts, 2 * slots * shots, local_y, rock_z, width_x
    )
    rock_back = jnp.transpose(rock_back, (1, 4, 3, 0, 2)).reshape(
        2, slots, shots, width_x, rock_z, parts * local_y
    )
    late_misfits = recorded - observed[first_late:]
    scales = lax.rsqrt(jnp.mean(late_misfits * late_misfits, axis=2) + 1e-06)
    weights = jnp.concatenate([jnp.ones((1, shots), jnp.float32), scales])
    grad_kappa = jnp.sum(kappa_acc * weights[:, :, None, None, None], axis=(0, 1))
    rock_weights = weights[:slots, :, None, None, None]
    grad_lambda = jnp.sum(rock_back[0] * rock_weights, axis=(0, 1))
    grad_mu = jnp.sum(rock_back[1] * rock_weights, axis=(0, 1))
    misfits = jnp.concatenate([jnp.stack(early_misfits), late_misfits]) if early_misfits else late_misfits
    return (grad_lambda, grad_mu, grad_kappa, misfits)


def solution(mesh):
    placed = (
        P(None, None, "groups", "gx", None, None),
        P(None, None, "groups", "gx", None, None),
        P("gx", None, None),
        P("gx", None, None),
        P("gx", None, None),
        P("gx", None, None),
        P("gx", None, None),
        P("gx", None),
        P("groups"),
        P(None, "groups"),
        P(),
        P(None, "groups", None),
    )
    return jax.shard_map(
        on_device,
        mesh=mesh,
        in_specs=placed,
        out_specs=(
            P("gx", "groups", None),
            P("gx", "groups", None),
            P("gx", "groups", None),
            P(None, "groups", None),
        ),
        check_vma=False,
    )
```

```python
import jax
import jax.numpy as jnp
from jax import lax
from jax.sharding import PartitionSpec as P

COEFF = (1225.0 / 1024.0, -245.0 / 3072.0, 49.0 / 5120.0, -5.0 / 7168.0)
TIME_STEP = 0.2
HALO = 4
ROW_AXIS = 2
DEPTH_AXIS = 3
DEFERRED = 3


def halo_rows(fields):
    devices = lax.axis_size("gx")
    odd = lax.axis_index("gx") % 2 == 1
    within = [(i, i ^ 1) for i in range(devices) if i ^ 1 < devices]
    across = [(i, i + 1) for i in range(1, devices - 1, 2)] + [(i + 1, i) for i in range(1, devices - 1, 2)]
    packed = jnp.concatenate(fields, axis=DEPTH_AXIS)
    length = packed.shape[ROW_AXIS]
    last = lax.slice_in_dim(packed, length - HALO, length, axis=ROW_AXIS)
    first = lax.slice_in_dim(packed, 0, HALO, axis=ROW_AXIS)
    got_within = lax.ppermute(jnp.where(odd, first, last), "gx", within)
    got_across = lax.ppermute(jnp.where(odd, last, first), "gx", across)
    before = jnp.where(odd, got_within, got_across)
    after = jnp.where(odd, got_across, got_within)
    padded = jnp.concatenate([before, packed, after], axis=ROW_AXIS)
    out, start = [], 0
    for f in fields:
        depth = f.shape[DEPTH_AXIS]
        out.append(lax.slice_in_dim(padded, start, start + depth, axis=DEPTH_AXIS))
        start += depth
    return out


def fill_waves(field, waves):
    extra = waves - field.shape[0]
    if extra == 0:
        return field
    return jnp.concatenate([field, jnp.zeros((extra,) + field.shape[1:], field.dtype)])


def gather_sum(partial, parts):
    copies = jnp.broadcast_to(partial[None], (parts,) + partial.shape)
    return jnp.sum(lax.all_to_all(copies, "gx", 0, 0, tiled=True), axis=0)


def stencil(padded, axis, forward):
    length = padded.shape[axis] - 8
    summed = None
    for offset in range(1, 5):
        if forward:
            front_at, back_at = (4 + offset, 5 - offset)
        else:
            front_at, back_at = (3 + offset, 4 - offset)
        front = lax.slice_in_dim(padded, front_at, front_at + length, axis=axis)
        back = lax.slice_in_dim(padded, back_at, back_at + length, axis=axis)
        addend = COEFF[offset - 1] * (front - back)
        summed = addend if summed is None else summed + addend
    return summed


def padded_zero(field, axis):
    widths = [(0, 0)] * field.ndim
    widths[axis] = (4, 4)
    return jnp.pad(field, widths)


def derive(field, axis, forward):
    return stencil(padded_zero(field, axis), axis, forward)


def on_device(
    solid_state,
    water_state,
    lame_lambda,
    shear_mu,
    solid_buoy,
    water_kappa,
    water_buoy,
    seafloor,
    source_cell,
    wavelet,
    receiver_column,
    observed,
):
    parts = lax.axis_size("gx")
    place = lax.axis_index("gx")
    n_fields, waves, shots, width_x, rock_z, total_y = solid_state.shape
    local_y = water_state.shape[3]
    depth_rows = water_state.shape[4]
    total_x = water_state.shape[5]
    anchor_y = place * local_y

    rock_in = jnp.concatenate(
        [
            solid_state.reshape(n_fields * waves * shots, width_x, rock_z, total_y),
            jnp.stack([lame_lambda, shear_mu, solid_buoy]),
        ],
        axis=0,
    )
    rock = jnp.transpose(
        lax.all_to_all(rock_in, "gx", split_axis=3, concat_axis=1, tiled=True), (0, 3, 2, 1)
    )
    rock_state = rock[: n_fields * waves * shots].reshape(
        n_fields, waves, shots, local_y, rock_z, total_x
    )
    lam, mu, buoy = rock[-3], rock[-2], rock[-1]

    vel_x, vel_y, vel_z = (rock_state[0], rock_state[1], rock_state[2])
    sig_xx, sig_yy, sig_zz = (rock_state[3], rock_state[4], rock_state[5])
    sig_xy, sig_xz, sig_yz = (rock_state[6], rock_state[7], rock_state[8])
    pressure, flow_x, flow_y, flow_z = (
        water_state[0],
        water_state[1],
        water_state[2],
        water_state[3],
    )
    depth_idx = lax.broadcasted_iota(jnp.int32, (1, depth_rows, 1), 1)
    floor_rows = seafloor[:, None, :]
    live = (depth_idx < floor_rows).astype(jnp.float32)
    bottom = (depth_idx == floor_rows - 1).astype(jnp.float32)
    above = (depth_idx < floor_rows - 1).astype(jnp.float32)
    rows_y = lax.broadcasted_iota(jnp.int32, (local_y, 1, 1), 0) + anchor_y
    cols_x = lax.broadcasted_iota(jnp.int32, (1, 1, total_x), 2)
    flat_cell = (depth_idx * total_y + rows_y) * total_x + cols_x
    source_hot = (flat_cell[None] == source_cell[:, None, None, None]).astype(jnp.float32)
    node_y = receiver_column // total_x
    node_x = receiver_column % total_x
    inside = (node_y >= anchor_y) & (node_y < anchor_y + local_y)
    local_col = (node_y - anchor_y) * total_x + node_x
    column_iota = lax.broadcasted_iota(jnp.int32, (1, local_y * total_x), 1)
    node_hot = ((column_iota == local_col[:, None]) & inside[:, None]).astype(jnp.float32)
    steps = wavelet.shape[0]
    first_late = steps - min(DEFERRED, steps)
    lam_acc = jnp.zeros((1, shots) + lam.shape, jnp.float32)
    mu_acc = jnp.zeros((1, shots) + lam.shape, jnp.float32)
    kappa_acc = jnp.zeros((1, shots) + water_kappa.shape, jnp.float32)
    early_misfits = []
    late_records = []
    pending = []
    for step in range(steps):
        if pending and pending[0][0] == step - 2:
            _, saved_floor = pending.pop(0)
            rock_zero = jnp.zeros((1,) + vel_x.shape[1:], jnp.float32)
            vel_x, vel_y, vel_z = [jnp.concatenate([f, rock_zero]) for f in (vel_x, vel_y, vel_z)]
            sig_xx, sig_yy, sig_xy, sig_xz, sig_yz = [
                jnp.concatenate([f, rock_zero]) for f in (sig_xx, sig_yy, sig_xy, sig_xz, sig_yz)
            ]
            sig_zz = jnp.concatenate([sig_zz, rock_zero.at[:, :, :, 0, :].set(-saved_floor)])
            lam_acc = jnp.concatenate([lam_acc, jnp.zeros((1,) + lam_acc.shape[1:], jnp.float32)])
            mu_acc = jnp.concatenate([mu_acc, jnp.zeros((1,) + mu_acc.shape[1:], jnp.float32)])
        rock_waves = vel_x.shape[0]
        water_waves = pressure.shape[0]
        floor_pressure = jnp.sum(pressure * bottom, axis=3)
        pending = [(at, floor_pressure[rock_waves + i : rock_waves + i + 1]) for i, (at, _) in enumerate(pending)]
        (dx_sxx, dz_sxz, dx_sxy, dz_syz, dx_sxz, dz_szz, flow_x, flow_z_part) = lax.optimization_barrier(
            (
                derive(sig_xx, 4, True),
                derive(sig_xz, 3, False),
                derive(sig_xy, 4, False),
                derive(sig_yz, 3, False),
                derive(sig_xz, 4, False),
                derive(sig_zz, 3, True),
                (flow_x - TIME_STEP * water_buoy * derive(pressure, 4, True)) * live,
                (flow_z - TIME_STEP * water_buoy * derive(pressure, 3, True)) * above,
            )
        )
        sxy_pad, syy_pad, syz_pad, p_pad = halo_rows(
            [fill_waves(f, water_waves) for f in (sig_xy, sig_yy, sig_yz)] + [pressure]
        )
        sxy_pad, syy_pad, syz_pad = [f[:rock_waves] for f in (sxy_pad, syy_pad, syz_pad)]
        vel_x = vel_x + TIME_STEP * buoy * (dx_sxx + stencil(sxy_pad, 2, False) + dz_sxz)
        vel_y = vel_y + TIME_STEP * buoy * (dx_sxy + stencil(syy_pad, 2, True) + dz_syz)
        vel_z = vel_z + TIME_STEP * buoy * (dx_sxz + stencil(syz_pad, 2, False) + dz_szz)
        floor_velocity = fill_waves(vel_z[:, :, :, 0, :], water_waves)
        flow_y = (flow_y - TIME_STEP * water_buoy * stencil(p_pad, 2, True)) * live
        flow_z = flow_z_part + floor_velocity[:, :, :, None, :] * bottom
        (strain_x, strain_z, dx_vy, dz_vy, shear_xz, dx_ux, dz_uz) = lax.optimization_barrier(
            (
                derive(vel_x, 4, False),
                derive(vel_z, 3, False),
                derive(vel_y, 4, True),
                derive(vel_y, 3, True),
                derive(vel_x, 3, True) + derive(vel_z, 4, True),
                derive(flow_x, 4, False),
                derive(flow_z, 3, False),
            )
        )
        vx_pad, vy_pad, vz_pad, uy_pad = halo_rows(
            [fill_waves(f, water_waves) for f in (vel_x, vel_y, vel_z)] + [flow_y]
        )
        vx_pad, vy_pad, vz_pad = [f[:rock_waves] for f in (vx_pad, vy_pad, vz_pad)]
        strain_y = stencil(vy_pad, 2, False)
        dilation = strain_x + strain_y + strain_z
        shear_xy = stencil(vx_pad, 2, True) + dx_vy
        shear_yz = dz_vy + stencil(vz_pad, 2, True)
        lam_part = lam * dilation
        sig_xx = sig_xx + TIME_STEP * (lam_part + 2.0 * mu * strain_x)
        sig_yy = sig_yy + TIME_STEP * (lam_part + 2.0 * mu * strain_y)
        sig_zz = sig_zz + TIME_STEP * (lam_part + 2.0 * mu * strain_z)
        sig_xy = sig_xy + TIME_STEP * mu * shear_xy
        sig_xz = sig_xz + TIME_STEP * mu * shear_xz
        sig_yz = sig_yz + TIME_STEP * mu * shear_yz
        sig_zz = sig_zz.at[:, :, :, 0, :].set(-floor_pressure[:rock_waves])
        lam_acc = lam_acc + dilation[:1] * dilation[1:]
        normal_part = (
            strain_x[:1] * strain_x[1:] + strain_y[:1] * strain_y[1:] + strain_z[:1] * strain_z[1:]
        )
        shear_part = (
            shear_xy[:1] * shear_xy[1:] + shear_xz[:1] * shear_xz[1:] + shear_yz[:1] * shear_yz[1:]
        )
        mu_acc = mu_acc + (2.0 * normal_part + shear_part)
        pressure = (
            pressure
            - TIME_STEP
            * water_kappa
            * (dx_ux + stencil(uy_pad, 2, False) + dz_uz)
        ) * live
        pressure = pressure.at[0].add(wavelet[step][:, None, None, None] * source_hot)
        surface = jnp.sum(pressure[0] * bottom, axis=2)
        partial_record = jnp.einsum(
            "sc,rc->sr",
            surface.reshape(shots, local_y * total_x),
            node_hot,
            precision=lax.Precision.HIGHEST,
        )
        if step < first_late:
            misfit = gather_sum(partial_record, parts) - observed[step]
            scaled = misfit * lax.rsqrt(jnp.mean(misfit * misfit, axis=1, keepdims=True) + 1e-06)
            inject = jnp.dot(
                scaled, node_hot, precision=lax.Precision.HIGHEST, preferred_element_type=jnp.float32
            ).reshape(shots, local_y, total_x)
            pressure = pressure.at[1].add(inject[:, :, None, :] * bottom)
            kappa_acc = kappa_acc + pressure[:1] * pressure[1:]
            early_misfits.append(misfit)
            continue
        late_records.append(partial_record)
        local_misfit = partial_record - observed[step]
        inject = jnp.dot(
            local_misfit, node_hot, precision=lax.Precision.HIGHEST, preferred_element_type=jnp.float32
        ).reshape(shots, local_y, total_x)
        kick = inject[:, :, None, :] * bottom
        kappa_acc = jnp.concatenate(
            [kappa_acc + pressure[:1] * pressure[1:], (pressure[0] * kick)[None]], axis=0
        )
        if step + 1 < steps:
            water_zero = jnp.zeros((1,) + flow_x.shape[1:], jnp.float32)
            flow_x, flow_y, flow_z = [jnp.concatenate([f, water_zero]) for f in (flow_x, flow_y, flow_z)]
            pressure = jnp.concatenate([pressure, kick[None]])
            pending.append((step, None))

    slots = lam_acc.shape[0]
    rock_acc = jnp.concatenate([lam_acc, mu_acc]).reshape(
        2 * slots * shots, local_y, rock_z, parts, width_x
    )
    rock_out = jnp.transpose(rock_acc, (3, 0, 1, 2, 4)).reshape(parts, -1)
    records = jnp.stack(late_records).reshape(1, -1)
    packed = jnp.concatenate([jnp.broadcast_to(records, (parts, records.shape[1])), rock_out], axis=1)
    got = lax.all_to_all(packed, "gx", 0, 0, tiled=True)
    late_count = len(late_records)
    recorded = jnp.sum(got[:, : records.shape[1]], axis=0).reshape(late_count, shots, -1)
    rock_back = got[:, records.shape[1] :].reshape(
        parts, 2 * slots * shots, local_y, rock_z, width_x
    )
    rock_back = jnp.transpose(rock_back, (1, 4, 3, 0, 2)).reshape(
        2, slots, shots, width_x, rock_z, parts * local_y
    )
    late_misfits = recorded - observed[first_late:]
    scales = lax.rsqrt(jnp.mean(late_misfits * late_misfits, axis=2) + 1e-06)
    weights = jnp.concatenate([jnp.ones((1, shots), jnp.float32), scales])
    grad_kappa = jnp.sum(kappa_acc * weights[:, :, None, None, None], axis=(0, 1))
    rock_weights = weights[:slots, :, None, None, None]
    grad_lambda = jnp.sum(rock_back[0] * rock_weights, axis=(0, 1))
    grad_mu = jnp.sum(rock_back[1] * rock_weights, axis=(0, 1))
    misfits = jnp.concatenate([jnp.stack(early_misfits), late_misfits]) if early_misfits else late_misfits
    return (grad_lambda, grad_mu, grad_kappa, misfits)


def solution(mesh):
    placed = (
        P(None, None, "groups", "gx", None, None),
        P(None, None, "groups", "gx", None, None),
        P("gx", None, None),
        P("gx", None, None),
        P("gx", None, None),
        P("gx", None, None),
        P("gx", None, None),
        P("gx", None),
        P("groups"),
        P(None, "groups"),
        P(),
        P(None, "groups", None),
    )
    return jax.shard_map(
        on_device,
        mesh=mesh,
        in_specs=placed,
        out_specs=(
            P("gx", "groups", None),
            P("gx", "groups", None),
            P("gx", "groups", None),
            P(None, "groups", None),
        ),
        check_vma=False,
    )
```

```python
import jax
import jax.numpy as jnp
from jax import lax
from jax.sharding import PartitionSpec as P

COEFF = (1225.0 / 1024.0, -245.0 / 3072.0, 49.0 / 5120.0, -5.0 / 7168.0)
TIME_STEP = 0.2
HALO = 4
ROW_AXIS = 2
DEPTH_AXIS = 3
DEFERRED = 3


def halo_rows(fields):
    devices = lax.axis_size("gx")
    odd = lax.axis_index("gx") % 2 == 1
    within = [(i, i ^ 1) for i in range(devices) if i ^ 1 < devices]
    across = [(i, i + 1) for i in range(1, devices - 1, 2)] + [(i + 1, i) for i in range(1, devices - 1, 2)]
    packed = jnp.concatenate(fields, axis=DEPTH_AXIS)
    length = packed.shape[ROW_AXIS]
    last = lax.slice_in_dim(packed, length - HALO, length, axis=ROW_AXIS)
    first = lax.slice_in_dim(packed, 0, HALO, axis=ROW_AXIS)
    got_within = lax.ppermute(jnp.where(odd, first, last), "gx", within)
    got_across = lax.ppermute(jnp.where(odd, last, first), "gx", across)
    before = jnp.where(odd, got_within, got_across)
    after = jnp.where(odd, got_across, got_within)
    padded = jnp.concatenate([before, packed, after], axis=ROW_AXIS)
    out, start = [], 0
    for f in fields:
        depth = f.shape[DEPTH_AXIS]
        out.append(lax.slice_in_dim(padded, start, start + depth, axis=DEPTH_AXIS))
        start += depth
    return out


def fill_waves(field, waves):
    extra = waves - field.shape[0]
    if extra == 0:
        return field
    return jnp.concatenate([field, jnp.zeros((extra,) + field.shape[1:], field.dtype)])


def gather_sum(partial, parts):
    copies = jnp.broadcast_to(partial[None], (parts,) + partial.shape)
    return jnp.sum(lax.all_to_all(copies, "gx", 0, 0, tiled=True), axis=0)


def stencil(padded, axis, forward):
    length = padded.shape[axis] - 8
    summed = None
    for offset in range(1, 5):
        if forward:
            front_at, back_at = (4 + offset, 5 - offset)
        else:
            front_at, back_at = (3 + offset, 4 - offset)
        front = lax.slice_in_dim(padded, front_at, front_at + length, axis=axis)
        back = lax.slice_in_dim(padded, back_at, back_at + length, axis=axis)
        addend = COEFF[offset - 1] * (front - back)
        summed = addend if summed is None else summed + addend
    return summed


def padded_zero(field, axis):
    widths = [(0, 0)] * field.ndim
    widths[axis] = (4, 4)
    return jnp.pad(field, widths)


def derive(field, axis, forward):
    return stencil(padded_zero(field, axis), axis, forward)


def on_device(
    solid_state,
    water_state,
    lame_lambda,
    shear_mu,
    solid_buoy,
    water_kappa,
    water_buoy,
    seafloor,
    source_cell,
    wavelet,
    receiver_column,
    observed,
):
    parts = lax.axis_size("gx")
    place = lax.axis_index("gx")
    n_fields, waves, shots, width_x, rock_z, total_y = solid_state.shape
    local_y = water_state.shape[3]
    depth_rows = water_state.shape[4]
    total_x = water_state.shape[5]
    anchor_y = place * local_y

    rock_in = jnp.concatenate(
        [
            solid_state.reshape(n_fields * waves * shots, width_x, rock_z, total_y),
            jnp.stack([lame_lambda, shear_mu, solid_buoy]),
        ],
        axis=0,
    )
    rock = jnp.transpose(
        lax.all_to_all(rock_in, "gx", split_axis=3, concat_axis=1, tiled=True), (0, 3, 2, 1)
    )
    rock_state = rock[: n_fields * waves * shots].reshape(
        n_fields, waves, shots, local_y, rock_z, total_x
    )
    lam, mu, buoy = rock[-3], rock[-2], rock[-1]

    vel_x, vel_y, vel_z = (rock_state[0], rock_state[1], rock_state[2])
    sig_xx, sig_yy, sig_zz = (rock_state[3], rock_state[4], rock_state[5])
    sig_xy, sig_xz, sig_yz = (rock_state[6], rock_state[7], rock_state[8])
    pressure, flow_x, flow_y, flow_z = (
        water_state[0],
        water_state[1],
        water_state[2],
        water_state[3],
    )
    depth_idx = lax.broadcasted_iota(jnp.int32, (1, depth_rows, 1), 1)
    floor_rows = seafloor[:, None, :]
    live = (depth_idx < floor_rows).astype(jnp.float32)
    bottom = (depth_idx == floor_rows - 1).astype(jnp.float32)
    above = (depth_idx < floor_rows - 1).astype(jnp.float32)
    rows_y = lax.broadcasted_iota(jnp.int32, (local_y, 1, 1), 0) + anchor_y
    cols_x = lax.broadcasted_iota(jnp.int32, (1, 1, total_x), 2)
    flat_cell = (depth_idx * total_y + rows_y) * total_x + cols_x
    source_hot = (flat_cell[None] == source_cell[:, None, None, None]).astype(jnp.float32)
    node_y = receiver_column // total_x
    node_x = receiver_column % total_x
    inside = (node_y >= anchor_y) & (node_y < anchor_y + local_y)
    local_col = (node_y - anchor_y) * total_x + node_x
    column_iota = lax.broadcasted_iota(jnp.int32, (1, local_y * total_x), 1)
    node_hot = ((column_iota == local_col[:, None]) & inside[:, None]).astype(jnp.float32)
    steps = wavelet.shape[0]
    first_late = steps - min(DEFERRED, steps)
    lam_acc = jnp.zeros((1, shots) + lam.shape, jnp.float32)
    mu_acc = jnp.zeros((1, shots) + lam.shape, jnp.float32)
    kappa_acc = jnp.zeros((1, shots) + water_kappa.shape, jnp.float32)
    early_misfits = []
    late_records = []
    pending = []
    for step in range(steps):
        if pending and pending[0][0] == step - 2:
            _, saved_floor = pending.pop(0)
            rock_zero = jnp.zeros((1,) + vel_x.shape[1:], jnp.float32)
            vel_x, vel_y, vel_z = [jnp.concatenate([f, rock_zero]) for f in (vel_x, vel_y, vel_z)]
            sig_xx, sig_yy, sig_xy, sig_xz, sig_yz = [
                jnp.concatenate([f, rock_zero]) for f in (sig_xx, sig_yy, sig_xy, sig_xz, sig_yz)
            ]
            sig_zz = jnp.concatenate([sig_zz, rock_zero.at[:, :, :, 0, :].set(-saved_floor)])
            lam_acc = jnp.concatenate([lam_acc, jnp.zeros((1,) + lam_acc.shape[1:], jnp.float32)])
            mu_acc = jnp.concatenate([mu_acc, jnp.zeros((1,) + mu_acc.shape[1:], jnp.float32)])
        rock_waves = vel_x.shape[0]
        water_waves = pressure.shape[0]
        floor_pressure = jnp.sum(pressure * bottom, axis=3)
        pending = [(at, floor_pressure[rock_waves + i : rock_waves + i + 1]) for i, (at, _) in enumerate(pending)]
        (flow_x, flow_z_part) = lax.optimization_barrier(
            (
                (flow_x - TIME_STEP * water_buoy * derive(pressure, 4, True)) * live,
                (flow_z - TIME_STEP * water_buoy * derive(pressure, 3, True)) * above,
            )
        )
        (dx_sxx, dz_sxz, dx_sxy, dz_syz, dx_sxz, dz_szz) = lax.optimization_barrier(
            (
                derive(sig_xx, 4, True),
                derive(sig_xz, 3, False),
                derive(sig_xy, 4, False),
                derive(sig_yz, 3, False),
                derive(sig_xz, 4, False),
                derive(sig_zz, 3, True),
            )
        )
        sxy_pad, syy_pad, syz_pad, p_pad = halo_rows(
            [fill_waves(f, water_waves) for f in (sig_xy, sig_yy, sig_yz)] + [pressure]
        )
        sxy_pad, syy_pad, syz_pad = [f[:rock_waves] for f in (sxy_pad, syy_pad, syz_pad)]
        vel_x = vel_x + TIME_STEP * buoy * (dx_sxx + stencil(sxy_pad, 2, False) + dz_sxz)
        vel_y = vel_y + TIME_STEP * buoy * (dx_sxy + stencil(syy_pad, 2, True) + dz_syz)
        vel_z = vel_z + TIME_STEP * buoy * (dx_sxz + stencil(syz_pad, 2, False) + dz_szz)
        floor_velocity = fill_waves(vel_z[:, :, :, 0, :], water_waves)
        flow_y = (flow_y - TIME_STEP * water_buoy * stencil(p_pad, 2, True)) * live
        flow_z = flow_z_part + floor_velocity[:, :, :, None, :] * bottom
        (dx_ux, dz_uz) = lax.optimization_barrier(
            (derive(flow_x, 4, False), derive(flow_z, 3, False))
        )
        (strain_x, strain_z, dx_vy, dz_vy, shear_xz) = lax.optimization_barrier(
            (
                derive(vel_x, 4, False),
                derive(vel_z, 3, False),
                derive(vel_y, 4, True),
                derive(vel_y, 3, True),
                derive(vel_x, 3, True) + derive(vel_z, 4, True),
            )
        )
        vx_pad, vy_pad, vz_pad, uy_pad = halo_rows(
            [fill_waves(f, water_waves) for f in (vel_x, vel_y, vel_z)] + [flow_y]
        )
        vx_pad, vy_pad, vz_pad = [f[:rock_waves] for f in (vx_pad, vy_pad, vz_pad)]
        strain_y = stencil(vy_pad, 2, False)
        dilation = strain_x + strain_y + strain_z
        shear_xy = stencil(vx_pad, 2, True) + dx_vy
        shear_yz = dz_vy + stencil(vz_pad, 2, True)
        lam_part = lam * dilation
        sig_xx = sig_xx + TIME_STEP * (lam_part + 2.0 * mu * strain_x)
        sig_yy = sig_yy + TIME_STEP * (lam_part + 2.0 * mu * strain_y)
        sig_zz = sig_zz + TIME_STEP * (lam_part + 2.0 * mu * strain_z)
        sig_xy = sig_xy + TIME_STEP * mu * shear_xy
        sig_xz = sig_xz + TIME_STEP * mu * shear_xz
        sig_yz = sig_yz + TIME_STEP * mu * shear_yz
        sig_zz = sig_zz.at[:, :, :, 0, :].set(-floor_pressure[:rock_waves])
        lam_acc = lam_acc + dilation[:1] * dilation[1:]
        normal_part = (
            strain_x[:1] * strain_x[1:] + strain_y[:1] * strain_y[1:] + strain_z[:1] * strain_z[1:]
        )
        shear_part = (
            shear_xy[:1] * shear_xy[1:] + shear_xz[:1] * shear_xz[1:] + shear_yz[:1] * shear_yz[1:]
        )
        mu_acc = mu_acc + (2.0 * normal_part + shear_part)
        pressure = (
            pressure
            - TIME_STEP
            * water_kappa
            * (dx_ux + stencil(uy_pad, 2, False) + dz_uz)
        ) * live
        pressure = pressure.at[0].add(wavelet[step][:, None, None, None] * source_hot)
        surface = jnp.sum(pressure[0] * bottom, axis=2)
        partial_record = jnp.einsum(
            "sc,rc->sr",
            surface.reshape(shots, local_y * total_x),
            node_hot,
            precision=lax.Precision.HIGHEST,
        )
        if step < first_late:
            misfit = gather_sum(partial_record, parts) - observed[step]
            scaled = misfit * lax.rsqrt(jnp.mean(misfit * misfit, axis=1, keepdims=True) + 1e-06)
            inject = jnp.dot(
                scaled, node_hot, precision=lax.Precision.HIGHEST, preferred_element_type=jnp.float32
            ).reshape(shots, local_y, total_x)
            pressure = pressure.at[1].add(inject[:, :, None, :] * bottom)
            kappa_acc = kappa_acc + pressure[:1] * pressure[1:]
            early_misfits.append(misfit)
            continue
        late_records.append(partial_record)
        local_misfit = partial_record - observed[step]
        inject = jnp.dot(
            local_misfit, node_hot, precision=lax.Precision.HIGHEST, preferred_element_type=jnp.float32
        ).reshape(shots, local_y, total_x)
        kick = inject[:, :, None, :] * bottom
        kappa_acc = jnp.concatenate(
            [kappa_acc + pressure[:1] * pressure[1:], (pressure[0] * kick)[None]], axis=0
        )
        if step + 1 < steps:
            water_zero = jnp.zeros((1,) + flow_x.shape[1:], jnp.float32)
            flow_x, flow_y, flow_z = [jnp.concatenate([f, water_zero]) for f in (flow_x, flow_y, flow_z)]
            pressure = jnp.concatenate([pressure, kick[None]])
            pending.append((step, None))

    slots = lam_acc.shape[0]
    rock_acc = jnp.concatenate([lam_acc, mu_acc]).reshape(
        2 * slots * shots, local_y, rock_z, parts, width_x
    )
    rock_out = jnp.transpose(rock_acc, (3, 0, 1, 2, 4)).reshape(parts, -1)
    records = jnp.stack(late_records).reshape(1, -1)
    packed = jnp.concatenate([jnp.broadcast_to(records, (parts, records.shape[1])), rock_out], axis=1)
    got = lax.all_to_all(packed, "gx", 0, 0, tiled=True)
    late_count = len(late_records)
    recorded = jnp.sum(got[:, : records.shape[1]], axis=0).reshape(late_count, shots, -1)
    rock_back = got[:, records.shape[1] :].reshape(
        parts, 2 * slots * shots, local_y, rock_z, width_x
    )
    rock_back = jnp.transpose(rock_back, (1, 4, 3, 0, 2)).reshape(
        2, slots, shots, width_x, rock_z, parts * local_y
    )
    late_misfits = recorded - observed[first_late:]
    scales = lax.rsqrt(jnp.mean(late_misfits * late_misfits, axis=2) + 1e-06)
    weights = jnp.concatenate([jnp.ones((1, shots), jnp.float32), scales])
    grad_kappa = jnp.sum(kappa_acc * weights[:, :, None, None, None], axis=(0, 1))
    rock_weights = weights[:slots, :, None, None, None]
    grad_lambda = jnp.sum(rock_back[0] * rock_weights, axis=(0, 1))
    grad_mu = jnp.sum(rock_back[1] * rock_weights, axis=(0, 1))
    misfits = jnp.concatenate([jnp.stack(early_misfits), late_misfits]) if early_misfits else late_misfits
    return (grad_lambda, grad_mu, grad_kappa, misfits)


def solution(mesh):
    placed = (
        P(None, None, "groups", "gx", None, None),
        P(None, None, "groups", "gx", None, None),
        P("gx", None, None),
        P("gx", None, None),
        P("gx", None, None),
        P("gx", None, None),
        P("gx", None, None),
        P("gx", None),
        P("groups"),
        P(None, "groups"),
        P(),
        P(None, "groups", None),
    )
    return jax.shard_map(
        on_device,
        mesh=mesh,
        in_specs=placed,
        out_specs=(
            P("gx", "groups", None),
            P("gx", "groups", None),
            P("gx", "groups", None),
            P(None, "groups", None),
        ),
        check_vma=False,
    )
```

```python
import jax
import jax.numpy as jnp
from jax import lax
from jax.sharding import PartitionSpec as P

COEFF = (1225.0 / 1024.0, -245.0 / 3072.0, 49.0 / 5120.0, -5.0 / 7168.0)
TIME_STEP = 0.2
HALO = 4
ROW_AXIS = 2
DEPTH_AXIS = 3
DEFERRED = 2


def halo_rows(fields):
    devices = lax.axis_size("gx")
    odd = lax.axis_index("gx") % 2 == 1
    within = [(i, i ^ 1) for i in range(devices) if i ^ 1 < devices]
    across = [(i, i + 1) for i in range(1, devices - 1, 2)] + [(i + 1, i) for i in range(1, devices - 1, 2)]
    packed = jnp.concatenate(fields, axis=DEPTH_AXIS)
    length = packed.shape[ROW_AXIS]
    last = lax.slice_in_dim(packed, length - HALO, length, axis=ROW_AXIS)
    first = lax.slice_in_dim(packed, 0, HALO, axis=ROW_AXIS)
    got_within = lax.ppermute(jnp.where(odd, first, last), "gx", within)
    got_across = lax.ppermute(jnp.where(odd, last, first), "gx", across)
    before = jnp.where(odd, got_within, got_across)
    after = jnp.where(odd, got_across, got_within)
    padded = jnp.concatenate([before, packed, after], axis=ROW_AXIS)
    out, start = [], 0
    for f in fields:
        depth = f.shape[DEPTH_AXIS]
        out.append(lax.slice_in_dim(padded, start, start + depth, axis=DEPTH_AXIS))
        start += depth
    return out


def fill_waves(field, waves):
    extra = waves - field.shape[0]
    if extra == 0:
        return field
    return jnp.concatenate([field, jnp.zeros((extra,) + field.shape[1:], field.dtype)])


def gather_sum(partial, parts):
    copies = jnp.broadcast_to(partial[None], (parts,) + partial.shape)
    return jnp.sum(lax.all_to_all(copies, "gx", 0, 0, tiled=True), axis=0)


def stencil(padded, axis, forward):
    length = padded.shape[axis] - 8
    summed = None
    for offset in range(1, 5):
        if forward:
            front_at, back_at = (4 + offset, 5 - offset)
        else:
            front_at, back_at = (3 + offset, 4 - offset)
        front = lax.slice_in_dim(padded, front_at, front_at + length, axis=axis)
        back = lax.slice_in_dim(padded, back_at, back_at + length, axis=axis)
        addend = COEFF[offset - 1] * (front - back)
        summed = addend if summed is None else summed + addend
    return summed


def padded_zero(field, axis):
    widths = [(0, 0)] * field.ndim
    widths[axis] = (4, 4)
    return jnp.pad(field, widths)


def derive(field, axis, forward):
    return stencil(padded_zero(field, axis), axis, forward)


def on_device(
    solid_state,
    water_state,
    lame_lambda,
    shear_mu,
    solid_buoy,
    water_kappa,
    water_buoy,
    seafloor,
    source_cell,
    wavelet,
    receiver_column,
    observed,
):
    parts = lax.axis_size("gx")
    place = lax.axis_index("gx")
    n_fields, waves, shots, width_x, rock_z, total_y = solid_state.shape
    local_y = water_state.shape[3]
    depth_rows = water_state.shape[4]
    total_x = water_state.shape[5]
    anchor_y = place * local_y

    rock_in = jnp.concatenate(
        [
            solid_state.reshape(n_fields * waves * shots, width_x, rock_z, total_y),
            jnp.stack([lame_lambda, shear_mu, solid_buoy]),
        ],
        axis=0,
    )
    rock = jnp.transpose(
        lax.all_to_all(rock_in, "gx", split_axis=3, concat_axis=1, tiled=True), (0, 3, 2, 1)
    )
    rock_state = rock[: n_fields * waves * shots].reshape(
        n_fields, waves, shots, local_y, rock_z, total_x
    )
    lam, mu, buoy = rock[-3], rock[-2], rock[-1]

    vel_x, vel_y, vel_z = (rock_state[0], rock_state[1], rock_state[2])
    sig_xx, sig_yy, sig_zz = (rock_state[3], rock_state[4], rock_state[5])
    sig_xy, sig_xz, sig_yz = (rock_state[6], rock_state[7], rock_state[8])
    pressure, flow_x, flow_y, flow_z = (
        water_state[0],
        water_state[1],
        water_state[2],
        water_state[3],
    )
    depth_idx = lax.broadcasted_iota(jnp.int32, (1, depth_rows, 1), 1)
    floor_rows = seafloor[:, None, :]
    live = (depth_idx < floor_rows).astype(jnp.float32)
    bottom = (depth_idx == floor_rows - 1).astype(jnp.float32)
    above = (depth_idx < floor_rows - 1).astype(jnp.float32)
    rows_y = lax.broadcasted_iota(jnp.int32, (local_y, 1, 1), 0) + anchor_y
    cols_x = lax.broadcasted_iota(jnp.int32, (1, 1, total_x), 2)
    flat_cell = (depth_idx * total_y + rows_y) * total_x + cols_x
    source_hot = (flat_cell[None] == source_cell[:, None, None, None]).astype(jnp.float32)
    node_y = receiver_column // total_x
    node_x = receiver_column % total_x
    inside = (node_y >= anchor_y) & (node_y < anchor_y + local_y)
    local_col = (node_y - anchor_y) * total_x + node_x
    column_iota = lax.broadcasted_iota(jnp.int32, (1, local_y * total_x), 1)
    node_hot = ((column_iota == local_col[:, None]) & inside[:, None]).astype(jnp.float32)
    steps = wavelet.shape[0]
    first_late = steps - min(DEFERRED, steps)
    lam_acc = jnp.zeros((1, shots) + lam.shape, jnp.float32)
    mu_acc = jnp.zeros((1, shots) + lam.shape, jnp.float32)
    kappa_acc = jnp.zeros((1, shots) + water_kappa.shape, jnp.float32)
    early_misfits = []
    late_records = []
    pending = []
    for step in range(steps):
        if pending and pending[0][0] == step - 2:
            _, saved_floor = pending.pop(0)
            rock_zero = jnp.zeros((1,) + vel_x.shape[1:], jnp.float32)
            vel_x, vel_y, vel_z = [jnp.concatenate([f, rock_zero]) for f in (vel_x, vel_y, vel_z)]
            sig_xx, sig_yy, sig_xy, sig_xz, sig_yz = [
                jnp.concatenate([f, rock_zero]) for f in (sig_xx, sig_yy, sig_xy, sig_xz, sig_yz)
            ]
            sig_zz = jnp.concatenate([sig_zz, rock_zero.at[:, :, :, 0, :].set(-saved_floor)])
            lam_acc = jnp.concatenate([lam_acc, jnp.zeros((1,) + lam_acc.shape[1:], jnp.float32)])
            mu_acc = jnp.concatenate([mu_acc, jnp.zeros((1,) + mu_acc.shape[1:], jnp.float32)])
        rock_waves = vel_x.shape[0]
        water_waves = pressure.shape[0]
        floor_pressure = jnp.sum(pressure * bottom, axis=3)
        pending = [(at, floor_pressure[rock_waves + i : rock_waves + i + 1]) for i, (at, _) in enumerate(pending)]
        (flow_x, flow_z_part) = lax.optimization_barrier(
            (
                (flow_x - TIME_STEP * water_buoy * derive(pressure, 4, True)) * live,
                (flow_z - TIME_STEP * water_buoy * derive(pressure, 3, True)) * above,
            )
        )
        (dx_sxx, dz_sxz, dx_sxy, dz_syz, dx_sxz, dz_szz) = lax.optimization_barrier(
            (
                derive(sig_xx, 4, True),
                derive(sig_xz, 3, False),
                derive(sig_xy, 4, False),
                derive(sig_yz, 3, False),
                derive(sig_xz, 4, False),
                derive(sig_zz, 3, True),
            )
        )
        sxy_pad, syy_pad, syz_pad, p_pad = halo_rows(
            [fill_waves(f, water_waves) for f in (sig_xy, sig_yy, sig_yz)] + [pressure]
        )
        sxy_pad, syy_pad, syz_pad = [f[:rock_waves] for f in (sxy_pad, syy_pad, syz_pad)]
        vel_x = vel_x + TIME_STEP * buoy * (dx_sxx + stencil(sxy_pad, 2, False) + dz_sxz)
        vel_y = vel_y + TIME_STEP * buoy * (dx_sxy + stencil(syy_pad, 2, True) + dz_syz)
        vel_z = vel_z + TIME_STEP * buoy * (dx_sxz + stencil(syz_pad, 2, False) + dz_szz)
        floor_velocity = fill_waves(vel_z[:, :, :, 0, :], water_waves)
        flow_y = (flow_y - TIME_STEP * water_buoy * stencil(p_pad, 2, True)) * live
        flow_z = flow_z_part + floor_velocity[:, :, :, None, :] * bottom
        (dx_ux, dz_uz) = lax.optimization_barrier(
            (derive(flow_x, 4, False), derive(flow_z, 3, False))
        )
        (strain_x, strain_z, dx_vy, dz_vy, shear_xz) = lax.optimization_barrier(
            (
                derive(vel_x, 4, False),
                derive(vel_z, 3, False),
                derive(vel_y, 4, True),
                derive(vel_y, 3, True),
                derive(vel_x, 3, True) + derive(vel_z, 4, True),
            )
        )
        vx_pad, vy_pad, vz_pad, uy_pad = halo_rows(
            [fill_waves(f, water_waves) for f in (vel_x, vel_y, vel_z)] + [flow_y]
        )
        vx_pad, vy_pad, vz_pad = [f[:rock_waves] for f in (vx_pad, vy_pad, vz_pad)]
        strain_y = stencil(vy_pad, 2, False)
        dilation = strain_x + strain_y + strain_z
        shear_xy = stencil(vx_pad, 2, True) + dx_vy
        shear_yz = dz_vy + stencil(vz_pad, 2, True)
        lam_part = lam * dilation
        sig_xx = sig_xx + TIME_STEP * (lam_part + 2.0 * mu * strain_x)
        sig_yy = sig_yy + TIME_STEP * (lam_part + 2.0 * mu * strain_y)
        sig_zz = sig_zz + TIME_STEP * (lam_part + 2.0 * mu * strain_z)
        sig_xy = sig_xy + TIME_STEP * mu * shear_xy
        sig_xz = sig_xz + TIME_STEP * mu * shear_xz
        sig_yz = sig_yz + TIME_STEP * mu * shear_yz
        sig_zz = sig_zz.at[:, :, :, 0, :].set(-floor_pressure[:rock_waves])
        lam_acc = lam_acc + dilation[:1] * dilation[1:]
        normal_part = (
            strain_x[:1] * strain_x[1:] + strain_y[:1] * strain_y[1:] + strain_z[:1] * strain_z[1:]
        )
        shear_part = (
            shear_xy[:1] * shear_xy[1:] + shear_xz[:1] * shear_xz[1:] + shear_yz[:1] * shear_yz[1:]
        )
        mu_acc = mu_acc + (2.0 * normal_part + shear_part)
        pressure = (
            pressure
            - TIME_STEP
            * water_kappa
            * (dx_ux + stencil(uy_pad, 2, False) + dz_uz)
        ) * live
        pressure = pressure.at[0].add(wavelet[step][:, None, None, None] * source_hot)
        surface = jnp.sum(pressure[0] * bottom, axis=2)
        partial_record = jnp.einsum(
            "sc,rc->sr",
            surface.reshape(shots, local_y * total_x),
            node_hot,
            precision=lax.Precision.HIGHEST,
        )
        if step < first_late:
            misfit = gather_sum(partial_record, parts) - observed[step]
            scaled = misfit * lax.rsqrt(jnp.mean(misfit * misfit, axis=1, keepdims=True) + 1e-06)
            inject = jnp.dot(
                scaled, node_hot, precision=lax.Precision.HIGHEST, preferred_element_type=jnp.float32
            ).reshape(shots, local_y, total_x)
            pressure = pressure.at[1].add(inject[:, :, None, :] * bottom)
            kappa_acc = kappa_acc + pressure[:1] * pressure[1:]
            early_misfits.append(misfit)
            continue
        late_records.append(partial_record)
        local_misfit = partial_record - observed[step]
        inject = jnp.dot(
            local_misfit, node_hot, precision=lax.Precision.HIGHEST, preferred_element_type=jnp.float32
        ).reshape(shots, local_y, total_x)
        kick = inject[:, :, None, :] * bottom
        kappa_acc = jnp.concatenate(
            [kappa_acc + pressure[:1] * pressure[1:], (pressure[0] * kick)[None]], axis=0
        )
        if step + 1 < steps:
            water_zero = jnp.zeros((1,) + flow_x.shape[1:], jnp.float32)
            flow_x, flow_y, flow_z = [jnp.concatenate([f, water_zero]) for f in (flow_x, flow_y, flow_z)]
            pressure = jnp.concatenate([pressure, kick[None]])
            pending.append((step, None))

    slots = lam_acc.shape[0]
    rock_acc = jnp.concatenate([lam_acc, mu_acc]).reshape(
        2 * slots * shots, local_y, rock_z, parts, width_x
    )
    rock_out = jnp.transpose(rock_acc, (3, 0, 1, 2, 4)).reshape(parts, -1)
    records = jnp.stack(late_records).reshape(1, -1)
    packed = jnp.concatenate([jnp.broadcast_to(records, (parts, records.shape[1])), rock_out], axis=1)
    got = lax.all_to_all(packed, "gx", 0, 0, tiled=True)
    late_count = len(late_records)
    recorded = jnp.sum(got[:, : records.shape[1]], axis=0).reshape(late_count, shots, -1)
    rock_back = got[:, records.shape[1] :].reshape(
        parts, 2 * slots * shots, local_y, rock_z, width_x
    )
    rock_back = jnp.transpose(rock_back, (1, 4, 3, 0, 2)).reshape(
        2, slots, shots, width_x, rock_z, parts * local_y
    )
    late_misfits = recorded - observed[first_late:]
    scales = lax.rsqrt(jnp.mean(late_misfits * late_misfits, axis=2) + 1e-06)
    weights = jnp.concatenate([jnp.ones((1, shots), jnp.float32), scales])
    grad_kappa = jnp.sum(kappa_acc * weights[:, :, None, None, None], axis=(0, 1))
    rock_weights = weights[:slots, :, None, None, None]
    grad_lambda = jnp.sum(rock_back[0] * rock_weights, axis=(0, 1))
    grad_mu = jnp.sum(rock_back[1] * rock_weights, axis=(0, 1))
    misfits = jnp.concatenate([jnp.stack(early_misfits), late_misfits]) if early_misfits else late_misfits
    return (grad_lambda, grad_mu, grad_kappa, misfits)


def solution(mesh):
    placed = (
        P(None, None, "groups", "gx", None, None),
        P(None, None, "groups", "gx", None, None),
        P("gx", None, None),
        P("gx", None, None),
        P("gx", None, None),
        P("gx", None, None),
        P("gx", None, None),
        P("gx", None),
        P("groups"),
        P(None, "groups"),
        P(),
        P(None, "groups", None),
    )
    return jax.shard_map(
        on_device,
        mesh=mesh,
        in_specs=placed,
        out_specs=(
            P("gx", "groups", None),
            P("gx", "groups", None),
            P("gx", "groups", None),
            P(None, "groups", None),
        ),
        check_vma=False,
    )
```

```python
import jax
import jax.numpy as jnp
from jax import lax
from jax.sharding import PartitionSpec as P

COEFF = (1225.0 / 1024.0, -245.0 / 3072.0, 49.0 / 5120.0, -5.0 / 7168.0)
TIME_STEP = 0.2
HALO = 4
ROW_AXIS = 2
DEPTH_AXIS = 3
DEFERRED = 4


def halo_rows(fields):
    devices = lax.axis_size("gx")
    odd = lax.axis_index("gx") % 2 == 1
    within = [(i, i ^ 1) for i in range(devices) if i ^ 1 < devices]
    across = [(i, i + 1) for i in range(1, devices - 1, 2)] + [(i + 1, i) for i in range(1, devices - 1, 2)]
    packed = jnp.concatenate(fields, axis=DEPTH_AXIS)
    length = packed.shape[ROW_AXIS]
    last = lax.slice_in_dim(packed, length - HALO, length, axis=ROW_AXIS)
    first = lax.slice_in_dim(packed, 0, HALO, axis=ROW_AXIS)
    got_within = lax.ppermute(jnp.where(odd, first, last), "gx", within)
    got_across = lax.ppermute(jnp.where(odd, last, first), "gx", across)
    before = jnp.where(odd, got_within, got_across)
    after = jnp.where(odd, got_across, got_within)
    padded = jnp.concatenate([before, packed, after], axis=ROW_AXIS)
    out, start = [], 0
    for f in fields:
        depth = f.shape[DEPTH_AXIS]
        out.append(lax.slice_in_dim(padded, start, start + depth, axis=DEPTH_AXIS))
        start += depth
    return out


def fill_waves(field, waves):
    extra = waves - field.shape[0]
    if extra == 0:
        return field
    return jnp.concatenate([field, jnp.zeros((extra,) + field.shape[1:], field.dtype)])


def gather_sum(partial, parts):
    copies = jnp.broadcast_to(partial[None], (parts,) + partial.shape)
    return jnp.sum(lax.all_to_all(copies, "gx", 0, 0, tiled=True), axis=0)


def stencil(padded, axis, forward):
    length = padded.shape[axis] - 8
    summed = None
    for offset in range(1, 5):
        if forward:
            front_at, back_at = (4 + offset, 5 - offset)
        else:
            front_at, back_at = (3 + offset, 4 - offset)
        front = lax.slice_in_dim(padded, front_at, front_at + length, axis=axis)
        back = lax.slice_in_dim(padded, back_at, back_at + length, axis=axis)
        addend = COEFF[offset - 1] * (front - back)
        summed = addend if summed is None else summed + addend
    return summed


def padded_zero(field, axis):
    widths = [(0, 0)] * field.ndim
    widths[axis] = (4, 4)
    return jnp.pad(field, widths)


def derive(field, axis, forward):
    return stencil(padded_zero(field, axis), axis, forward)


def on_device(
    solid_state,
    water_state,
    lame_lambda,
    shear_mu,
    solid_buoy,
    water_kappa,
    water_buoy,
    seafloor,
    source_cell,
    wavelet,
    receiver_column,
    observed,
):
    parts = lax.axis_size("gx")
    place = lax.axis_index("gx")
    n_fields, waves, shots, width_x, rock_z, total_y = solid_state.shape
    local_y = water_state.shape[3]
    depth_rows = water_state.shape[4]
    total_x = water_state.shape[5]
    anchor_y = place * local_y

    rock_in = jnp.concatenate(
        [
            solid_state.reshape(n_fields * waves * shots, width_x, rock_z, total_y),
            jnp.stack([lame_lambda, shear_mu, solid_buoy]),
        ],
        axis=0,
    )
    rock = jnp.transpose(
        lax.all_to_all(rock_in, "gx", split_axis=3, concat_axis=1, tiled=True), (0, 3, 2, 1)
    )
    rock_state = rock[: n_fields * waves * shots].reshape(
        n_fields, waves, shots, local_y, rock_z, total_x
    )
    lam, mu, buoy = rock[-3], rock[-2], rock[-1]

    vel_x, vel_y, vel_z = (rock_state[0], rock_state[1], rock_state[2])
    sig_xx, sig_yy, sig_zz = (rock_state[3], rock_state[4], rock_state[5])
    sig_xy, sig_xz, sig_yz = (rock_state[6], rock_state[7], rock_state[8])
    pressure, flow_x, flow_y, flow_z = (
        water_state[0],
        water_state[1],
        water_state[2],
        water_state[3],
    )
    depth_idx = lax.broadcasted_iota(jnp.int32, (1, depth_rows, 1), 1)
    floor_rows = seafloor[:, None, :]
    live = (depth_idx < floor_rows).astype(jnp.float32)
    bottom = (depth_idx == floor_rows - 1).astype(jnp.float32)
    above = (depth_idx < floor_rows - 1).astype(jnp.float32)
    rows_y = lax.broadcasted_iota(jnp.int32, (local_y, 1, 1), 0) + anchor_y
    cols_x = lax.broadcasted_iota(jnp.int32, (1, 1, total_x), 2)
    flat_cell = (depth_idx * total_y + rows_y) * total_x + cols_x
    source_hot = (flat_cell[None] == source_cell[:, None, None, None]).astype(jnp.float32)
    node_y = receiver_column // total_x
    node_x = receiver_column % total_x
    inside = (node_y >= anchor_y) & (node_y < anchor_y + local_y)
    local_col = (node_y - anchor_y) * total_x + node_x
    column_iota = lax.broadcasted_iota(jnp.int32, (1, local_y * total_x), 1)
    node_hot = ((column_iota == local_col[:, None]) & inside[:, None]).astype(jnp.float32)
    steps = wavelet.shape[0]
    first_late = steps - min(DEFERRED, steps)
    lam_acc = jnp.zeros((1, shots) + lam.shape, jnp.float32)
    mu_acc = jnp.zeros((1, shots) + lam.shape, jnp.float32)
    kappa_acc = jnp.zeros((1, shots) + water_kappa.shape, jnp.float32)
    early_misfits = []
    late_records = []
    pending = []
    for step in range(steps):
        if pending and pending[0][0] == step - 2:
            _, saved_floor = pending.pop(0)
            rock_zero = jnp.zeros((1,) + vel_x.shape[1:], jnp.float32)
            vel_x, vel_y, vel_z = [jnp.concatenate([f, rock_zero]) for f in (vel_x, vel_y, vel_z)]
            sig_xx, sig_yy, sig_xy, sig_xz, sig_yz = [
                jnp.concatenate([f, rock_zero]) for f in (sig_xx, sig_yy, sig_xy, sig_xz, sig_yz)
            ]
            sig_zz = jnp.concatenate([sig_zz, rock_zero.at[:, :, :, 0, :].set(-saved_floor)])
            lam_acc = jnp.concatenate([lam_acc, jnp.zeros((1,) + lam_acc.shape[1:], jnp.float32)])
            mu_acc = jnp.concatenate([mu_acc, jnp.zeros((1,) + mu_acc.shape[1:], jnp.float32)])
        rock_waves = vel_x.shape[0]
        water_waves = pressure.shape[0]
        floor_pressure = jnp.sum(pressure * bottom, axis=3)
        pending = [(at, floor_pressure[rock_waves + i : rock_waves + i + 1]) for i, (at, _) in enumerate(pending)]
        (flow_x, flow_z_part) = lax.optimization_barrier(
            (
                (flow_x - TIME_STEP * water_buoy * derive(pressure, 4, True)) * live,
                (flow_z - TIME_STEP * water_buoy * derive(pressure, 3, True)) * above,
            )
        )
        (dx_sxx, dz_sxz, dx_sxy, dz_syz, dx_sxz, dz_szz) = lax.optimization_barrier(
            (
                derive(sig_xx, 4, True),
                derive(sig_xz, 3, False),
                derive(sig_xy, 4, False),
                derive(sig_yz, 3, False),
                derive(sig_xz, 4, False),
                derive(sig_zz, 3, True),
            )
        )
        sxy_pad, syy_pad, syz_pad, p_pad = halo_rows(
            [fill_waves(f, water_waves) for f in (sig_xy, sig_yy, sig_yz)] + [pressure]
        )
        sxy_pad, syy_pad, syz_pad = [f[:rock_waves] for f in (sxy_pad, syy_pad, syz_pad)]
        vel_x = vel_x + TIME_STEP * buoy * (dx_sxx + stencil(sxy_pad, 2, False) + dz_sxz)
        vel_y = vel_y + TIME_STEP * buoy * (dx_sxy + stencil(syy_pad, 2, True) + dz_syz)
        vel_z = vel_z + TIME_STEP * buoy * (dx_sxz + stencil(syz_pad, 2, False) + dz_szz)
        floor_velocity = fill_waves(vel_z[:, :, :, 0, :], water_waves)
        flow_y = (flow_y - TIME_STEP * water_buoy * stencil(p_pad, 2, True)) * live
        flow_z = flow_z_part + floor_velocity[:, :, :, None, :] * bottom
        (dx_ux, dz_uz) = lax.optimization_barrier(
            (derive(flow_x, 4, False), derive(flow_z, 3, False))
        )
        (strain_x, strain_z, dx_vy, dz_vy, shear_xz) = lax.optimization_barrier(
            (
                derive(vel_x, 4, False),
                derive(vel_z, 3, False),
                derive(vel_y, 4, True),
                derive(vel_y, 3, True),
                derive(vel_x, 3, True) + derive(vel_z, 4, True),
            )
        )
        vx_pad, vy_pad, vz_pad, uy_pad = halo_rows(
            [fill_waves(f, water_waves) for f in (vel_x, vel_y, vel_z)] + [flow_y]
        )
        vx_pad, vy_pad, vz_pad = [f[:rock_waves] for f in (vx_pad, vy_pad, vz_pad)]
        strain_y = stencil(vy_pad, 2, False)
        dilation = strain_x + strain_y + strain_z
        shear_xy = stencil(vx_pad, 2, True) + dx_vy
        shear_yz = dz_vy + stencil(vz_pad, 2, True)
        lam_part = lam * dilation
        sig_xx = sig_xx + TIME_STEP * (lam_part + 2.0 * mu * strain_x)
        sig_yy = sig_yy + TIME_STEP * (lam_part + 2.0 * mu * strain_y)
        sig_zz = sig_zz + TIME_STEP * (lam_part + 2.0 * mu * strain_z)
        sig_xy = sig_xy + TIME_STEP * mu * shear_xy
        sig_xz = sig_xz + TIME_STEP * mu * shear_xz
        sig_yz = sig_yz + TIME_STEP * mu * shear_yz
        sig_zz = sig_zz.at[:, :, :, 0, :].set(-floor_pressure[:rock_waves])
        lam_acc = lam_acc + dilation[:1] * dilation[1:]
        normal_part = (
            strain_x[:1] * strain_x[1:] + strain_y[:1] * strain_y[1:] + strain_z[:1] * strain_z[1:]
        )
        shear_part = (
            shear_xy[:1] * shear_xy[1:] + shear_xz[:1] * shear_xz[1:] + shear_yz[:1] * shear_yz[1:]
        )
        mu_acc = mu_acc + (2.0 * normal_part + shear_part)
        pressure = (
            pressure
            - TIME_STEP
            * water_kappa
            * (dx_ux + stencil(uy_pad, 2, False) + dz_uz)
        ) * live
        pressure = pressure.at[0].add(wavelet[step][:, None, None, None] * source_hot)
        surface = jnp.sum(pressure[0] * bottom, axis=2)
        partial_record = jnp.einsum(
            "sc,rc->sr",
            surface.reshape(shots, local_y * total_x),
            node_hot,
            precision=lax.Precision.HIGHEST,
        )
        if step < first_late:
            misfit = gather_sum(partial_record, parts) - observed[step]
            scaled = misfit * lax.rsqrt(jnp.mean(misfit * misfit, axis=1, keepdims=True) + 1e-06)
            inject = jnp.dot(
                scaled, node_hot, precision=lax.Precision.HIGHEST, preferred_element_type=jnp.float32
            ).reshape(shots, local_y, total_x)
            pressure = pressure.at[1].add(inject[:, :, None, :] * bottom)
            kappa_acc = kappa_acc + pressure[:1] * pressure[1:]
            early_misfits.append(misfit)
            continue
        late_records.append(partial_record)
        local_misfit = partial_record - observed[step]
        inject = jnp.dot(
            local_misfit, node_hot, precision=lax.Precision.HIGHEST, preferred_element_type=jnp.float32
        ).reshape(shots, local_y, total_x)
        kick = inject[:, :, None, :] * bottom
        kappa_acc = jnp.concatenate(
            [kappa_acc + pressure[:1] * pressure[1:], (pressure[0] * kick)[None]], axis=0
        )
        if step + 1 < steps:
            water_zero = jnp.zeros((1,) + flow_x.shape[1:], jnp.float32)
            flow_x, flow_y, flow_z = [jnp.concatenate([f, water_zero]) for f in (flow_x, flow_y, flow_z)]
            pressure = jnp.concatenate([pressure, kick[None]])
            pending.append((step, None))

    slots = lam_acc.shape[0]
    rock_acc = jnp.concatenate([lam_acc, mu_acc]).reshape(
        2 * slots * shots, local_y, rock_z, parts, width_x
    )
    rock_out = jnp.transpose(rock_acc, (3, 0, 1, 2, 4)).reshape(parts, -1)
    records = jnp.stack(late_records).reshape(1, -1)
    packed = jnp.concatenate([jnp.broadcast_to(records, (parts, records.shape[1])), rock_out], axis=1)
    got = lax.all_to_all(packed, "gx", 0, 0, tiled=True)
    late_count = len(late_records)
    recorded = jnp.sum(got[:, : records.shape[1]], axis=0).reshape(late_count, shots, -1)
    rock_back = got[:, records.shape[1] :].reshape(
        parts, 2 * slots * shots, local_y, rock_z, width_x
    )
    rock_back = jnp.transpose(rock_back, (1, 4, 3, 0, 2)).reshape(
        2, slots, shots, width_x, rock_z, parts * local_y
    )
    late_misfits = recorded - observed[first_late:]
    scales = lax.rsqrt(jnp.mean(late_misfits * late_misfits, axis=2) + 1e-06)
    weights = jnp.concatenate([jnp.ones((1, shots), jnp.float32), scales])
    grad_kappa = jnp.sum(kappa_acc * weights[:, :, None, None, None], axis=(0, 1))
    rock_weights = weights[:slots, :, None, None, None]
    grad_lambda = jnp.sum(rock_back[0] * rock_weights, axis=(0, 1))
    grad_mu = jnp.sum(rock_back[1] * rock_weights, axis=(0, 1))
    misfits = jnp.concatenate([jnp.stack(early_misfits), late_misfits]) if early_misfits else late_misfits
    return (grad_lambda, grad_mu, grad_kappa, misfits)


def solution(mesh):
    placed = (
        P(None, None, "groups", "gx", None, None),
        P(None, None, "groups", "gx", None, None),
        P("gx", None, None),
        P("gx", None, None),
        P("gx", None, None),
        P("gx", None, None),
        P("gx", None, None),
        P("gx", None),
        P("groups"),
        P(None, "groups"),
        P(),
        P(None, "groups", None),
    )
    return jax.shard_map(
        on_device,
        mesh=mesh,
        in_specs=placed,
        out_specs=(
            P("gx", "groups", None),
            P("gx", "groups", None),
            P("gx", "groups", None),
            P(None, "groups", None),
        ),
        check_vma=False,
    )
```

```python
import jax
import jax.numpy as jnp
from jax import lax
from jax.sharding import PartitionSpec as P

COEFF = (1225.0 / 1024.0, -245.0 / 3072.0, 49.0 / 5120.0, -5.0 / 7168.0)
TIME_STEP = 0.2
HALO = 4
ROW_AXIS = 2
DEPTH_AXIS = 3
DEFERRED = 3


def halo_rows(fields):
    devices = lax.axis_size("gx")
    odd = lax.axis_index("gx") % 2 == 1
    within = [(i, i ^ 1) for i in range(devices) if i ^ 1 < devices]
    across = [(i, i + 1) for i in range(1, devices - 1, 2)] + [(i + 1, i) for i in range(1, devices - 1, 2)]
    packed = jnp.concatenate(fields, axis=DEPTH_AXIS)
    length = packed.shape[ROW_AXIS]
    last = lax.slice_in_dim(packed, length - HALO, length, axis=ROW_AXIS)
    first = lax.slice_in_dim(packed, 0, HALO, axis=ROW_AXIS)
    got_within = lax.ppermute(jnp.where(odd, first, last), "gx", within)
    got_across = lax.ppermute(jnp.where(odd, last, first), "gx", across)
    before = jnp.where(odd, got_within, got_across)
    after = jnp.where(odd, got_across, got_within)
    padded = jnp.concatenate([before, packed, after], axis=ROW_AXIS)
    out, start = [], 0
    for f in fields:
        depth = f.shape[DEPTH_AXIS]
        out.append(lax.slice_in_dim(padded, start, start + depth, axis=DEPTH_AXIS))
        start += depth
    return out


def fill_waves(field, waves):
    extra = waves - field.shape[0]
    if extra == 0:
        return field
    return jnp.concatenate([field, jnp.zeros((extra,) + field.shape[1:], field.dtype)])


def gather_sum(partial, parts):
    copies = jnp.broadcast_to(partial[None], (parts,) + partial.shape)
    return jnp.sum(lax.all_to_all(copies, "gx", 0, 0, tiled=True), axis=0)


def stencil(padded, axis, forward):
    length = padded.shape[axis] - 8
    summed = None
    for offset in range(1, 5):
        if forward:
            front_at, back_at = (4 + offset, 5 - offset)
        else:
            front_at, back_at = (3 + offset, 4 - offset)
        front = lax.slice_in_dim(padded, front_at, front_at + length, axis=axis)
        back = lax.slice_in_dim(padded, back_at, back_at + length, axis=axis)
        addend = COEFF[offset - 1] * (front - back)
        summed = addend if summed is None else summed + addend
    return summed


def padded_zero(field, axis):
    widths = [(0, 0)] * field.ndim
    widths[axis] = (4, 4)
    return jnp.pad(field, widths)


def derive(field, axis, forward):
    return stencil(padded_zero(field, axis), axis, forward)


def on_device(
    solid_state,
    water_state,
    lame_lambda,
    shear_mu,
    solid_buoy,
    water_kappa,
    water_buoy,
    seafloor,
    source_cell,
    wavelet,
    receiver_column,
    observed,
):
    parts = lax.axis_size("gx")
    place = lax.axis_index("gx")
    n_fields, waves, shots, width_x, rock_z, total_y = solid_state.shape
    local_y = water_state.shape[3]
    depth_rows = water_state.shape[4]
    total_x = water_state.shape[5]
    anchor_y = place * local_y

    rock_in = jnp.concatenate(
        [
            solid_state.reshape(n_fields * waves * shots, width_x, rock_z, total_y),
            jnp.stack([lame_lambda, shear_mu, solid_buoy]),
        ],
        axis=0,
    )
    rock = jnp.transpose(
        lax.all_to_all(rock_in, "gx", split_axis=3, concat_axis=1, tiled=True), (0, 3, 2, 1)
    )
    rock_state = rock[: n_fields * waves * shots].reshape(
        n_fields, waves, shots, local_y, rock_z, total_x
    )
    lam, mu, buoy = rock[-3], rock[-2], rock[-1]

    vel_x, vel_y, vel_z = (rock_state[0], rock_state[1], rock_state[2])
    sig_xx, sig_yy, sig_zz = (rock_state[3], rock_state[4], rock_state[5])
    sig_xy, sig_xz, sig_yz = (rock_state[6], rock_state[7], rock_state[8])
    pressure, flow_x, flow_y, flow_z = (
        water_state[0],
        water_state[1],
        water_state[2],
        water_state[3],
    )
    depth_idx = lax.broadcasted_iota(jnp.int32, (1, depth_rows, 1), 1)
    floor_rows = seafloor[:, None, :]
    live = (depth_idx < floor_rows).astype(jnp.float32)
    bottom = (depth_idx == floor_rows - 1).astype(jnp.float32)
    above = (depth_idx < floor_rows - 1).astype(jnp.float32)
    rows_y = lax.broadcasted_iota(jnp.int32, (local_y, 1, 1), 0) + anchor_y
    cols_x = lax.broadcasted_iota(jnp.int32, (1, 1, total_x), 2)
    flat_cell = (depth_idx * total_y + rows_y) * total_x + cols_x
    source_hot = (flat_cell[None] == source_cell[:, None, None, None]).astype(jnp.float32)
    node_y = receiver_column // total_x
    node_x = receiver_column % total_x
    inside = (node_y >= anchor_y) & (node_y < anchor_y + local_y)
    local_col = (node_y - anchor_y) * total_x + node_x
    column_iota = lax.broadcasted_iota(jnp.int32, (1, local_y * total_x), 1)
    node_hot = ((column_iota == local_col[:, None]) & inside[:, None]).astype(jnp.float32)
    steps = wavelet.shape[0]
    first_late = steps - min(DEFERRED, steps)
    lam_acc = jnp.zeros((1, shots) + lam.shape, jnp.float32)
    mu_acc = jnp.zeros((1, shots) + lam.shape, jnp.float32)
    kappa_acc = jnp.zeros((1, shots) + water_kappa.shape, jnp.float32)
    early_misfits = []
    late_records = []
    pending = []
    for step in range(steps):
        if pending and pending[0][0] == step - 2:
            _, saved_floor = pending.pop(0)
            rock_zero = jnp.zeros((1,) + vel_x.shape[1:], jnp.float32)
            vel_x, vel_y, vel_z = [jnp.concatenate([f, rock_zero]) for f in (vel_x, vel_y, vel_z)]
            sig_xx, sig_yy, sig_xy, sig_xz, sig_yz = [
                jnp.concatenate([f, rock_zero]) for f in (sig_xx, sig_yy, sig_xy, sig_xz, sig_yz)
            ]
            sig_zz = jnp.concatenate([sig_zz, rock_zero.at[:, :, :, 0, :].set(-saved_floor)])
            lam_acc = jnp.concatenate([lam_acc, jnp.zeros((1,) + lam_acc.shape[1:], jnp.float32)])
            mu_acc = jnp.concatenate([mu_acc, jnp.zeros((1,) + mu_acc.shape[1:], jnp.float32)])
        rock_waves = vel_x.shape[0]
        water_waves = pressure.shape[0]
        floor_pressure = jnp.sum(pressure * bottom, axis=3)
        pending = [(at, floor_pressure[rock_waves + i : rock_waves + i + 1]) for i, (at, _) in enumerate(pending)]
        (flow_x, flow_z_part) = lax.optimization_barrier(
            (
                (flow_x - TIME_STEP * water_buoy * derive(pressure, 4, True)) * live,
                (flow_z - TIME_STEP * water_buoy * derive(pressure, 3, True)) * above,
            )
        )
        (dx_sxx, dz_sxz, dx_sxy, dz_syz, dx_sxz, dz_szz) = lax.optimization_barrier(
            (
                derive(sig_xx, 4, True),
                derive(sig_xz, 3, False),
                derive(sig_xy, 4, False),
                derive(sig_yz, 3, False),
                derive(sig_xz, 4, False),
                derive(sig_zz, 3, True),
            )
        )
        sxy_pad, syy_pad, syz_pad, p_pad = halo_rows(
            [fill_waves(f, water_waves) for f in (sig_xy, sig_yy, sig_yz)] + [pressure]
        )
        sxy_pad, syy_pad, syz_pad = [f[:rock_waves] for f in (sxy_pad, syy_pad, syz_pad)]
        vel_x = vel_x + TIME_STEP * buoy * (dx_sxx + stencil(sxy_pad, 2, False) + dz_sxz)
        vel_y = vel_y + TIME_STEP * buoy * (dx_sxy + stencil(syy_pad, 2, True) + dz_syz)
        vel_z = vel_z + TIME_STEP * buoy * (dx_sxz + stencil(syz_pad, 2, False) + dz_szz)
        floor_velocity = fill_waves(vel_z[:, :, :, 0, :], water_waves)
        flow_y = (flow_y - TIME_STEP * water_buoy * stencil(p_pad, 2, True)) * live
        flow_z = flow_z_part + floor_velocity[:, :, :, None, :] * bottom
        (dx_ux, dz_uz) = lax.optimization_barrier(
            (derive(flow_x, 4, False), derive(flow_z, 3, False))
        )
        (strain_x, strain_z, dx_vy, dz_vy, shear_xz) = lax.optimization_barrier(
            (
                derive(vel_x, 4, False),
                derive(vel_z, 3, False),
                derive(vel_y, 4, True),
                derive(vel_y, 3, True),
                derive(vel_x, 3, True) + derive(vel_z, 4, True),
            )
        )
        vx_pad, vy_pad, vz_pad, uy_pad = halo_rows(
            [fill_waves(f, water_waves) for f in (vel_x, vel_y, vel_z)] + [flow_y]
        )
        vx_pad, vy_pad, vz_pad = [f[:rock_waves] for f in (vx_pad, vy_pad, vz_pad)]
        strain_y = stencil(vy_pad, 2, False)
        dilation = strain_x + strain_y + strain_z
        shear_xy = stencil(vx_pad, 2, True) + dx_vy
        shear_yz = dz_vy + stencil(vz_pad, 2, True)
        lam_part = lam * dilation
        sig_xx = sig_xx + TIME_STEP * (lam_part + 2.0 * mu * strain_x)
        sig_yy = sig_yy + TIME_STEP * (lam_part + 2.0 * mu * strain_y)
        sig_zz = sig_zz + TIME_STEP * (lam_part + 2.0 * mu * strain_z)
        sig_xy = sig_xy + TIME_STEP * mu * shear_xy
        sig_xz = sig_xz + TIME_STEP * mu * shear_xz
        sig_yz = sig_yz + TIME_STEP * mu * shear_yz
        sig_zz = sig_zz.at[:, :, :, 0, :].set(-floor_pressure[:rock_waves])
        (g_dil, g_sx, g_sy, g_sz, g_xy, g_xz, g_yz) = lax.optimization_barrier(
            (dilation, strain_x, strain_y, strain_z, shear_xy, shear_xz, shear_yz)
        )
        lam_acc = lam_acc + g_dil[:1] * g_dil[1:]
        normal_part = g_sx[:1] * g_sx[1:] + g_sy[:1] * g_sy[1:] + g_sz[:1] * g_sz[1:]
        shear_part = g_xy[:1] * g_xy[1:] + g_xz[:1] * g_xz[1:] + g_yz[:1] * g_yz[1:]
        mu_acc = mu_acc + (2.0 * normal_part + shear_part)
        pressure = (
            pressure
            - TIME_STEP
            * water_kappa
            * (dx_ux + stencil(uy_pad, 2, False) + dz_uz)
        ) * live
        pressure = pressure.at[0].add(wavelet[step][:, None, None, None] * source_hot)
        surface = jnp.sum(pressure[0] * bottom, axis=2)
        partial_record = jnp.einsum(
            "sc,rc->sr",
            surface.reshape(shots, local_y * total_x),
            node_hot,
            precision=lax.Precision.HIGHEST,
        )
        if step < first_late:
            misfit = gather_sum(partial_record, parts) - observed[step]
            scaled = misfit * lax.rsqrt(jnp.mean(misfit * misfit, axis=1, keepdims=True) + 1e-06)
            inject = jnp.dot(
                scaled, node_hot, precision=lax.Precision.HIGHEST, preferred_element_type=jnp.float32
            ).reshape(shots, local_y, total_x)
            pressure = pressure.at[1].add(inject[:, :, None, :] * bottom)
            kappa_acc = kappa_acc + pressure[:1] * pressure[1:]
            early_misfits.append(misfit)
            continue
        late_records.append(partial_record)
        local_misfit = partial_record - observed[step]
        inject = jnp.dot(
            local_misfit, node_hot, precision=lax.Precision.HIGHEST, preferred_element_type=jnp.float32
        ).reshape(shots, local_y, total_x)
        kick = inject[:, :, None, :] * bottom
        kappa_acc = jnp.concatenate(
            [kappa_acc + pressure[:1] * pressure[1:], (pressure[0] * kick)[None]], axis=0
        )
        if step + 1 < steps:
            water_zero = jnp.zeros((1,) + flow_x.shape[1:], jnp.float32)
            flow_x, flow_y, flow_z = [jnp.concatenate([f, water_zero]) for f in (flow_x, flow_y, flow_z)]
            pressure = jnp.concatenate([pressure, kick[None]])
            pending.append((step, None))

    slots = lam_acc.shape[0]
    rock_acc = jnp.concatenate([lam_acc, mu_acc]).reshape(
        2 * slots * shots, local_y, rock_z, parts, width_x
    )
    rock_out = jnp.transpose(rock_acc, (3, 0, 1, 2, 4)).reshape(parts, -1)
    records = jnp.stack(late_records).reshape(1, -1)
    packed = jnp.concatenate([jnp.broadcast_to(records, (parts, records.shape[1])), rock_out], axis=1)
    got = lax.all_to_all(packed, "gx", 0, 0, tiled=True)
    late_count = len(late_records)
    recorded = jnp.sum(got[:, : records.shape[1]], axis=0).reshape(late_count, shots, -1)
    rock_back = got[:, records.shape[1] :].reshape(
        parts, 2 * slots * shots, local_y, rock_z, width_x
    )
    rock_back = jnp.transpose(rock_back, (1, 4, 3, 0, 2)).reshape(
        2, slots, shots, width_x, rock_z, parts * local_y
    )
    late_misfits = recorded - observed[first_late:]
    scales = lax.rsqrt(jnp.mean(late_misfits * late_misfits, axis=2) + 1e-06)
    weights = jnp.concatenate([jnp.ones((1, shots), jnp.float32), scales])
    grad_kappa = jnp.sum(kappa_acc * weights[:, :, None, None, None], axis=(0, 1))
    rock_weights = weights[:slots, :, None, None, None]
    grad_lambda = jnp.sum(rock_back[0] * rock_weights, axis=(0, 1))
    grad_mu = jnp.sum(rock_back[1] * rock_weights, axis=(0, 1))
    misfits = jnp.concatenate([jnp.stack(early_misfits), late_misfits]) if early_misfits else late_misfits
    return (grad_lambda, grad_mu, grad_kappa, misfits)


def solution(mesh):
    placed = (
        P(None, None, "groups", "gx", None, None),
        P(None, None, "groups", "gx", None, None),
        P("gx", None, None),
        P("gx", None, None),
        P("gx", None, None),
        P("gx", None, None),
        P("gx", None, None),
        P("gx", None),
        P("groups"),
        P(None, "groups"),
        P(),
        P(None, "groups", None),
    )
    return jax.shard_map(
        on_device,
        mesh=mesh,
        in_specs=placed,
        out_specs=(
            P("gx", "groups", None),
            P("gx", "groups", None),
            P("gx", "groups", None),
            P(None, "groups", None),
        ),
        check_vma=False,
    )
```

```python
import jax
import jax.numpy as jnp
from jax import lax
from jax.sharding import PartitionSpec as P

COEFF = (1225.0 / 1024.0, -245.0 / 3072.0, 49.0 / 5120.0, -5.0 / 7168.0)
TIME_STEP = 0.2
HALO = 4
ROW_AXIS = 2
DEPTH_AXIS = 3
DEFERRED = 3


def halo_rows(fields):
    devices = lax.axis_size("gx")
    odd = lax.axis_index("gx") % 2 == 1
    within = [(i, i ^ 1) for i in range(devices) if i ^ 1 < devices]
    across = [(i, i + 1) for i in range(1, devices - 1, 2)] + [(i + 1, i) for i in range(1, devices - 1, 2)]
    packed = jnp.concatenate(fields, axis=DEPTH_AXIS)
    length = packed.shape[ROW_AXIS]
    last = lax.slice_in_dim(packed, length - HALO, length, axis=ROW_AXIS)
    first = lax.slice_in_dim(packed, 0, HALO, axis=ROW_AXIS)
    got_within = lax.ppermute(jnp.where(odd, first, last), "gx", within)
    got_across = lax.ppermute(jnp.where(odd, last, first), "gx", across)
    before = jnp.where(odd, got_within, got_across)
    after = jnp.where(odd, got_across, got_within)
    padded = jnp.concatenate([before, packed, after], axis=ROW_AXIS)
    out, start = [], 0
    for f in fields:
        depth = f.shape[DEPTH_AXIS]
        out.append(lax.slice_in_dim(padded, start, start + depth, axis=DEPTH_AXIS))
        start += depth
    return out


def fill_waves(field, waves):
    extra = waves - field.shape[0]
    if extra == 0:
        return field
    return jnp.concatenate([field, jnp.zeros((extra,) + field.shape[1:], field.dtype)])


def halo_pair(rock_fields, water_field):
    rock_waves, water_waves = rock_fields[0].shape[0], water_field.shape[0]
    rock_pack = jnp.concatenate(rock_fields, axis=DEPTH_AXIS)
    if rock_pack.shape[1:] == water_field.shape[1:]:
        (padded,) = halo_rows([jnp.concatenate([rock_pack, water_field])])
        rock_pad, water_pad = padded[:rock_waves], padded[rock_waves:]
    else:
        rock_pad, water_pad = halo_rows([fill_waves(rock_pack, water_waves), water_field])
        rock_pad = rock_pad[:rock_waves]
    out, start = [], 0
    for f in rock_fields:
        depth = f.shape[DEPTH_AXIS]
        out.append(lax.slice_in_dim(rock_pad, start, start + depth, axis=DEPTH_AXIS))
        start += depth
    return out + [water_pad]


def gather_sum(partial, parts):
    copies = jnp.broadcast_to(partial[None], (parts,) + partial.shape)
    return jnp.sum(lax.all_to_all(copies, "gx", 0, 0, tiled=True), axis=0)


def stencil(padded, axis, forward):
    length = padded.shape[axis] - 8
    summed = None
    for offset in range(1, 5):
        if forward:
            front_at, back_at = (4 + offset, 5 - offset)
        else:
            front_at, back_at = (3 + offset, 4 - offset)
        front = lax.slice_in_dim(padded, front_at, front_at + length, axis=axis)
        back = lax.slice_in_dim(padded, back_at, back_at + length, axis=axis)
        addend = COEFF[offset - 1] * (front - back)
        summed = addend if summed is None else summed + addend
    return summed


def padded_zero(field, axis):
    widths = [(0, 0)] * field.ndim
    widths[axis] = (4, 4)
    return jnp.pad(field, widths)


def derive(field, axis, forward):
    return stencil(padded_zero(field, axis), axis, forward)


def on_device(
    solid_state,
    water_state,
    lame_lambda,
    shear_mu,
    solid_buoy,
    water_kappa,
    water_buoy,
    seafloor,
    source_cell,
    wavelet,
    receiver_column,
    observed,
):
    parts = lax.axis_size("gx")
    place = lax.axis_index("gx")
    n_fields, waves, shots, width_x, rock_z, total_y = solid_state.shape
    local_y = water_state.shape[3]
    depth_rows = water_state.shape[4]
    total_x = water_state.shape[5]
    anchor_y = place * local_y

    rock_in = jnp.concatenate(
        [
            solid_state.reshape(n_fields * waves * shots, width_x, rock_z, total_y),
            jnp.stack([lame_lambda, shear_mu, solid_buoy]),
        ],
        axis=0,
    )
    rock = jnp.transpose(
        lax.all_to_all(rock_in, "gx", split_axis=3, concat_axis=1, tiled=True), (0, 3, 2, 1)
    )
    rock_state = rock[: n_fields * waves * shots].reshape(
        n_fields, waves, shots, local_y, rock_z, total_x
    )
    lam, mu, buoy = rock[-3], rock[-2], rock[-1]

    vel_x, vel_y, vel_z = (rock_state[0], rock_state[1], rock_state[2])
    sig_xx, sig_yy, sig_zz = (rock_state[3], rock_state[4], rock_state[5])
    sig_xy, sig_xz, sig_yz = (rock_state[6], rock_state[7], rock_state[8])
    pressure, flow_x, flow_y, flow_z = (
        water_state[0],
        water_state[1],
        water_state[2],
        water_state[3],
    )
    depth_idx = lax.broadcasted_iota(jnp.int32, (1, depth_rows, 1), 1)
    floor_rows = seafloor[:, None, :]
    live = (depth_idx < floor_rows).astype(jnp.float32)
    bottom = (depth_idx == floor_rows - 1).astype(jnp.float32)
    above = (depth_idx < floor_rows - 1).astype(jnp.float32)
    rows_y = lax.broadcasted_iota(jnp.int32, (local_y, 1, 1), 0) + anchor_y
    cols_x = lax.broadcasted_iota(jnp.int32, (1, 1, total_x), 2)
    flat_cell = (depth_idx * total_y + rows_y) * total_x + cols_x
    source_hot = (flat_cell[None] == source_cell[:, None, None, None]).astype(jnp.float32)
    node_y = receiver_column // total_x
    node_x = receiver_column % total_x
    inside = (node_y >= anchor_y) & (node_y < anchor_y + local_y)
    local_col = (node_y - anchor_y) * total_x + node_x
    column_iota = lax.broadcasted_iota(jnp.int32, (1, local_y * total_x), 1)
    node_hot = ((column_iota == local_col[:, None]) & inside[:, None]).astype(jnp.float32)
    steps = wavelet.shape[0]
    first_late = steps - min(DEFERRED, steps)
    lam_acc = jnp.zeros((1, shots) + lam.shape, jnp.float32)
    mu_acc = jnp.zeros((1, shots) + lam.shape, jnp.float32)
    kappa_acc = jnp.zeros((1, shots) + water_kappa.shape, jnp.float32)
    early_misfits = []
    late_records = []
    pending = []
    for step in range(steps):
        if pending and pending[0][0] == step - 2:
            _, saved_floor = pending.pop(0)
            rock_zero = jnp.zeros((1,) + vel_x.shape[1:], jnp.float32)
            vel_x, vel_y, vel_z = [jnp.concatenate([f, rock_zero]) for f in (vel_x, vel_y, vel_z)]
            sig_xx, sig_yy, sig_xy, sig_xz, sig_yz = [
                jnp.concatenate([f, rock_zero]) for f in (sig_xx, sig_yy, sig_xy, sig_xz, sig_yz)
            ]
            sig_zz = jnp.concatenate([sig_zz, rock_zero.at[:, :, :, 0, :].set(-saved_floor)])
            lam_acc = jnp.concatenate([lam_acc, jnp.zeros((1,) + lam_acc.shape[1:], jnp.float32)])
            mu_acc = jnp.concatenate([mu_acc, jnp.zeros((1,) + mu_acc.shape[1:], jnp.float32)])
        rock_waves = vel_x.shape[0]
        water_waves = pressure.shape[0]
        floor_pressure = jnp.sum(pressure * bottom, axis=3)
        pending = [(at, floor_pressure[rock_waves + i : rock_waves + i + 1]) for i, (at, _) in enumerate(pending)]
        (flow_x, flow_z_part) = lax.optimization_barrier(
            (
                (flow_x - TIME_STEP * water_buoy * derive(pressure, 4, True)) * live,
                (flow_z - TIME_STEP * water_buoy * derive(pressure, 3, True)) * above,
            )
        )
        (dx_sxx, dz_sxz, dx_sxy, dz_syz, dx_sxz, dz_szz) = lax.optimization_barrier(
            (
                derive(sig_xx, 4, True),
                derive(sig_xz, 3, False),
                derive(sig_xy, 4, False),
                derive(sig_yz, 3, False),
                derive(sig_xz, 4, False),
                derive(sig_zz, 3, True),
            )
        )
        sxy_pad, syy_pad, syz_pad, p_pad = halo_pair([sig_xy, sig_yy, sig_yz], pressure)
        vel_x = vel_x + TIME_STEP * buoy * (dx_sxx + stencil(sxy_pad, 2, False) + dz_sxz)
        vel_y = vel_y + TIME_STEP * buoy * (dx_sxy + stencil(syy_pad, 2, True) + dz_syz)
        vel_z = vel_z + TIME_STEP * buoy * (dx_sxz + stencil(syz_pad, 2, False) + dz_szz)
        floor_velocity = fill_waves(vel_z[:, :, :, 0, :], water_waves)
        flow_y = (flow_y - TIME_STEP * water_buoy * stencil(p_pad, 2, True)) * live
        flow_z = flow_z_part + floor_velocity[:, :, :, None, :] * bottom
        (dx_ux, dz_uz) = lax.optimization_barrier(
            (derive(flow_x, 4, False), derive(flow_z, 3, False))
        )
        (strain_x, strain_z, dx_vy, dz_vy, shear_xz) = lax.optimization_barrier(
            (
                derive(vel_x, 4, False),
                derive(vel_z, 3, False),
                derive(vel_y, 4, True),
                derive(vel_y, 3, True),
                derive(vel_x, 3, True) + derive(vel_z, 4, True),
            )
        )
        vx_pad, vy_pad, vz_pad, uy_pad = halo_pair([vel_x, vel_y, vel_z], flow_y)
        strain_y = stencil(vy_pad, 2, False)
        dilation = strain_x + strain_y + strain_z
        shear_xy = stencil(vx_pad, 2, True) + dx_vy
        shear_yz = dz_vy + stencil(vz_pad, 2, True)
        lam_part = lam * dilation
        sig_xx = sig_xx + TIME_STEP * (lam_part + 2.0 * mu * strain_x)
        sig_yy = sig_yy + TIME_STEP * (lam_part + 2.0 * mu * strain_y)
        sig_zz = sig_zz + TIME_STEP * (lam_part + 2.0 * mu * strain_z)
        sig_xy = sig_xy + TIME_STEP * mu * shear_xy
        sig_xz = sig_xz + TIME_STEP * mu * shear_xz
        sig_yz = sig_yz + TIME_STEP * mu * shear_yz
        sig_zz = sig_zz.at[:, :, :, 0, :].set(-floor_pressure[:rock_waves])
        lam_acc = lam_acc + dilation[:1] * dilation[1:]
        normal_part = (
            strain_x[:1] * strain_x[1:] + strain_y[:1] * strain_y[1:] + strain_z[:1] * strain_z[1:]
        )
        shear_part = (
            shear_xy[:1] * shear_xy[1:] + shear_xz[:1] * shear_xz[1:] + shear_yz[:1] * shear_yz[1:]
        )
        mu_acc = mu_acc + (2.0 * normal_part + shear_part)
        pressure = (
            pressure
            - TIME_STEP
            * water_kappa
            * (dx_ux + stencil(uy_pad, 2, False) + dz_uz)
        ) * live
        pressure = pressure.at[0].add(wavelet[step][:, None, None, None] * source_hot)
        surface = jnp.sum(pressure[0] * bottom, axis=2)
        partial_record = jnp.einsum(
            "sc,rc->sr",
            surface.reshape(shots, local_y * total_x),
            node_hot,
            precision=lax.Precision.HIGHEST,
        )
        if step < first_late:
            misfit = gather_sum(partial_record, parts) - observed[step]
            scaled = misfit * lax.rsqrt(jnp.mean(misfit * misfit, axis=1, keepdims=True) + 1e-06)
            inject = jnp.dot(
                scaled, node_hot, precision=lax.Precision.HIGHEST, preferred_element_type=jnp.float32
            ).reshape(shots, local_y, total_x)
            pressure = pressure.at[1].add(inject[:, :, None, :] * bottom)
            kappa_acc = kappa_acc + pressure[:1] * pressure[1:]
            early_misfits.append(misfit)
            continue
        late_records.append(partial_record)
        local_misfit = partial_record - observed[step]
        inject = jnp.dot(
            local_misfit, node_hot, precision=lax.Precision.HIGHEST, preferred_element_type=jnp.float32
        ).reshape(shots, local_y, total_x)
        kick = inject[:, :, None, :] * bottom
        kappa_acc = jnp.concatenate(
            [kappa_acc + pressure[:1] * pressure[1:], (pressure[0] * kick)[None]], axis=0
        )
        if step + 1 < steps:
            water_zero = jnp.zeros((1,) + flow_x.shape[1:], jnp.float32)
            flow_x, flow_y, flow_z = [jnp.concatenate([f, water_zero]) for f in (flow_x, flow_y, flow_z)]
            pressure = jnp.concatenate([pressure, kick[None]])
            pending.append((step, None))

    slots = lam_acc.shape[0]
    rock_acc = jnp.concatenate([lam_acc, mu_acc]).reshape(
        2 * slots * shots, local_y, rock_z, parts, width_x
    )
    rock_out = jnp.transpose(rock_acc, (3, 0, 1, 2, 4)).reshape(parts, -1)
    records = jnp.stack(late_records).reshape(1, -1)
    packed = jnp.concatenate([jnp.broadcast_to(records, (parts, records.shape[1])), rock_out], axis=1)
    got = lax.all_to_all(packed, "gx", 0, 0, tiled=True)
    late_count = len(late_records)
    recorded = jnp.sum(got[:, : records.shape[1]], axis=0).reshape(late_count, shots, -1)
    rock_back = got[:, records.shape[1] :].reshape(
        parts, 2 * slots * shots, local_y, rock_z, width_x
    )
    rock_back = jnp.transpose(rock_back, (1, 4, 3, 0, 2)).reshape(
        2, slots, shots, width_x, rock_z, parts * local_y
    )
    late_misfits = recorded - observed[first_late:]
    scales = lax.rsqrt(jnp.mean(late_misfits * late_misfits, axis=2) + 1e-06)
    weights = jnp.concatenate([jnp.ones((1, shots), jnp.float32), scales])
    grad_kappa = jnp.sum(kappa_acc * weights[:, :, None, None, None], axis=(0, 1))
    rock_weights = weights[:slots, :, None, None, None]
    grad_lambda = jnp.sum(rock_back[0] * rock_weights, axis=(0, 1))
    grad_mu = jnp.sum(rock_back[1] * rock_weights, axis=(0, 1))
    misfits = jnp.concatenate([jnp.stack(early_misfits), late_misfits]) if early_misfits else late_misfits
    return (grad_lambda, grad_mu, grad_kappa, misfits)


def solution(mesh):
    placed = (
        P(None, None, "groups", "gx", None, None),
        P(None, None, "groups", "gx", None, None),
        P("gx", None, None),
        P("gx", None, None),
        P("gx", None, None),
        P("gx", None, None),
        P("gx", None, None),
        P("gx", None),
        P("groups"),
        P(None, "groups"),
        P(),
        P(None, "groups", None),
    )
    return jax.shard_map(
        on_device,
        mesh=mesh,
        in_specs=placed,
        out_specs=(
            P("gx", "groups", None),
            P("gx", "groups", None),
            P("gx", "groups", None),
            P(None, "groups", None),
        ),
        check_vma=False,
    )
```
